32 devices in a mesh: dp: 2 (over y), mp: 16 (over z, x, core).
Axes of the slice: x: 2, y: 2, z: 4, core: 2. Of those that a mesh axis runs over, the one named last changes fastest.
Arguments:
- queries: bfloat16 [2048, 1024], P(('dp', 'mp')), may hold values from -16 to 16
- hidden: bfloat16 [2048, 2048], P(('dp', 'mp')), may hold values from -6 to 6
- kv_pages: bfloat16 [192, 16, 2, 1024], P(('dp', 'mp')), may hold values from -8 to 8
- page_table: int32 [2, 96], replicated, may hold values from 0 to 191, as said below
- cache_len: int32 [2], replicated, may hold values from 1 to 512, as said below
- deal_table: int32 [2, 16], P('dp'), may hold values from 0 to 15, as said below
- out_weight: bfloat16 [1024, 2048], P('dp', 'mp'), may hold values from -0.1875 to 0.1875
- norm_gain: float32 [2048], replicated, may hold values from 0.1 to 1.9
- expert_ids: int32 [2048, 6], P(('dp', 'mp')), may hold values from 0 to 15, all different within a row; in each aligned block of 64 rows (0 to 63, 64 to 127, ...) at most 32 rows name the same one
- expert_gates: float32 [2048, 6], P(('dp', 'mp')), may hold values from 0.05 to 0.5
- experts_in: bfloat16 [16, 2048, 1408], P('mp', 'dp'), may hold values from -0.125 to 0.125
- experts_out: bfloat16 [16, 704, 2048], P('mp', None, 'dp'), may hold values from -0.21875 to 0.21875
Outputs:
- mixed: bfloat16 [2048, 2048], P(('dp', 'mp'))
The draws below stay inside these ranges and needn't reach their ends.
Inputs may be any that keep to these rules, and one draw needn't show every extreme that they name: `deal_table`: each row is an ordering of 0 to 15: every piece of the 1 request of row d is held by one device of that row. For request r = d + j, the entries page_table[r, l] over all l are exactly the pages (d * 16 + m) * 6 + j * 6 + k for m < 16, k < 6, each once, in an order given by the draw. `cache_len`: some request has 512 cached tokens and some has 1. `expert_ids`: the 6 ids of a token differ; among the 64 tokens of one device no expert is named more than 32 times, and in some device one expert is named exactly 32 times.
All inputs are finite; a program needn't handle non-finite values.
Results may differ from the reference program's by a relative error of at most 0.0095.
Values may be sent and summed in bfloat16 or wider, within the bound.
No kernel may reach another device: no remote copies, remote signals or barrier semaphores. Data moves between devices by JAX's collectives and lax.ppermute only.
A program may use at most 128 MiB of HBM per device.

```python
import math
import jax
import jax.numpy as jnp
import numpy as np
from jax import lax

D = 2048
HEADS = 8
HD = 128
FF = 704
TOPK = 6
QB = 64
PAGE = 16
BLOCKS = 16
EXPERTS = 16
CACHE_MAX = 512
MAXP = 96
REQ_ROW = 1
REQUESTS = 2
PPD = 6
PAGES_DEV = 6
POOL = 192
TOKENS = 2048
CAP = 32
N_DP = 2
N_MP = 16


def draw_queries(key, part):
    base = jax.random.normal(key, (TOKENS, HEADS * HD), jnp.float32)
    values = jnp.clip(1.5 * base, -9.0, 9.0)
    return values.astype(jnp.bfloat16)


def draw_kv_pages(key, part):
    base = jnp.clip(jax.random.normal(key, (POOL, PAGE, 2, HEADS * HD), jnp.float32), -6.0, 6.0)
    return base.astype(jnp.bfloat16)


def draw_page_table(key, part):
    keys = jax.random.split(key, REQUESTS)
    orders = jax.vmap(lambda one_key: jax.random.permutation(one_key, MAXP))(keys).astype(jnp.int32)
    request = jnp.arange(REQUESTS, dtype=jnp.int32)[:, None]
    row_index = request // REQ_ROW
    local_req = request % REQ_ROW
    return ((row_index * N_MP + orders // PPD) * PAGES_DEV + local_req * PPD + orders % PPD).astype(jnp.int32)


def draw_cache_len(key, part):
    lengths = jax.random.randint(jax.random.fold_in(key, 1), (REQUESTS,), 1, CACHE_MAX + 1).astype(jnp.int32)
    order = jax.random.permutation(jax.random.fold_in(key, 2), REQUESTS)
    lengths = lengths.at[order[0]].set(CACHE_MAX)
    lengths = lengths.at[order[1]].set(1)
    return lengths.astype(jnp.int32)


def draw_deal_table(key, part):
    keys = jax.random.split(key, N_DP)
    return jax.vmap(lambda one_key: jax.random.permutation(one_key, N_MP))(keys).astype(jnp.int32)


def level_of(stream_key, dims, cuts, smallest, high):
    def one(position, shards_of):
        steps = jax.random.uniform(jax.random.fold_in(jax.random.fold_in(stream_key, 6), position), (shards_of,), jnp.float32, smallest / len(cuts), high / len(cuts))
        return jnp.repeat(jnp.exp(steps), dims[position] // shards_of).reshape((-1,) + (1,) * (len(dims) - position - 1))

    level = one(*cuts[0])
    for cut in cuts[1:]:
        level = level * one(*cut)
    return level


def assign_block(stream_key, own, number, rows, number_of, top, most, slope):
    ranking = jax.random.permutation(stream_key, number_of)
    packed, usual = shares(number_of, rows * top, most, slope, True), shares(number_of, rows * top, most, slope, False)
    places = jnp.arange(number_of)

    def named(sizes, offset_by):
        used = int((sizes > 0).sum())
        fixed = max(1, used // 4)
        shifted = fixed + (places - fixed + offset_by * (used - fixed)) % max(1, number_of - fixed)
        return jnp.zeros((number_of,), jnp.int32).at[ranking[jnp.where(places < fixed, places, shifted)]].set(jnp.asarray(sizes, jnp.int32))

    sizes = jnp.where(number % 4 == 0, named(packed, number // 4), named(usual, number - number // 4 - 1))
    mixed = jax.random.permutation(jax.random.fold_in(own, 3), number_of)
    donor, taker = mixed[0:number_of // 2 * 2:2], mixed[1:number_of // 2 * 2:2]
    room = jnp.minimum(sizes[donor] - 1, most - sizes[taker]) // 2
    room = jnp.where((donor == ranking[0]) | (taker == ranking[0]) | (sizes[taker] == 0), 0, jnp.maximum(room, 0))
    shifted = jax.random.randint(jax.random.fold_in(own, 4), (number_of // 2,), 0, 1 << 20) % (room + 1)
    sizes = sizes.at[donor].add(-shifted).at[taker].add(shifted)
    labels = jnp.searchsorted(jnp.cumsum(sizes), jnp.arange(rows * top), side="right").astype(jnp.int32)
    grid = labels.reshape(top, rows).T
    grid = grid[jax.random.permutation(jax.random.fold_in(own, 1), rows)]
    offset_by = jax.random.randint(jax.random.fold_in(own, 2), (rows, 1), 0, top)
    return jnp.take_along_axis(grid, (jnp.arange(top)[None, :] + offset_by) % top, axis=1)


def shares(amount, total, most, slope, full):
    loads = [(1 << 20) // math.isqrt(rank ** slope) + 1 for rank in range(1, amount + 1)]
    largest = most if full else min(most, max(-(-total // amount), total * loads[0] // sum(loads)))
    least = 1 if total - largest >= amount - 1 else 0
    given, rest = [largest] + [least] * (amount - 1), total - largest - least * (amount - 1)
    while rest > 0:
        free = [i for i in range(1, amount) if given[i] < largest] or [i for i in range(1, amount) if given[i] < most]
        whole, budget = sum([loads[i] for i in free]), rest
        for i in free:
            more = min(most - given[i], max(1, budget * loads[i] // whole), rest)
            given[i] = given[i] + more
            rest = rest - more
    return np.array(given)


def centred(rng, shape, scale, limit, cuts=(), kind=jnp.bfloat16):
    gain = level_of(rng, shape, cuts, -0.22, 0.18) if cuts else 1.0
    array = jax.random.normal(rng, shape, jnp.float32) * scale * gain
    return jnp.minimum(jnp.maximum(array, -limit), limit).astype(kind)


def setup_inputs(seed: int = 0) -> dict:
    arg_keys = jax.random.split(jax.random.key(seed), 13)
    queries = draw_queries(jax.random.fold_in(arg_keys[12], 71), 0)
    hidden = centred(arg_keys[1], (TOKENS, D), 1.0, 6.0, ((0, 32),))
    kv_pages = draw_kv_pages(jax.random.fold_in(arg_keys[12], 71), 0)
    page_table = draw_page_table(jax.random.fold_in(arg_keys[12], 71), 0)
    cache_len = draw_cache_len(jax.random.fold_in(arg_keys[12], 71), 0)
    deal_table = draw_deal_table(jax.random.fold_in(arg_keys[12], 71), 0)
    out_weight = centred(arg_keys[6], (HEADS * HD, D), (HEADS * HD) ** -0.5, 0.1875, ((0, 2), (1, 16)))
    norm_gain = jnp.clip(1.0 + 0.18 * jax.random.normal(arg_keys[7], (D,), jnp.float32), 0.1, 1.9)
    expert_ids_keys = jax.random.split(jax.random.fold_in(arg_keys[8], 1), TOKENS // QB)
    expert_ids_turns = jax.random.permutation(jax.random.fold_in(arg_keys[8], 3), TOKENS // QB)
    expert_ids = jax.vmap(lambda own, number: assign_block(jax.random.fold_in(arg_keys[8], 2), own, number, QB, EXPERTS, TOPK, CAP, 2))(expert_ids_keys, expert_ids_turns).reshape((TOKENS, TOPK))
    expert_gates = jnp.clip(jnp.exp(math.log(0.5) - 2.3025851 * jax.random.uniform(arg_keys[9], (TOKENS, TOPK), jnp.float32) ** level_of(arg_keys[9], (TOKENS, TOPK), ((0, 32),), -0.2, 0.2)), 0.05, 0.5)
    experts_in = centred(arg_keys[10], (EXPERTS, D, 2 * FF), D ** -0.5, 0.125, ((0, 16), (1, 2)))
    experts_out = centred(arg_keys[11], (EXPERTS, FF, D), FF ** -0.5, 0.21875, ((0, 16), (2, 2)))
    return {"queries": queries, "hidden": hidden, "kv_pages": kv_pages, "page_table": page_table, "cache_len": cache_len, "deal_table": deal_table, "out_weight": out_weight, "norm_gain": norm_gain, "expert_ids": expert_ids, "expert_gates": expert_gates, "experts_in": experts_in, "experts_out": experts_out}


epsilon = 1e-06

def attend(q_rows, key_rows, value_rows, key_pos, first_pos):
    q_count = q_rows.shape[0]
    heads_q = q_rows.reshape(q_count, HEADS, HD).astype(jnp.float32)
    scores = jnp.einsum('qhd,khd->hqk', heads_q, key_rows.astype(jnp.float32)) * (1.0 / math.sqrt(HD))
    query_pos = first_pos + jnp.arange(q_count, dtype=jnp.int32)
    allowed = key_pos[None, :] <= query_pos[:, None]
    scores = jnp.where(allowed[None, :, :], scores, -1e+30)
    row_max = lax.optimization_barrier(jnp.max(scores, axis=2, keepdims=True))
    weights = jnp.exp(scores - row_max)
    weights_bf = (weights / lax.optimization_barrier(jnp.sum(weights, axis=2, keepdims=True))).astype(jnp.bfloat16)
    blended = jnp.einsum('hqk,khd->qhd', weights_bf.astype(jnp.float32), value_rows.astype(jnp.float32))
    return blended.reshape(q_count, HEADS * HD).astype(jnp.bfloat16)

def reference(queries, hidden, kv_pages, page_table, cache_len, deal_table, out_weight, norm_gain, expert_ids, expert_gates, experts_in, experts_out):
    pieces = N_DP * N_MP
    width = HEADS * HD
    q_pieces = queries.reshape(pieces, QB, width)
    dealt = deal_table.reshape(pieces).astype(jnp.int32)
    slot_ids = jnp.arange(pieces, dtype=jnp.int32)
    key_pos = jnp.arange(MAXP * PAGE, dtype=jnp.int32)

    def one_piece(inputs):
        q_rows, slot_id, piece_id = inputs
        request = slot_id // N_MP * REQ_ROW + piece_id // BLOCKS
        first_pos = cache_len[request].astype(jnp.int32) + piece_id % BLOCKS * QB
        pages = jnp.take(kv_pages, page_table[request], axis=0)
        key_rows = pages[:, :, 0, :].reshape(MAXP * PAGE, HEADS, HD)
        value_rows = pages[:, :, 1, :].reshape(MAXP * PAGE, HEADS, HD)
        return attend(q_rows, key_rows, value_rows, key_pos, first_pos)
    attended = lax.map(one_piece, (q_pieces, slot_ids, dealt)).reshape(TOKENS, width)
    projected = jnp.dot(attended, out_weight, preferred_element_type=jnp.float32)
    residual = (hidden.astype(jnp.float32) + projected).astype(jnp.bfloat16)
    resid_f = residual.astype(jnp.float32)
    mean_square = lax.optimization_barrier(jnp.mean(resid_f * resid_f, axis=1, keepdims=True))
    normed = (resid_f * lax.rsqrt(mean_square + epsilon) * norm_gain.astype(jnp.float32)[None, :]).astype(jnp.bfloat16)
    cap_all = N_DP * N_MP * CAP

    def add_expert(expert, running):
        chosen = expert_ids == expert
        routed = jnp.any(chosen, axis=1)
        weight = lax.optimization_barrier(jnp.sum(jnp.where(chosen, expert_gates, 0.0), axis=1))
        row_ids = jnp.nonzero(routed, size=cap_all, fill_value=0)[0].astype(jnp.int32)
        valid = jnp.arange(cap_all, dtype=jnp.int32) < jnp.sum(routed.astype(jnp.int32))
        picked = jnp.take(normed, row_ids, axis=0)
        gate_up = jnp.dot(picked, lax.dynamic_index_in_dim(experts_in, expert, 0, False), preferred_element_type=jnp.float32)
        act = (jax.nn.silu(gate_up[:, :FF]) * gate_up[:, FF:]).astype(jnp.bfloat16)
        result = jnp.dot(act, lax.dynamic_index_in_dim(experts_out, expert, 0, False), preferred_element_type=jnp.float32).astype(jnp.bfloat16)
        addend = jnp.where(valid[:, None], result.astype(jnp.float32) * jnp.take(weight, row_ids)[:, None], 0.0)
        return running.at[row_ids].add(addend)
    expert_sum = lax.fori_loop(0, EXPERTS, add_expert, jnp.zeros((TOKENS, D), jnp.float32))
    return (resid_f + expert_sum).astype(jnp.bfloat16)
```

```python
import math

import jax
import jax.numpy as jnp
from jax import lax
from jax.sharding import PartitionSpec as P

HEADS = 8
HD = 128
TOPK = 6
PAGE = 16


epsilon = 1e-06


def attend_head(q_rows, key_rows, value_rows, key_pos, query_pos):
    scores = jnp.dot(q_rows, key_rows.T, preferred_element_type=jnp.float32) * (1.0 / math.sqrt(HD))
    allowed = key_pos[None, :] <= query_pos[:, None]
    scores = jnp.where(allowed, scores, -1e30)
    row_max = jnp.max(scores, axis=1, keepdims=True)
    weights = jnp.exp(scores - row_max)
    weights_bf = (weights / jnp.sum(weights, axis=1, keepdims=True)).astype(jnp.bfloat16)
    blended = jnp.dot(weights_bf, value_rows, preferred_element_type=jnp.float32)
    return blended.astype(jnp.bfloat16)


def swap_dp(x):
    return lax.ppermute(x, "dp", [(0, 1), (1, 0)])


def on_device(
    queries,
    hidden,
    kv_pages,
    page_table,
    cache_len,
    deal_table,
    out_weight,
    norm_gain,
    expert_ids,
    expert_gates,
    experts_in,
    experts_out,
):
    n_mp = lax.axis_size("mp")
    n_dp = lax.axis_size("dp")
    row_index = lax.axis_index("dp")
    column = lax.axis_index("mp")
    q_count = queries.shape[0]
    width = queries.shape[1]
    d_model = hidden.shape[1]
    heads = width // HD
    groups = n_mp // heads
    sub = q_count // groups
    my_head = column % heads
    my_group = column // heads
    page_share = page_table.shape[1] // n_mp
    pages_dev = kv_pages.shape[0]
    deal_row = deal_table[0]
    request = row_index
    page_count = page_table.shape[1]

    q_out = queries.reshape(sub, groups, heads, HD).transpose(1, 2, 0, 3).reshape(n_mp, sub, HD)
    q_in = lax.all_to_all(q_out, "mp", split_axis=0, concat_axis=0, tiled=True)
    first_pos = cache_len[request] + deal_row % n_mp * q_count
    query_pos = (
        first_pos[:, None] + jnp.arange(sub, dtype=jnp.int32)[None, :] * groups + my_group
    ).reshape(-1)

    kv_heads = kv_pages.reshape(pages_dev, PAGE, 2, heads, HD).transpose(3, 0, 1, 2, 4)
    kv_out = jnp.tile(kv_heads, (groups, 1, 1, 1, 1))
    arrived = lax.all_to_all(kv_out, "mp", split_axis=0, concat_axis=0, tiled=True)
    slot_ids = jnp.arange(n_mp * page_share, dtype=jnp.int32)
    physical = (row_index * n_mp + slot_ids // page_share) * pages_dev + slot_ids % page_share
    table_row = page_table[request]
    matches = table_row[None, :] == physical[:, None]
    logical = jnp.sum(
        jnp.where(matches, jnp.arange(page_count, dtype=jnp.int32)[None, :], 0), axis=1
    )
    key_pos = (logical[:, None] * PAGE + jnp.arange(PAGE, dtype=jnp.int32)[None, :]).reshape(-1)
    key_rows = arrived[:, :, :, 0, :].reshape(-1, HD)
    value_rows = arrived[:, :, :, 1, :].reshape(-1, HD)
    blended = attend_head(q_in.reshape(-1, HD), key_rows, value_rows, key_pos, query_pos)
    back = lax.all_to_all(blended.reshape(n_mp, sub, HD), "mp", split_axis=0, concat_axis=0, tiled=True)
    attended = back.reshape(groups, heads, sub, HD).transpose(2, 0, 1, 3).reshape(q_count, width)

    wo_rows = lax.all_gather(out_weight, "dp", axis=0, tiled=True)
    projected = jnp.dot(
        attended,
        lax.all_gather(wo_rows, "mp", axis=1, tiled=True),
        preferred_element_type=jnp.float32,
    )
    resid_f = (hidden.astype(jnp.float32) + projected).astype(jnp.bfloat16).astype(jnp.float32)
    mean_square = jnp.mean(resid_f * resid_f, axis=1, keepdims=True)
    normed = (resid_f * lax.rsqrt(mean_square + epsilon) * norm_gain[None, :]).astype(jnp.bfloat16)
    capacity = min(q_count, q_count * TOPK * 4 // (3 * n_mp))
    flat_ids = expert_ids.reshape(-1)
    one_hot = (flat_ids[:, None] == jnp.arange(n_mp, dtype=jnp.int32)[None, :]).astype(jnp.int32)
    slot_of = jnp.sum(jnp.cumsum(one_hot, axis=0) * one_hot, axis=1) - 1
    target = flat_ids * capacity + slot_of
    token_of_pair = jnp.arange(q_count * TOPK, dtype=jnp.int32) // TOPK
    sending = (
        jnp.zeros((n_mp * capacity, d_model), jnp.bfloat16)
        .at[target]
        .set(jnp.take(normed, token_of_pair, axis=0))
    )
    sending = sending.reshape(n_mp, capacity, d_model)
    ff_width = experts_out.shape[1]
    received = lax.all_to_all(sending, "mp", split_axis=0, concat_axis=0, tiled=True)
    flat_rows = received.reshape(-1, d_model)
    if n_dp == 2:
        half_in = experts_in.shape[1]
        in_other = swap_dp(experts_in)
        out_other = swap_dp(experts_out)
        rows_mine = lax.dynamic_slice_in_dim(flat_rows, row_index * half_in, half_in, axis=1)
        rows_other = lax.dynamic_slice_in_dim(flat_rows, (1 - row_index) * half_in, half_in, axis=1)
        gate_vals = jnp.dot(rows_mine, experts_in[0], preferred_element_type=jnp.float32) + jnp.dot(
            rows_other, in_other[0], preferred_element_type=jnp.float32
        )
        act = (jax.nn.silu(gate_vals[:, :ff_width]) * gate_vals[:, ff_width:]).astype(jnp.bfloat16)
        part_mine = jnp.dot(act, experts_out[0], preferred_element_type=jnp.float32).astype(jnp.bfloat16)
        part_other = jnp.dot(act, out_other[0], preferred_element_type=jnp.float32).astype(jnp.bfloat16)
        outcome = jnp.where(
            row_index == 0,
            jnp.concatenate([part_mine, part_other], axis=1),
            jnp.concatenate([part_other, part_mine], axis=1),
        )
    else:
        gate_up = lax.all_gather(experts_in, "dp", axis=1, tiled=True)
        down = lax.all_gather(experts_out, "dp", axis=2, tiled=True)
        gate_vals = jnp.dot(flat_rows, gate_up[0], preferred_element_type=jnp.float32)
        act = (jax.nn.silu(gate_vals[:, :ff_width]) * gate_vals[:, ff_width:]).astype(jnp.bfloat16)
        outcome = jnp.dot(act, down[0], preferred_element_type=jnp.float32).astype(jnp.bfloat16)
    results = lax.all_to_all(
        outcome.reshape(received.shape), "mp", split_axis=0, concat_axis=0, tiled=True
    )
    picked = jnp.take(results.reshape(-1, d_model), target, axis=0)
    weighted = picked.astype(jnp.float32) * expert_gates.reshape(-1)[:, None]
    expert_sum = jnp.sum(weighted.reshape(q_count, TOPK, d_model), axis=1)
    return (resid_f + expert_sum).astype(jnp.bfloat16)


def solution(mesh):
    in_specs = (
        P(("dp", "mp"), None),
        P(("dp", "mp"), None),
        P(("dp", "mp"), None, None, None),
        P(),
        P(),
        P("dp", None),
        P("dp", "mp"),
        P(),
        P(("dp", "mp"), None),
        P(("dp", "mp"), None),
        P("mp", "dp", None),
        P("mp", None, "dp"),
    )
    out_specs = P(("dp", "mp"), None)
    return jax.shard_map(
        on_device, mesh=mesh, in_specs=in_specs, out_specs=out_specs, check_vma=False
    )
```

```python
import math

import jax
import jax.numpy as jnp
from jax import lax
from jax.sharding import PartitionSpec as P

HEADS = 8
HD = 128
TOPK = 6
PAGE = 16


epsilon = 1e-06


def attend_head(q_rows, key_rows, value_rows, key_pos, query_pos):
    scores = jnp.dot(q_rows, key_rows.T, preferred_element_type=jnp.float32) * (1.0 / math.sqrt(HD))
    allowed = key_pos[None, :] <= query_pos[:, None]
    scores = jnp.where(allowed, scores, -1e30)
    row_max = jnp.max(scores, axis=1, keepdims=True)
    weights = jnp.exp(scores - row_max)
    weights_bf = (weights / jnp.sum(weights, axis=1, keepdims=True)).astype(jnp.bfloat16)
    blended = jnp.dot(weights_bf, value_rows, preferred_element_type=jnp.float32)
    return blended.astype(jnp.bfloat16)


def swap_dp(x):
    return lax.ppermute(x, "dp", [(0, 1), (1, 0)])


def on_device(
    queries,
    hidden,
    kv_pages,
    page_table,
    cache_len,
    deal_table,
    out_weight,
    norm_gain,
    expert_ids,
    expert_gates,
    experts_in,
    experts_out,
):
    n_mp = lax.axis_size("mp")
    n_dp = lax.axis_size("dp")
    row_index = lax.axis_index("dp")
    column = lax.axis_index("mp")
    q_count = queries.shape[0]
    width = queries.shape[1]
    d_model = hidden.shape[1]
    heads = width // HD
    groups = n_mp // heads
    sub = q_count // groups
    my_head = column % heads
    my_group = column // heads
    page_share = page_table.shape[1] // n_mp
    pages_dev = kv_pages.shape[0]
    deal_row = deal_table[0]
    request = row_index
    page_count = page_table.shape[1]

    q_out = queries.reshape(sub, groups, heads, HD).transpose(1, 2, 0, 3).reshape(n_mp, sub, HD)
    kv_heads = kv_pages.reshape(pages_dev, PAGE, 2, heads, HD).transpose(3, 0, 1, 2, 4)
    kv_out = jnp.tile(kv_heads, (groups, 1, 1, 1, 1)).reshape(n_mp, pages_dev * PAGE * 2, HD)
    both = lax.all_to_all(
        jnp.concatenate([q_out, kv_out], axis=1), "mp", split_axis=0, concat_axis=0, tiled=True
    )
    q_in = both[:, :sub, :]
    arrived = both[:, sub:, :].reshape(n_mp, pages_dev, PAGE, 2, HD)
    first_pos = cache_len[request] + deal_row % n_mp * q_count
    query_pos = (
        first_pos[:, None] + jnp.arange(sub, dtype=jnp.int32)[None, :] * groups + my_group
    ).reshape(-1)
    slot_ids = jnp.arange(n_mp * page_share, dtype=jnp.int32)
    physical = (row_index * n_mp + slot_ids // page_share) * pages_dev + slot_ids % page_share
    table_row = page_table[request]
    matches = table_row[None, :] == physical[:, None]
    logical = jnp.sum(
        jnp.where(matches, jnp.arange(page_count, dtype=jnp.int32)[None, :], 0), axis=1
    )
    key_pos = (logical[:, None] * PAGE + jnp.arange(PAGE, dtype=jnp.int32)[None, :]).reshape(-1)
    key_rows = arrived[:, :, :, 0, :].reshape(-1, HD)
    value_rows = arrived[:, :, :, 1, :].reshape(-1, HD)
    blended = attend_head(q_in.reshape(-1, HD), key_rows, value_rows, key_pos, query_pos)
    back = lax.all_to_all(blended.reshape(n_mp, sub, HD), "mp", split_axis=0, concat_axis=0, tiled=True)
    attended = back.reshape(groups, heads, sub, HD).transpose(2, 0, 1, 3).reshape(q_count, width)

    wo_rows = lax.all_gather(out_weight, "dp", axis=0, tiled=True)
    projected = jnp.dot(
        attended,
        lax.all_gather(wo_rows, "mp", axis=1, tiled=True),
        preferred_element_type=jnp.float32,
    )
    resid_f = (hidden.astype(jnp.float32) + projected).astype(jnp.bfloat16).astype(jnp.float32)
    mean_square = jnp.mean(resid_f * resid_f, axis=1, keepdims=True)
    normed = (resid_f * lax.rsqrt(mean_square + epsilon) * norm_gain[None, :]).astype(jnp.bfloat16)
    capacity = min(q_count, q_count * TOPK * 4 // (3 * n_mp))
    flat_ids = expert_ids.reshape(-1)
    one_hot = (flat_ids[:, None] == jnp.arange(n_mp, dtype=jnp.int32)[None, :]).astype(jnp.int32)
    slot_of = jnp.sum(jnp.cumsum(one_hot, axis=0) * one_hot, axis=1) - 1
    target = (flat_ids * capacity + slot_of).reshape(q_count, TOPK)
    hits = target[:, :, None] == jnp.arange(n_mp * capacity, dtype=jnp.int32)[None, None, :]
    dispatch = jnp.any(hits, axis=1).astype(jnp.bfloat16)
    combine = jnp.sum(jnp.where(hits, expert_gates[:, :, None], 0.0), axis=1)
    ff_width = experts_out.shape[1]
    if n_dp == 2:
        in_other = swap_dp(experts_in)
        out_other = swap_dp(experts_out)
        normed, in_other, out_other = lax.optimization_barrier((normed, in_other, out_other))
    sending = lax.dot_general(
        dispatch, normed, (((0,), (0,)), ((), ())), preferred_element_type=jnp.float32
    ).astype(jnp.bfloat16)
    received = lax.all_to_all(
        sending.reshape(n_mp, capacity, d_model), "mp", split_axis=0, concat_axis=0, tiled=True
    )
    flat_rows = received.reshape(-1, d_model)
    if n_dp == 2:
        half_in = experts_in.shape[1]
        rows_mine = lax.dynamic_slice_in_dim(flat_rows, row_index * half_in, half_in, axis=1)
        rows_other = lax.dynamic_slice_in_dim(flat_rows, (1 - row_index) * half_in, half_in, axis=1)
        gate_vals = jnp.dot(rows_mine, experts_in[0], preferred_element_type=jnp.float32) + jnp.dot(
            rows_other, in_other[0], preferred_element_type=jnp.float32
        )
        act = (jax.nn.silu(gate_vals[:, :ff_width]) * gate_vals[:, ff_width:]).astype(jnp.bfloat16)
        part_mine = jnp.dot(act, experts_out[0], preferred_element_type=jnp.float32).astype(jnp.bfloat16)
        part_other = jnp.dot(act, out_other[0], preferred_element_type=jnp.float32).astype(jnp.bfloat16)
        outcome = jnp.where(
            row_index == 0,
            jnp.concatenate([part_mine, part_other], axis=1),
            jnp.concatenate([part_other, part_mine], axis=1),
        )
    else:
        gate_up = lax.all_gather(experts_in, "dp", axis=1, tiled=True)
        down = lax.all_gather(experts_out, "dp", axis=2, tiled=True)
        gate_vals = jnp.dot(flat_rows, gate_up[0], preferred_element_type=jnp.float32)
        act = (jax.nn.silu(gate_vals[:, :ff_width]) * gate_vals[:, ff_width:]).astype(jnp.bfloat16)
        outcome = jnp.dot(act, down[0], preferred_element_type=jnp.float32).astype(jnp.bfloat16)
    results = lax.all_to_all(
        outcome.reshape(n_mp, capacity, d_model), "mp", split_axis=0, concat_axis=0, tiled=True
    )
    expert_sum = jnp.dot(
        combine,
        results.reshape(-1, d_model).astype(jnp.float32),
        precision=lax.Precision.HIGHEST,
        preferred_element_type=jnp.float32,
    )
    return (resid_f + expert_sum).astype(jnp.bfloat16)


def solution(mesh):
    in_specs = (
        P(("dp", "mp"), None),
        P(("dp", "mp"), None),
        P(("dp", "mp"), None, None, None),
        P(),
        P(),
        P("dp", None),
        P("dp", "mp"),
        P(),
        P(("dp", "mp"), None),
        P(("dp", "mp"), None),
        P("mp", "dp", None),
        P("mp", None, "dp"),
    )
    out_specs = P(("dp", "mp"), None)
    return jax.shard_map(
        on_device, mesh=mesh, in_specs=in_specs, out_specs=out_specs, check_vma=False
    )
```

```python
import math

import jax
import jax.numpy as jnp
from jax import lax
from jax.sharding import PartitionSpec as P

HEADS = 8
HD = 128
TOPK = 6
PAGE = 16


epsilon = 1e-06


def attend_head(q_rows, key_rows, value_rows, key_pos, query_pos):
    scores = jnp.dot(q_rows, key_rows.T, preferred_element_type=jnp.float32) * (1.0 / math.sqrt(HD))
    allowed = key_pos[None, :] <= query_pos[:, None]
    scores = jnp.where(allowed, scores, -1e30)
    row_max = jnp.max(scores, axis=1, keepdims=True)
    weights = jnp.exp(scores - row_max)
    weights_bf = (weights / jnp.sum(weights, axis=1, keepdims=True)).astype(jnp.bfloat16)
    blended = jnp.dot(weights_bf, value_rows, preferred_element_type=jnp.float32)
    return blended.astype(jnp.bfloat16)


def swap_dp(x):
    return lax.ppermute(x, "dp", [(0, 1), (1, 0)])


def on_device(
    queries,
    hidden,
    kv_pages,
    page_table,
    cache_len,
    deal_table,
    out_weight,
    norm_gain,
    expert_ids,
    expert_gates,
    experts_in,
    experts_out,
):
    n_mp = lax.axis_size("mp")
    n_dp = lax.axis_size("dp")
    row_index = lax.axis_index("dp")
    column = lax.axis_index("mp")
    q_count = queries.shape[0]
    width = queries.shape[1]
    d_model = hidden.shape[1]
    heads = width // HD
    groups = n_mp // heads
    sub = q_count // groups
    my_head = column % heads
    my_group = column // heads
    page_share = page_table.shape[1] // n_mp
    pages_dev = kv_pages.shape[0]
    deal_row = deal_table[0]
    request = row_index
    page_count = page_table.shape[1]

    q_out = queries.reshape(sub, groups, heads, HD).transpose(1, 2, 0, 3).reshape(n_mp, sub, HD)
    kv_heads = kv_pages.reshape(pages_dev, PAGE, 2, heads, HD).transpose(3, 0, 1, 2, 4)
    kv_out = jnp.tile(kv_heads, (groups, 1, 1, 1, 1)).reshape(n_mp, pages_dev * PAGE * 2, HD)
    both = lax.all_to_all(
        jnp.concatenate([q_out, kv_out], axis=1), "mp", split_axis=0, concat_axis=0, tiled=True
    )
    q_in = both[:, :sub, :]
    arrived = both[:, sub:, :].reshape(n_mp, pages_dev, PAGE, 2, HD)
    first_pos = cache_len[request] + deal_row % n_mp * q_count
    query_pos = (
        first_pos[:, None] + jnp.arange(sub, dtype=jnp.int32)[None, :] * groups + my_group
    ).reshape(-1)
    slot_ids = jnp.arange(n_mp * page_share, dtype=jnp.int32)
    physical = (row_index * n_mp + slot_ids // page_share) * pages_dev + slot_ids % page_share
    table_row = page_table[request]
    matches = table_row[None, :] == physical[:, None]
    logical = jnp.sum(
        jnp.where(matches, jnp.arange(page_count, dtype=jnp.int32)[None, :], 0), axis=1
    )
    key_pos = (logical[:, None] * PAGE + jnp.arange(PAGE, dtype=jnp.int32)[None, :]).reshape(-1)
    key_rows = arrived[:, :, :, 0, :].reshape(-1, HD)
    value_rows = arrived[:, :, :, 1, :].reshape(-1, HD)
    blended = attend_head(q_in.reshape(-1, HD), key_rows, value_rows, key_pos, query_pos)
    back = lax.all_to_all(blended.reshape(n_mp, sub, HD), "mp", split_axis=0, concat_axis=0, tiled=True)
    attended = back.reshape(groups, heads, sub, HD).transpose(2, 0, 1, 3).reshape(q_count, width)

    if n_dp == 2:
        half_w = out_weight.shape[0]
        w_mine = lax.all_gather(out_weight, "mp", axis=1, tiled=True)
        w_other = lax.all_gather(swap_dp(out_weight), "mp", axis=1, tiled=True)
        att_mine = lax.dynamic_slice_in_dim(attended, row_index * half_w, half_w, axis=1)
        att_other = lax.dynamic_slice_in_dim(attended, (1 - row_index) * half_w, half_w, axis=1)
        projected = jnp.dot(att_mine, w_mine, preferred_element_type=jnp.float32) + jnp.dot(
            att_other, w_other, preferred_element_type=jnp.float32
        )
    else:
        wo_rows = lax.all_gather(out_weight, "dp", axis=0, tiled=True)
        projected = jnp.dot(
            attended,
            lax.all_gather(wo_rows, "mp", axis=1, tiled=True),
            preferred_element_type=jnp.float32,
        )
    resid_f = (hidden.astype(jnp.float32) + projected).astype(jnp.bfloat16).astype(jnp.float32)
    mean_square = jnp.mean(resid_f * resid_f, axis=1, keepdims=True)
    normed = (resid_f * lax.rsqrt(mean_square + epsilon) * norm_gain[None, :]).astype(jnp.bfloat16)
    capacity = min(q_count, q_count * TOPK * 4 // (3 * n_mp))
    flat_ids = expert_ids.reshape(-1)
    one_hot = (flat_ids[:, None] == jnp.arange(n_mp, dtype=jnp.int32)[None, :]).astype(jnp.int32)
    slot_of = jnp.sum(jnp.cumsum(one_hot, axis=0) * one_hot, axis=1) - 1
    target = (flat_ids * capacity + slot_of).reshape(q_count, TOPK)
    hits = target[:, :, None] == jnp.arange(n_mp * capacity, dtype=jnp.int32)[None, None, :]
    dispatch = jnp.any(hits, axis=1).astype(jnp.bfloat16)
    combine = jnp.sum(jnp.where(hits, expert_gates[:, :, None], 0.0), axis=1)
    ff_width = experts_out.shape[1]
    if n_dp == 2:
        in_other = swap_dp(experts_in)
        out_other = swap_dp(experts_out)
        normed, in_other = lax.optimization_barrier((normed, in_other))
    sending = lax.dot_general(
        dispatch, normed, (((0,), (0,)), ((), ())), preferred_element_type=jnp.float32
    ).astype(jnp.bfloat16)
    received = lax.all_to_all(
        sending.reshape(n_mp, capacity, d_model), "mp", split_axis=0, concat_axis=0, tiled=True
    )
    flat_rows = received.reshape(-1, d_model)
    if n_dp == 2:
        flat_rows, out_other = lax.optimization_barrier((flat_rows, out_other))
        half_in = experts_in.shape[1]
        rows_mine = lax.dynamic_slice_in_dim(flat_rows, row_index * half_in, half_in, axis=1)
        rows_other = lax.dynamic_slice_in_dim(flat_rows, (1 - row_index) * half_in, half_in, axis=1)
        gate_vals = jnp.dot(rows_mine, experts_in[0], preferred_element_type=jnp.float32) + jnp.dot(
            rows_other, in_other[0], preferred_element_type=jnp.float32
        )
        act = (jax.nn.silu(gate_vals[:, :ff_width]) * gate_vals[:, ff_width:]).astype(jnp.bfloat16)
        part_mine = jnp.dot(act, experts_out[0], preferred_element_type=jnp.float32).astype(jnp.bfloat16)
        part_other = jnp.dot(act, out_other[0], preferred_element_type=jnp.float32).astype(jnp.bfloat16)
        outcome = jnp.where(
            row_index == 0,
            jnp.concatenate([part_mine, part_other], axis=1),
            jnp.concatenate([part_other, part_mine], axis=1),
        )
    else:
        gate_up = lax.all_gather(experts_in, "dp", axis=1, tiled=True)
        down = lax.all_gather(experts_out, "dp", axis=2, tiled=True)
        gate_vals = jnp.dot(flat_rows, gate_up[0], preferred_element_type=jnp.float32)
        act = (jax.nn.silu(gate_vals[:, :ff_width]) * gate_vals[:, ff_width:]).astype(jnp.bfloat16)
        outcome = jnp.dot(act, down[0], preferred_element_type=jnp.float32).astype(jnp.bfloat16)
    results = lax.all_to_all(
        outcome.reshape(n_mp, capacity, d_model), "mp", split_axis=0, concat_axis=0, tiled=True
    )
    expert_sum = jnp.dot(
        combine,
        results.reshape(-1, d_model).astype(jnp.float32),
        precision=lax.Precision.HIGHEST,
        preferred_element_type=jnp.float32,
    )
    return (resid_f + expert_sum).astype(jnp.bfloat16)


def solution(mesh):
    in_specs = (
        P(("dp", "mp"), None),
        P(("dp", "mp"), None),
        P(("dp", "mp"), None, None, None),
        P(),
        P(),
        P("dp", None),
        P("dp", "mp"),
        P(),
        P(("dp", "mp"), None),
        P(("dp", "mp"), None),
        P("mp", "dp", None),
        P("mp", None, "dp"),
    )
    out_specs = P(("dp", "mp"), None)
    return jax.shard_map(
        on_device, mesh=mesh, in_specs=in_specs, out_specs=out_specs, check_vma=False
    )
```

```python
import math

import jax
import jax.numpy as jnp
from jax import lax
from jax.sharding import PartitionSpec as P

HEADS = 8
HD = 128
TOPK = 6
PAGE = 16


epsilon = 1e-06


def attend_head(q_rows, key_rows, value_rows, key_pos, query_pos):
    scores = jnp.dot(q_rows, key_rows.T, preferred_element_type=jnp.float32) * (1.0 / math.sqrt(HD))
    allowed = key_pos[None, :] <= query_pos[:, None]
    scores = jnp.where(allowed, scores, -1e30)
    row_max = jnp.max(scores, axis=1, keepdims=True)
    weights = jnp.exp(scores - row_max)
    weights_bf = (weights / jnp.sum(weights, axis=1, keepdims=True)).astype(jnp.bfloat16)
    blended = jnp.dot(weights_bf, value_rows, preferred_element_type=jnp.float32)
    return blended.astype(jnp.bfloat16)


def swap_dp(x):
    return lax.ppermute(x, "dp", [(0, 1), (1, 0)])


def on_device(
    queries,
    hidden,
    kv_pages,
    page_table,
    cache_len,
    deal_table,
    out_weight,
    norm_gain,
    expert_ids,
    expert_gates,
    experts_in,
    experts_out,
):
    n_mp = lax.axis_size("mp")
    n_dp = lax.axis_size("dp")
    row_index = lax.axis_index("dp")
    column = lax.axis_index("mp")
    q_count = queries.shape[0]
    width = queries.shape[1]
    d_model = hidden.shape[1]
    heads = width // HD
    groups = n_mp // heads
    sub = q_count // groups
    my_head = column % heads
    my_group = column // heads
    page_share = page_table.shape[1] // n_mp
    pages_dev = kv_pages.shape[0]
    deal_row = deal_table[0]
    request = row_index
    page_count = page_table.shape[1]

    q_out = queries.reshape(sub, groups, heads, HD).transpose(1, 2, 0, 3).reshape(n_mp, sub, HD)
    kv_heads = kv_pages.reshape(pages_dev, PAGE, 2, heads, HD).transpose(3, 0, 1, 2, 4)
    kv_out = jnp.tile(kv_heads, (groups, 1, 1, 1, 1)).reshape(n_mp, pages_dev * PAGE * 2, HD)
    both = lax.all_to_all(
        jnp.concatenate([q_out, kv_out], axis=1), "mp", split_axis=0, concat_axis=0, tiled=True
    )
    q_in = both[:, :sub, :]
    arrived = both[:, sub:, :].reshape(n_mp, pages_dev, PAGE, 2, HD)
    first_pos = cache_len[request] + deal_row % n_mp * q_count
    query_pos = (
        first_pos[:, None] + jnp.arange(sub, dtype=jnp.int32)[None, :] * groups + my_group
    ).reshape(-1)
    slot_ids = jnp.arange(n_mp * page_share, dtype=jnp.int32)
    physical = (row_index * n_mp + slot_ids // page_share) * pages_dev + slot_ids % page_share
    table_row = page_table[request]
    matches = table_row[None, :] == physical[:, None]
    logical = jnp.sum(
        jnp.where(matches, jnp.arange(page_count, dtype=jnp.int32)[None, :], 0), axis=1
    )
    key_pos = (logical[:, None] * PAGE + jnp.arange(PAGE, dtype=jnp.int32)[None, :]).reshape(-1)
    key_rows = arrived[:, :, :, 0, :].reshape(-1, HD)
    value_rows = arrived[:, :, :, 1, :].reshape(-1, HD)
    blended = attend_head(q_in.reshape(-1, HD), key_rows, value_rows, key_pos, query_pos)
    back = lax.all_to_all(blended.reshape(n_mp, sub, HD), "mp", split_axis=0, concat_axis=0, tiled=True)
    attended = back.reshape(groups, heads, sub, HD).transpose(2, 0, 1, 3).reshape(q_count, width)

    if n_dp == 2:
        w_pair = swap_dp(out_weight)
        wo_rows = jnp.where(
            row_index == 0,
            jnp.concatenate([out_weight, w_pair], axis=0),
            jnp.concatenate([w_pair, out_weight], axis=0),
        )
    else:
        wo_rows = lax.all_gather(out_weight, "dp", axis=0, tiled=True)
    projected = jnp.dot(
        attended,
        lax.all_gather(wo_rows, "mp", axis=1, tiled=True),
        preferred_element_type=jnp.float32,
    )
    resid_f = (hidden.astype(jnp.float32) + projected).astype(jnp.bfloat16).astype(jnp.float32)
    mean_square = jnp.mean(resid_f * resid_f, axis=1, keepdims=True)
    normed = (resid_f * lax.rsqrt(mean_square + epsilon) * norm_gain[None, :]).astype(jnp.bfloat16)
    capacity = min(q_count, q_count * TOPK * 4 // (3 * n_mp))
    flat_ids = expert_ids.reshape(-1)
    one_hot = (flat_ids[:, None] == jnp.arange(n_mp, dtype=jnp.int32)[None, :]).astype(jnp.int32)
    slot_of = jnp.sum(jnp.cumsum(one_hot, axis=0) * one_hot, axis=1) - 1
    target = (flat_ids * capacity + slot_of).reshape(q_count, TOPK)
    hits = target[:, :, None] == jnp.arange(n_mp * capacity, dtype=jnp.int32)[None, None, :]
    dispatch = jnp.any(hits, axis=1).astype(jnp.bfloat16)
    combine = jnp.sum(jnp.where(hits, expert_gates[:, :, None], 0.0), axis=1)
    ff_width = experts_out.shape[1]
    if n_dp == 2:
        in_other = swap_dp(experts_in)
        out_other = swap_dp(experts_out)
        normed, in_other = lax.optimization_barrier((normed, in_other))
    sending = lax.dot_general(
        dispatch, normed, (((0,), (0,)), ((), ())), preferred_element_type=jnp.float32
    ).astype(jnp.bfloat16)
    received = lax.all_to_all(
        sending.reshape(n_mp, capacity, d_model), "mp", split_axis=0, concat_axis=0, tiled=True
    )
    flat_rows = received.reshape(-1, d_model)
    if n_dp == 2:
        flat_rows, out_other = lax.optimization_barrier((flat_rows, out_other))
        half_in = experts_in.shape[1]
        rows_mine = lax.dynamic_slice_in_dim(flat_rows, row_index * half_in, half_in, axis=1)
        rows_other = lax.dynamic_slice_in_dim(flat_rows, (1 - row_index) * half_in, half_in, axis=1)
        gate_vals = jnp.dot(rows_mine, experts_in[0], preferred_element_type=jnp.float32) + jnp.dot(
            rows_other, in_other[0], preferred_element_type=jnp.float32
        )
        act = (jax.nn.silu(gate_vals[:, :ff_width]) * gate_vals[:, ff_width:]).astype(jnp.bfloat16)
        part_mine = jnp.dot(act, experts_out[0], preferred_element_type=jnp.float32).astype(jnp.bfloat16)
        part_other = jnp.dot(act, out_other[0], preferred_element_type=jnp.float32).astype(jnp.bfloat16)
        outcome = jnp.where(
            row_index == 0,
            jnp.concatenate([part_mine, part_other], axis=1),
            jnp.concatenate([part_other, part_mine], axis=1),
        )
    else:
        gate_up = lax.all_gather(experts_in, "dp", axis=1, tiled=True)
        down = lax.all_gather(experts_out, "dp", axis=2, tiled=True)
        gate_vals = jnp.dot(flat_rows, gate_up[0], preferred_element_type=jnp.float32)
        act = (jax.nn.silu(gate_vals[:, :ff_width]) * gate_vals[:, ff_width:]).astype(jnp.bfloat16)
        outcome = jnp.dot(act, down[0], preferred_element_type=jnp.float32).astype(jnp.bfloat16)
    results = lax.all_to_all(
        outcome.reshape(n_mp, capacity, d_model), "mp", split_axis=0, concat_axis=0, tiled=True
    )
    expert_sum = jnp.dot(
        combine,
        results.reshape(-1, d_model).astype(jnp.float32),
        precision=lax.Precision.HIGHEST,
        preferred_element_type=jnp.float32,
    )
    return (resid_f + expert_sum).astype(jnp.bfloat16)


def solution(mesh):
    in_specs = (
        P(("dp", "mp"), None),
        P(("dp", "mp"), None),
        P(("dp", "mp"), None, None, None),
        P(),
        P(),
        P("dp", None),
        P("dp", "mp"),
        P(),
        P(("dp", "mp"), None),
        P(("dp", "mp"), None),
        P("mp", "dp", None),
        P("mp", None, "dp"),
    )
    out_specs = P(("dp", "mp"), None)
    return jax.shard_map(
        on_device, mesh=mesh, in_specs=in_specs, out_specs=out_specs, check_vma=False
    )
```

```python
import math

import jax
import jax.numpy as jnp
from jax import lax
from jax.sharding import PartitionSpec as P

HEADS = 8
HD = 128
TOPK = 6
PAGE = 16


epsilon = 1e-06


def attend_head(q_rows, key_rows, value_rows, key_pos, query_pos):
    scores = jnp.dot(q_rows, key_rows.T, preferred_element_type=jnp.float32) * (1.0 / math.sqrt(HD))
    allowed = key_pos[None, :] <= query_pos[:, None]
    scores = jnp.where(allowed, scores, -1e30)
    row_max = jnp.max(scores, axis=1, keepdims=True)
    weights = jnp.exp(scores - row_max)
    weights_bf = (weights / jnp.sum(weights, axis=1, keepdims=True)).astype(jnp.bfloat16)
    blended = jnp.dot(weights_bf, value_rows, preferred_element_type=jnp.float32)
    return blended.astype(jnp.bfloat16)


def swap_dp(x):
    return lax.ppermute(x, "dp", [(0, 1), (1, 0)])


def on_device(
    queries,
    hidden,
    kv_pages,
    page_table,
    cache_len,
    deal_table,
    out_weight,
    norm_gain,
    expert_ids,
    expert_gates,
    experts_in,
    experts_out,
):
    n_mp = lax.axis_size("mp")
    n_dp = lax.axis_size("dp")
    row_index = lax.axis_index("dp")
    column = lax.axis_index("mp")
    q_count = queries.shape[0]
    width = queries.shape[1]
    d_model = hidden.shape[1]
    heads = width // HD
    groups = n_mp // heads
    sub = q_count // groups
    my_head = column % heads
    my_group = column // heads
    page_share = page_table.shape[1] // n_mp
    pages_dev = kv_pages.shape[0]
    deal_row = deal_table[0]
    request = row_index
    page_count = page_table.shape[1]

    q_out = queries.reshape(sub, groups, heads, HD).transpose(1, 2, 0, 3).reshape(n_mp, sub, HD)
    kv_heads = kv_pages.reshape(pages_dev, PAGE, 2, heads, HD).transpose(3, 0, 1, 2, 4)
    kv_out = jnp.tile(kv_heads, (groups, 1, 1, 1, 1)).reshape(n_mp, pages_dev * PAGE * 2, HD)
    both = lax.all_to_all(
        jnp.concatenate([q_out, kv_out], axis=1), "mp", split_axis=0, concat_axis=0, tiled=True
    )
    q_in = both[:, :sub, :]
    arrived = both[:, sub:, :].reshape(n_mp, pages_dev, PAGE, 2, HD)
    first_pos = cache_len[request] + deal_row % n_mp * q_count
    query_pos = (
        first_pos[:, None] + jnp.arange(sub, dtype=jnp.int32)[None, :] * groups + my_group
    ).reshape(-1)
    slot_ids = jnp.arange(n_mp * page_share, dtype=jnp.int32)
    physical = (row_index * n_mp + slot_ids // page_share) * pages_dev + slot_ids % page_share
    table_row = page_table[request]
    matches = table_row[None, :] == physical[:, None]
    logical = jnp.sum(
        jnp.where(matches, jnp.arange(page_count, dtype=jnp.int32)[None, :], 0), axis=1
    )
    key_pos = (logical[:, None] * PAGE + jnp.arange(PAGE, dtype=jnp.int32)[None, :]).reshape(-1)
    key_rows = arrived[:, :, :, 0, :].reshape(-1, HD)
    value_rows = arrived[:, :, :, 1, :].reshape(-1, HD)
    blended = attend_head(q_in.reshape(-1, HD), key_rows, value_rows, key_pos, query_pos)
    back = lax.all_to_all(blended.reshape(n_mp, sub, HD), "mp", split_axis=0, concat_axis=0, tiled=True)
    attended = back.reshape(groups, heads, sub, HD).transpose(2, 0, 1, 3).reshape(q_count, width)

    if n_dp == 2:
        w_pair = swap_dp(out_weight)
        wo_rows = jnp.where(
            row_index == 0,
            jnp.concatenate([out_weight, w_pair], axis=0),
            jnp.concatenate([w_pair, out_weight], axis=0),
        )
    else:
        wo_rows = lax.all_gather(out_weight, "dp", axis=0, tiled=True)
    half = n_mp // 2
    mirror = lax.ppermute(wo_rows, "mp", [(m, (m + half) % n_mp) for m in range(n_mp)])
    sides = [list(range(half)), list(range(half, n_mp))]
    gathered = lax.all_gather(
        jnp.stack([wo_rows, mirror]), "mp", axis=1, axis_index_groups=sides
    )
    near_side = column // half == 0
    w_stack = jnp.concatenate(
        [
            jnp.where(near_side, gathered[0], gathered[1]),
            jnp.where(near_side, gathered[1], gathered[0]),
        ],
        axis=0,
    )
    projected = jnp.einsum(
        "tk,mkc->tmc", attended, w_stack, preferred_element_type=jnp.float32
    ).reshape(q_count, d_model)
    resid_f = (hidden.astype(jnp.float32) + projected).astype(jnp.bfloat16).astype(jnp.float32)
    mean_square = jnp.mean(resid_f * resid_f, axis=1, keepdims=True)
    normed = (resid_f * lax.rsqrt(mean_square + epsilon) * norm_gain[None, :]).astype(jnp.bfloat16)
    capacity = min(q_count, q_count * TOPK * 4 // (3 * n_mp))
    flat_ids = expert_ids.reshape(-1)
    one_hot = (flat_ids[:, None] == jnp.arange(n_mp, dtype=jnp.int32)[None, :]).astype(jnp.int32)
    slot_of = jnp.sum(jnp.cumsum(one_hot, axis=0) * one_hot, axis=1) - 1
    target = (flat_ids * capacity + slot_of).reshape(q_count, TOPK)
    hits = target[:, :, None] == jnp.arange(n_mp * capacity, dtype=jnp.int32)[None, None, :]
    dispatch = jnp.any(hits, axis=1).astype(jnp.bfloat16)
    combine = jnp.sum(jnp.where(hits, expert_gates[:, :, None], 0.0), axis=1)
    ff_width = experts_out.shape[1]
    if n_dp == 2:
        in_other = swap_dp(experts_in)
        out_other = swap_dp(experts_out)
        normed, in_other = lax.optimization_barrier((normed, in_other))
    sending = lax.dot_general(
        dispatch, normed, (((0,), (0,)), ((), ())), preferred_element_type=jnp.float32
    ).astype(jnp.bfloat16)
    received = lax.all_to_all(
        sending.reshape(n_mp, capacity, d_model), "mp", split_axis=0, concat_axis=0, tiled=True
    )
    flat_rows = received.reshape(-1, d_model)
    if n_dp == 2:
        flat_rows, out_other = lax.optimization_barrier((flat_rows, out_other))
        half_in = experts_in.shape[1]
        rows_mine = lax.dynamic_slice_in_dim(flat_rows, row_index * half_in, half_in, axis=1)
        rows_other = lax.dynamic_slice_in_dim(flat_rows, (1 - row_index) * half_in, half_in, axis=1)
        gate_vals = jnp.dot(rows_mine, experts_in[0], preferred_element_type=jnp.float32) + jnp.dot(
            rows_other, in_other[0], preferred_element_type=jnp.float32
        )
        act = (jax.nn.silu(gate_vals[:, :ff_width]) * gate_vals[:, ff_width:]).astype(jnp.bfloat16)
        part_mine = jnp.dot(act, experts_out[0], preferred_element_type=jnp.float32).astype(jnp.bfloat16)
        part_other = jnp.dot(act, out_other[0], preferred_element_type=jnp.float32).astype(jnp.bfloat16)
        outcome = jnp.where(
            row_index == 0,
            jnp.concatenate([part_mine, part_other], axis=1),
            jnp.concatenate([part_other, part_mine], axis=1),
        )
    else:
        gate_up = lax.all_gather(experts_in, "dp", axis=1, tiled=True)
        down = lax.all_gather(experts_out, "dp", axis=2, tiled=True)
        gate_vals = jnp.dot(flat_rows, gate_up[0], preferred_element_type=jnp.float32)
        act = (jax.nn.silu(gate_vals[:, :ff_width]) * gate_vals[:, ff_width:]).astype(jnp.bfloat16)
        outcome = jnp.dot(act, down[0], preferred_element_type=jnp.float32).astype(jnp.bfloat16)
    results = lax.all_to_all(
        outcome.reshape(n_mp, capacity, d_model), "mp", split_axis=0, concat_axis=0, tiled=True
    )
    expert_sum = jnp.dot(
        combine,
        results.reshape(-1, d_model).astype(jnp.float32),
        precision=lax.Precision.HIGHEST,
        preferred_element_type=jnp.float32,
    )
    return (resid_f + expert_sum).astype(jnp.bfloat16)


def solution(mesh):
    in_specs = (
        P(("dp", "mp"), None),
        P(("dp", "mp"), None),
        P(("dp", "mp"), None, None, None),
        P(),
        P(),
        P("dp", None),
        P("dp", "mp"),
        P(),
        P(("dp", "mp"), None),
        P(("dp", "mp"), None),
        P("mp", "dp", None),
        P("mp", None, "dp"),
    )
    out_specs = P(("dp", "mp"), None)
    return jax.shard_map(
        on_device, mesh=mesh, in_specs=in_specs, out_specs=out_specs, check_vma=False
    )
```

```python
import math

import jax
import jax.numpy as jnp
from jax import lax
from jax.sharding import PartitionSpec as P

HEADS = 8
HD = 128
TOPK = 6
PAGE = 16


epsilon = 1e-06


def attend_head(q_rows, key_rows, value_rows, key_pos, query_pos):
    scores = jnp.dot(q_rows, key_rows.T, preferred_element_type=jnp.float32) * (1.0 / math.sqrt(HD))
    allowed = key_pos[None, :] <= query_pos[:, None]
    scores = jnp.where(allowed, scores, -1e30)
    row_max = jnp.max(scores, axis=1, keepdims=True)
    weights = jnp.exp(scores - row_max)
    weights_bf = (weights / jnp.sum(weights, axis=1, keepdims=True)).astype(jnp.bfloat16)
    blended = jnp.dot(weights_bf, value_rows, preferred_element_type=jnp.float32)
    return blended.astype(jnp.bfloat16)


def swap_dp(x):
    return lax.ppermute(x, "dp", [(0, 1), (1, 0)])


def on_device(
    queries,
    hidden,
    kv_pages,
    page_table,
    cache_len,
    deal_table,
    out_weight,
    norm_gain,
    expert_ids,
    expert_gates,
    experts_in,
    experts_out,
):
    n_mp = lax.axis_size("mp")
    n_dp = lax.axis_size("dp")
    row_index = lax.axis_index("dp")
    column = lax.axis_index("mp")
    q_count = queries.shape[0]
    width = queries.shape[1]
    d_model = hidden.shape[1]
    heads = width // HD
    groups = n_mp // heads
    sub = q_count // groups
    my_head = column % heads
    my_group = column // heads
    page_share = page_table.shape[1] // n_mp
    pages_dev = kv_pages.shape[0]
    deal_row = deal_table[0]
    request = row_index
    page_count = page_table.shape[1]

    q_out = queries.reshape(sub, groups, heads, HD).transpose(1, 2, 0, 3).reshape(n_mp, sub, HD)
    kv_heads = kv_pages.reshape(pages_dev, PAGE, 2, heads, HD).transpose(3, 0, 1, 2, 4)
    kv_out = jnp.tile(kv_heads, (groups, 1, 1, 1, 1)).reshape(n_mp, pages_dev * PAGE * 2, HD)
    both = lax.all_to_all(
        jnp.concatenate([q_out, kv_out], axis=1), "mp", split_axis=0, concat_axis=0, tiled=True
    )
    q_in = both[:, :sub, :]
    arrived = both[:, sub:, :].reshape(n_mp, pages_dev, PAGE, 2, HD)
    first_pos = cache_len[request] + deal_row % n_mp * q_count
    query_pos = (
        first_pos[:, None] + jnp.arange(sub, dtype=jnp.int32)[None, :] * groups + my_group
    ).reshape(-1)
    slot_ids = jnp.arange(n_mp * page_share, dtype=jnp.int32)
    physical = (row_index * n_mp + slot_ids // page_share) * pages_dev + slot_ids % page_share
    table_row = page_table[request]
    matches = table_row[None, :] == physical[:, None]
    logical = jnp.sum(
        jnp.where(matches, jnp.arange(page_count, dtype=jnp.int32)[None, :], 0), axis=1
    )
    key_pos = (logical[:, None] * PAGE + jnp.arange(PAGE, dtype=jnp.int32)[None, :]).reshape(-1)
    key_rows = arrived[:, :, :, 0, :].reshape(-1, HD)
    value_rows = arrived[:, :, :, 1, :].reshape(-1, HD)
    blended = attend_head(q_in.reshape(-1, HD), key_rows, value_rows, key_pos, query_pos)
    back = lax.all_to_all(blended.reshape(n_mp, sub, HD), "mp", split_axis=0, concat_axis=0, tiled=True)
    attended = back.reshape(groups, heads, sub, HD).transpose(2, 0, 1, 3).reshape(q_count, width)

    if n_dp == 2:
        w_pair = swap_dp(out_weight)
        wo_rows = jnp.where(
            row_index == 0,
            jnp.concatenate([out_weight, w_pair], axis=0),
            jnp.concatenate([w_pair, out_weight], axis=0),
        )
    else:
        wo_rows = lax.all_gather(out_weight, "dp", axis=0, tiled=True)
    projected = jnp.dot(
        attended,
        lax.all_gather(wo_rows, "mp", axis=1, tiled=True),
        preferred_element_type=jnp.float32,
    )
    resid_f = (hidden.astype(jnp.float32) + projected).astype(jnp.bfloat16).astype(jnp.float32)
    mean_square = jnp.mean(resid_f * resid_f, axis=1, keepdims=True)
    normed = (resid_f * lax.rsqrt(mean_square + epsilon) * norm_gain[None, :]).astype(jnp.bfloat16)
    capacity = min(q_count, q_count * TOPK * 4 // (3 * n_mp))
    flat_ids = expert_ids.reshape(-1)
    one_hot = (flat_ids[:, None] == jnp.arange(n_mp, dtype=jnp.int32)[None, :]).astype(jnp.int32)
    slot_of = jnp.sum(jnp.cumsum(one_hot, axis=0) * one_hot, axis=1) - 1
    target = (flat_ids * capacity + slot_of).reshape(q_count, TOPK)
    hits = target[:, :, None] == jnp.arange(n_mp * capacity, dtype=jnp.int32)[None, None, :]
    dispatch = jnp.any(hits, axis=1).astype(jnp.bfloat16)
    combine = jnp.sum(jnp.where(hits, expert_gates[:, :, None], 0.0), axis=1)
    ff_width = experts_out.shape[1]
    if n_dp == 2:
        in_other = swap_dp(experts_in)
        out_other = swap_dp(experts_out)
        normed, in_other = lax.optimization_barrier((normed, in_other))
    sending = lax.dot_general(
        dispatch, normed, (((0,), (0,)), ((), ())), preferred_element_type=jnp.float32
    ).astype(jnp.bfloat16)
    received = lax.all_to_all(
        sending.reshape(n_mp, capacity, d_model), "mp", split_axis=0, concat_axis=0, tiled=True
    )
    flat_rows = received.reshape(-1, d_model)
    if n_dp == 2:
        first = row_index == 0
        gate_up = jnp.where(
            first,
            jnp.concatenate([experts_in[0], in_other[0]], axis=0),
            jnp.concatenate([in_other[0], experts_in[0]], axis=0),
        )
        flat_rows, out_other = lax.optimization_barrier((flat_rows, out_other))
        down = jnp.where(
            first,
            jnp.concatenate([experts_out[0], out_other[0]], axis=1),
            jnp.concatenate([out_other[0], experts_out[0]], axis=1),
        )
    else:
        gate_up = lax.all_gather(experts_in, "dp", axis=1, tiled=True)[0]
        down = lax.all_gather(experts_out, "dp", axis=2, tiled=True)[0]
    gate_vals = jnp.dot(flat_rows, gate_up, preferred_element_type=jnp.float32)
    act = (jax.nn.silu(gate_vals[:, :ff_width]) * gate_vals[:, ff_width:]).astype(jnp.bfloat16)
    outcome = jnp.dot(act, down, preferred_element_type=jnp.float32).astype(jnp.bfloat16)
    results = lax.all_to_all(
        outcome.reshape(n_mp, capacity, d_model), "mp", split_axis=0, concat_axis=0, tiled=True
    )
    expert_sum = jnp.dot(
        combine,
        results.reshape(-1, d_model).astype(jnp.float32),
        precision=lax.Precision.HIGHEST,
        preferred_element_type=jnp.float32,
    )
    return (resid_f + expert_sum).astype(jnp.bfloat16)


def solution(mesh):
    in_specs = (
        P(("dp", "mp"), None),
        P(("dp", "mp"), None),
        P(("dp", "mp"), None, None, None),
        P(),
        P(),
        P("dp", None),
        P("dp", "mp"),
        P(),
        P(("dp", "mp"), None),
        P(("dp", "mp"), None),
        P("mp", "dp", None),
        P("mp", None, "dp"),
    )
    out_specs = P(("dp", "mp"), None)
    return jax.shard_map(
        on_device, mesh=mesh, in_specs=in_specs, out_specs=out_specs, check_vma=False
    )
```

```python
import math

import jax
import jax.numpy as jnp
from jax import lax
from jax.sharding import PartitionSpec as P

HEADS = 8
HD = 128
TOPK = 6
PAGE = 16


epsilon = 1e-06


def attend_head(q_rows, key_rows, value_rows, key_pos, query_pos):
    scores = jnp.dot(q_rows, key_rows.T, preferred_element_type=jnp.float32) * (1.0 / math.sqrt(HD))
    allowed = key_pos[None, :] <= query_pos[:, None]
    scores = jnp.where(allowed, scores, -1e30)
    row_max = jnp.max(scores, axis=1, keepdims=True)
    weights = jnp.exp(scores - row_max)
    weights_bf = (weights / jnp.sum(weights, axis=1, keepdims=True)).astype(jnp.bfloat16)
    blended = jnp.dot(weights_bf, value_rows, preferred_element_type=jnp.float32)
    return blended.astype(jnp.bfloat16)


def swap_dp(x):
    return lax.ppermute(x, "dp", [(0, 1), (1, 0)])


def on_device(
    queries,
    hidden,
    kv_pages,
    page_table,
    cache_len,
    deal_table,
    out_weight,
    norm_gain,
    expert_ids,
    expert_gates,
    experts_in,
    experts_out,
):
    n_mp = lax.axis_size("mp")
    n_dp = lax.axis_size("dp")
    row_index = lax.axis_index("dp")
    column = lax.axis_index("mp")
    q_count = queries.shape[0]
    width = queries.shape[1]
    d_model = hidden.shape[1]
    heads = width // HD
    groups = n_mp // heads
    sub = q_count // groups
    my_head = column % heads
    my_group = column // heads
    page_share = page_table.shape[1] // n_mp
    pages_dev = kv_pages.shape[0]
    deal_row = deal_table[0]
    request = row_index
    page_count = page_table.shape[1]

    q_out = queries.reshape(sub, groups, heads, HD).transpose(1, 2, 0, 3).reshape(n_mp, sub, HD)
    kv_heads = kv_pages.reshape(pages_dev, PAGE, 2, heads, HD).transpose(3, 0, 1, 2, 4)
    kv_out = jnp.tile(kv_heads, (groups, 1, 1, 1, 1)).reshape(n_mp, pages_dev * PAGE * 2, HD)
    both = lax.all_to_all(
        jnp.concatenate([q_out, kv_out], axis=1), "mp", split_axis=0, concat_axis=0, tiled=True
    )
    q_in = both[:, :sub, :]
    arrived = both[:, sub:, :].reshape(n_mp, pages_dev, PAGE, 2, HD)
    first_pos = cache_len[request] + deal_row % n_mp * q_count
    query_pos = (
        first_pos[:, None] + jnp.arange(sub, dtype=jnp.int32)[None, :] * groups + my_group
    ).reshape(-1)
    slot_ids = jnp.arange(n_mp * page_share, dtype=jnp.int32)
    physical = (row_index * n_mp + slot_ids // page_share) * pages_dev + slot_ids % page_share
    table_row = page_table[request]
    matches = table_row[None, :] == physical[:, None]
    logical = jnp.sum(
        jnp.where(matches, jnp.arange(page_count, dtype=jnp.int32)[None, :], 0), axis=1
    )
    key_pos = (logical[:, None] * PAGE + jnp.arange(PAGE, dtype=jnp.int32)[None, :]).reshape(-1)
    key_rows = arrived[:, :, :, 0, :].reshape(-1, HD)
    value_rows = arrived[:, :, :, 1, :].reshape(-1, HD)
    blended = attend_head(q_in.reshape(-1, HD), key_rows, value_rows, key_pos, query_pos)
    back = lax.all_to_all(blended.reshape(n_mp, sub, HD), "mp", split_axis=0, concat_axis=0, tiled=True)
    attended = back.reshape(groups, heads, sub, HD).transpose(2, 0, 1, 3).reshape(q_count, width)

    if n_dp == 2:
        w_pair = swap_dp(out_weight)
        wo_rows = jnp.where(
            row_index == 0,
            jnp.concatenate([out_weight, w_pair], axis=0),
            jnp.concatenate([w_pair, out_weight], axis=0),
        )
    else:
        wo_rows = lax.all_gather(out_weight, "dp", axis=0, tiled=True)
    bits = n_mp.bit_length() - 1
    if n_mp == 1 << bits:
        block = wo_rows[None]
        for b in reversed(range(bits)):
            pair = lax.ppermute(block, "mp", [(m, m ^ (1 << b)) for m in range(n_mp)])
            low = (column >> b) % 2 == 0
            block = jnp.concatenate(
                [jnp.where(low, block, pair), jnp.where(low, pair, block)], axis=0
            )
        by_shard = jnp.einsum("tk,jkc->tjc", attended, block, preferred_element_type=jnp.float32)
        order = (0,) + tuple(range(bits, 0, -1)) + (bits + 1,)
        shard_w = wo_rows.shape[1]
        projected = (
            by_shard.reshape((q_count,) + (2,) * bits + (shard_w,))
            .transpose(order)
            .reshape(q_count, d_model)
        )
    else:
        projected = jnp.dot(
            attended,
            lax.all_gather(wo_rows, "mp", axis=1, tiled=True),
            preferred_element_type=jnp.float32,
        )
    resid_f = (hidden.astype(jnp.float32) + projected).astype(jnp.bfloat16).astype(jnp.float32)
    mean_square = jnp.mean(resid_f * resid_f, axis=1, keepdims=True)
    normed = (resid_f * lax.rsqrt(mean_square + epsilon) * norm_gain[None, :]).astype(jnp.bfloat16)
    capacity = min(q_count, q_count * TOPK * 4 // (3 * n_mp))
    flat_ids = expert_ids.reshape(-1)
    one_hot = (flat_ids[:, None] == jnp.arange(n_mp, dtype=jnp.int32)[None, :]).astype(jnp.int32)
    slot_of = jnp.sum(jnp.cumsum(one_hot, axis=0) * one_hot, axis=1) - 1
    target = (flat_ids * capacity + slot_of).reshape(q_count, TOPK)
    hits = target[:, :, None] == jnp.arange(n_mp * capacity, dtype=jnp.int32)[None, None, :]
    dispatch = jnp.any(hits, axis=1).astype(jnp.bfloat16)
    combine = jnp.sum(jnp.where(hits, expert_gates[:, :, None], 0.0), axis=1)
    ff_width = experts_out.shape[1]
    if n_dp == 2:
        in_other = swap_dp(experts_in)
        out_other = swap_dp(experts_out)
        normed, in_other = lax.optimization_barrier((normed, in_other))
    sending = lax.dot_general(
        dispatch, normed, (((0,), (0,)), ((), ())), preferred_element_type=jnp.float32
    ).astype(jnp.bfloat16)
    received = lax.all_to_all(
        sending.reshape(n_mp, capacity, d_model), "mp", split_axis=0, concat_axis=0, tiled=True
    )
    flat_rows = received.reshape(-1, d_model)
    if n_dp == 2:
        first = row_index == 0
        gate_up = jnp.where(
            first,
            jnp.concatenate([experts_in[0], in_other[0]], axis=0),
            jnp.concatenate([in_other[0], experts_in[0]], axis=0),
        )
        flat_rows, out_other = lax.optimization_barrier((flat_rows, out_other))
        down = jnp.where(
            first,
            jnp.concatenate([experts_out[0], out_other[0]], axis=1),
            jnp.concatenate([out_other[0], experts_out[0]], axis=1),
        )
    else:
        gate_up = lax.all_gather(experts_in, "dp", axis=1, tiled=True)[0]
        down = lax.all_gather(experts_out, "dp", axis=2, tiled=True)[0]
    gate_vals = jnp.dot(flat_rows, gate_up, preferred_element_type=jnp.float32)
    act = (jax.nn.silu(gate_vals[:, :ff_width]) * gate_vals[:, ff_width:]).astype(jnp.bfloat16)
    outcome = jnp.dot(act, down, preferred_element_type=jnp.float32).astype(jnp.bfloat16)
    results = lax.all_to_all(
        outcome.reshape(n_mp, capacity, d_model), "mp", split_axis=0, concat_axis=0, tiled=True
    )
    expert_sum = jnp.dot(
        combine,
        results.reshape(-1, d_model).astype(jnp.float32),
        precision=lax.Precision.HIGHEST,
        preferred_element_type=jnp.float32,
    )
    return (resid_f + expert_sum).astype(jnp.bfloat16)


def solution(mesh):
    in_specs = (
        P(("dp", "mp"), None),
        P(("dp", "mp"), None),
        P(("dp", "mp"), None, None, None),
        P(),
        P(),
        P("dp", None),
        P("dp", "mp"),
        P(),
        P(("dp", "mp"), None),
        P(("dp", "mp"), None),
        P("mp", "dp", None),
        P("mp", None, "dp"),
    )
    out_specs = P(("dp", "mp"), None)
    return jax.shard_map(
        on_device, mesh=mesh, in_specs=in_specs, out_specs=out_specs, check_vma=False
    )
```

```python
import math

import jax
import jax.numpy as jnp
from jax import lax
from jax.sharding import PartitionSpec as P

HEADS = 8
HD = 128
TOPK = 6
PAGE = 16


epsilon = 1e-06


def attend_head(q_rows, key_rows, value_rows, key_pos, query_pos):
    scores = jnp.dot(q_rows, key_rows.T, preferred_element_type=jnp.float32) * (1.0 / math.sqrt(HD))
    allowed = key_pos[None, :] <= query_pos[:, None]
    scores = jnp.where(allowed, scores, -1e30)
    row_max = jnp.max(scores, axis=1, keepdims=True)
    weights = jnp.exp(scores - row_max)
    weights_bf = (weights / jnp.sum(weights, axis=1, keepdims=True)).astype(jnp.bfloat16)
    blended = jnp.dot(weights_bf, value_rows, preferred_element_type=jnp.float32)
    return blended.astype(jnp.bfloat16)


def swap_dp(x):
    return lax.ppermute(x, "dp", [(0, 1), (1, 0)])


def on_device(
    queries,
    hidden,
    kv_pages,
    page_table,
    cache_len,
    deal_table,
    out_weight,
    norm_gain,
    expert_ids,
    expert_gates,
    experts_in,
    experts_out,
):
    n_mp = lax.axis_size("mp")
    n_dp = lax.axis_size("dp")
    row_index = lax.axis_index("dp")
    column = lax.axis_index("mp")
    q_count = queries.shape[0]
    width = queries.shape[1]
    d_model = hidden.shape[1]
    heads = width // HD
    groups = n_mp // heads
    sub = q_count // groups
    my_head = column % heads
    my_group = column // heads
    page_share = page_table.shape[1] // n_mp
    pages_dev = kv_pages.shape[0]
    deal_row = deal_table[0]
    request = row_index
    page_count = page_table.shape[1]

    q_out = queries.reshape(sub, groups, heads, HD).transpose(1, 2, 0, 3).reshape(n_mp, sub, HD)
    kv_heads = kv_pages.reshape(pages_dev, PAGE, 2, heads, HD).transpose(3, 0, 1, 2, 4)
    kv_out = jnp.tile(kv_heads, (groups, 1, 1, 1, 1)).reshape(n_mp, pages_dev * PAGE * 2, HD)
    both = lax.all_to_all(
        jnp.concatenate([q_out, kv_out], axis=1), "mp", split_axis=0, concat_axis=0, tiled=True
    )
    q_in = both[:, :sub, :]
    arrived = both[:, sub:, :].reshape(n_mp, pages_dev, PAGE, 2, HD)
    first_pos = cache_len[request] + deal_row % n_mp * q_count
    query_pos = (
        first_pos[:, None] + jnp.arange(sub, dtype=jnp.int32)[None, :] * groups + my_group
    ).reshape(-1)
    slot_ids = jnp.arange(n_mp * page_share, dtype=jnp.int32)
    physical = (row_index * n_mp + slot_ids // page_share) * pages_dev + slot_ids % page_share
    table_row = page_table[request]
    matches = table_row[None, :] == physical[:, None]
    logical = jnp.sum(
        jnp.where(matches, jnp.arange(page_count, dtype=jnp.int32)[None, :], 0), axis=1
    )
    key_pos = (logical[:, None] * PAGE + jnp.arange(PAGE, dtype=jnp.int32)[None, :]).reshape(-1)
    key_rows = arrived[:, :, :, 0, :].reshape(-1, HD)
    value_rows = arrived[:, :, :, 1, :].reshape(-1, HD)
    blended = attend_head(q_in.reshape(-1, HD), key_rows, value_rows, key_pos, query_pos)

    def gather_heads(rows):
        back = lax.all_to_all(rows.reshape(n_mp, sub, HD), "mp", split_axis=0, concat_axis=0, tiled=True)
        return back.reshape(groups, heads, sub, HD).transpose(2, 0, 1, 3).reshape(q_count, width)

    if n_dp == 2:
        w_pair = swap_dp(out_weight)
        wo_rows = jnp.where(
            row_index == 0,
            jnp.concatenate([out_weight, w_pair], axis=0),
            jnp.concatenate([w_pair, out_weight], axis=0),
        )
    else:
        wo_rows = lax.all_gather(out_weight, "dp", axis=0, tiled=True)
    bits = n_mp.bit_length() - 1
    if n_mp == 1 << bits:
        block = wo_rows[None]
        for b in reversed(range(bits)):
            if b == 1:
                block, blended = lax.optimization_barrier((block, blended))
            pair = lax.ppermute(block, "mp", [(m, m ^ (1 << b)) for m in range(n_mp)])
            low = (column >> b) % 2 == 0
            block = jnp.concatenate(
                [jnp.where(low, block, pair), jnp.where(low, pair, block)], axis=0
            )
        attended = gather_heads(blended)
        by_shard = jnp.einsum("tk,jkc->tjc", attended, block, preferred_element_type=jnp.float32)
        order = (0,) + tuple(range(bits, 0, -1)) + (bits + 1,)
        shard_w = wo_rows.shape[1]
        projected = (
            by_shard.reshape((q_count,) + (2,) * bits + (shard_w,))
            .transpose(order)
            .reshape(q_count, d_model)
        )
    else:
        attended = gather_heads(blended)
        projected = jnp.dot(
            attended,
            lax.all_gather(wo_rows, "mp", axis=1, tiled=True),
            preferred_element_type=jnp.float32,
        )
    resid_f = (hidden.astype(jnp.float32) + projected).astype(jnp.bfloat16).astype(jnp.float32)
    mean_square = jnp.mean(resid_f * resid_f, axis=1, keepdims=True)
    normed = (resid_f * lax.rsqrt(mean_square + epsilon) * norm_gain[None, :]).astype(jnp.bfloat16)
    capacity = min(q_count, q_count * TOPK * 4 // (3 * n_mp))
    flat_ids = expert_ids.reshape(-1)
    one_hot = (flat_ids[:, None] == jnp.arange(n_mp, dtype=jnp.int32)[None, :]).astype(jnp.int32)
    slot_of = jnp.sum(jnp.cumsum(one_hot, axis=0) * one_hot, axis=1) - 1
    target = (flat_ids * capacity + slot_of).reshape(q_count, TOPK)
    hits = target[:, :, None] == jnp.arange(n_mp * capacity, dtype=jnp.int32)[None, None, :]
    dispatch = jnp.any(hits, axis=1).astype(jnp.bfloat16)
    combine = jnp.sum(jnp.where(hits, expert_gates[:, :, None], 0.0), axis=1)
    ff_width = experts_out.shape[1]
    if n_dp == 2:
        in_other = swap_dp(experts_in)
        out_other = swap_dp(experts_out)
        normed, in_other = lax.optimization_barrier((normed, in_other))
    sending = lax.dot_general(
        dispatch, normed, (((0,), (0,)), ((), ())), preferred_element_type=jnp.float32
    ).astype(jnp.bfloat16)
    received = lax.all_to_all(
        sending.reshape(n_mp, capacity, d_model), "mp", split_axis=0, concat_axis=0, tiled=True
    )
    flat_rows = received.reshape(-1, d_model)
    if n_dp == 2:
        first = row_index == 0
        gate_up = jnp.where(
            first,
            jnp.concatenate([experts_in[0], in_other[0]], axis=0),
            jnp.concatenate([in_other[0], experts_in[0]], axis=0),
        )
        flat_rows, out_other, gate_up = lax.optimization_barrier((flat_rows, out_other, gate_up))
        down = jnp.where(
            first,
            jnp.concatenate([experts_out[0], out_other[0]], axis=1),
            jnp.concatenate([out_other[0], experts_out[0]], axis=1),
        )
    else:
        gate_up = lax.all_gather(experts_in, "dp", axis=1, tiled=True)[0]
        down = lax.all_gather(experts_out, "dp", axis=2, tiled=True)[0]
    gate_vals = jnp.dot(flat_rows, gate_up, preferred_element_type=jnp.float32)
    act = (jax.nn.silu(gate_vals[:, :ff_width]) * gate_vals[:, ff_width:]).astype(jnp.bfloat16)
    outcome = jnp.dot(act, down, preferred_element_type=jnp.float32).astype(jnp.bfloat16)
    results = lax.all_to_all(
        outcome.reshape(n_mp, capacity, d_model), "mp", split_axis=0, concat_axis=0, tiled=True
    )
    expert_sum = jnp.dot(
        combine,
        results.reshape(-1, d_model).astype(jnp.float32),
        precision=lax.Precision.HIGHEST,
        preferred_element_type=jnp.float32,
    )
    return (resid_f + expert_sum).astype(jnp.bfloat16)


def solution(mesh):
    in_specs = (
        P(("dp", "mp"), None),
        P(("dp", "mp"), None),
        P(("dp", "mp"), None, None, None),
        P(),
        P(),
        P("dp", None),
        P("dp", "mp"),
        P(),
        P(("dp", "mp"), None),
        P(("dp", "mp"), None),
        P("mp", "dp", None),
        P("mp", None, "dp"),
    )
    out_specs = P(("dp", "mp"), None)
    return jax.shard_map(
        on_device, mesh=mesh, in_specs=in_specs, out_specs=out_specs, check_vma=False
    )
```

```python
import math

import jax
import jax.numpy as jnp
from jax import lax
from jax.sharding import PartitionSpec as P

HEADS = 8
HD = 128
TOPK = 6
PAGE = 16


epsilon = 1e-06


def attend_head(q_rows, key_rows, value_rows, key_pos, query_pos):
    scores = jnp.dot(q_rows, key_rows.T, preferred_element_type=jnp.float32) * (1.0 / math.sqrt(HD))
    allowed = key_pos[None, :] <= query_pos[:, None]
    scores = jnp.where(allowed, scores, -1e30)
    row_max = jnp.max(scores, axis=1, keepdims=True)
    weights = jnp.exp(scores - row_max)
    weights_bf = (weights / jnp.sum(weights, axis=1, keepdims=True)).astype(jnp.bfloat16)
    blended = jnp.dot(weights_bf, value_rows, preferred_element_type=jnp.float32)
    return blended.astype(jnp.bfloat16)


def swap_dp(x):
    return lax.ppermute(x, "dp", [(0, 1), (1, 0)])


def on_device(
    queries,
    hidden,
    kv_pages,
    page_table,
    cache_len,
    deal_table,
    out_weight,
    norm_gain,
    expert_ids,
    expert_gates,
    experts_in,
    experts_out,
):
    n_mp = lax.axis_size("mp")
    n_dp = lax.axis_size("dp")
    row_index = lax.axis_index("dp")
    column = lax.axis_index("mp")
    q_count = queries.shape[0]
    width = queries.shape[1]
    d_model = hidden.shape[1]
    heads = width // HD
    groups = n_mp // heads
    sub = q_count // groups
    my_head = column % heads
    my_group = column // heads
    page_share = page_table.shape[1] // n_mp
    pages_dev = kv_pages.shape[0]
    deal_row = deal_table[0]
    request = row_index
    page_count = page_table.shape[1]

    q_out = queries.reshape(sub, groups, heads, HD).transpose(1, 2, 0, 3).reshape(n_mp, sub, HD)
    kv_heads = kv_pages.reshape(pages_dev, PAGE, 2, heads, HD).transpose(3, 0, 1, 2, 4)
    kv_out = jnp.tile(kv_heads, (groups, 1, 1, 1, 1)).reshape(n_mp, pages_dev * PAGE * 2, HD)
    both = lax.all_to_all(
        jnp.concatenate([q_out, kv_out], axis=1), "mp", split_axis=0, concat_axis=0, tiled=True
    )
    q_in = both[:, :sub, :]
    arrived = both[:, sub:, :].reshape(n_mp, pages_dev, PAGE, 2, HD)
    first_pos = cache_len[request] + deal_row % n_mp * q_count
    query_pos = (
        first_pos[:, None] + jnp.arange(sub, dtype=jnp.int32)[None, :] * groups + my_group
    ).reshape(-1)
    slot_ids = jnp.arange(n_mp * page_share, dtype=jnp.int32)
    physical = (row_index * n_mp + slot_ids // page_share) * pages_dev + slot_ids % page_share
    table_row = page_table[request]
    matches = table_row[None, :] == physical[:, None]
    logical = jnp.sum(
        jnp.where(matches, jnp.arange(page_count, dtype=jnp.int32)[None, :], 0), axis=1
    )
    key_pos = (logical[:, None] * PAGE + jnp.arange(PAGE, dtype=jnp.int32)[None, :]).reshape(-1)
    key_rows = arrived[:, :, :, 0, :].reshape(-1, HD)
    value_rows = arrived[:, :, :, 1, :].reshape(-1, HD)
    blended = attend_head(q_in.reshape(-1, HD), key_rows, value_rows, key_pos, query_pos)
    back = lax.all_to_all(blended.reshape(n_mp, sub, HD), "mp", split_axis=0, concat_axis=0, tiled=True)
    attended = back.reshape(groups, heads, sub, HD).transpose(2, 0, 1, 3).reshape(q_count, width)

    if n_dp == 2:
        w_pair = swap_dp(out_weight)
        wo_rows = jnp.where(
            row_index == 0,
            jnp.concatenate([out_weight, w_pair], axis=0),
            jnp.concatenate([w_pair, out_weight], axis=0),
        )
    else:
        wo_rows = lax.all_gather(out_weight, "dp", axis=0, tiled=True)
    bits = n_mp.bit_length() - 1
    if n_mp == 1 << bits:
        block = wo_rows[None]
        for b in reversed(range(bits)):
            pair = lax.ppermute(block, "mp", [(m, m ^ (1 << b)) for m in range(n_mp)])
            low = (column >> b) % 2 == 0
            block = jnp.concatenate(
                [jnp.where(low, block, pair), jnp.where(low, pair, block)], axis=0
            )
        by_shard = jnp.einsum("tk,jkc->tjc", attended, block, preferred_element_type=jnp.float32)
        order = (0,) + tuple(range(bits, 0, -1)) + (bits + 1,)
        shard_w = wo_rows.shape[1]
        projected = (
            by_shard.reshape((q_count,) + (2,) * bits + (shard_w,))
            .transpose(order)
            .reshape(q_count, d_model)
        )
    else:
        projected = jnp.dot(
            attended,
            lax.all_gather(wo_rows, "mp", axis=1, tiled=True),
            preferred_element_type=jnp.float32,
        )
    resid_f = (hidden.astype(jnp.float32) + projected).astype(jnp.bfloat16).astype(jnp.float32)
    mean_square = jnp.mean(resid_f * resid_f, axis=1, keepdims=True)
    normed = (resid_f * lax.rsqrt(mean_square + epsilon) * norm_gain[None, :]).astype(jnp.bfloat16)
    capacity = min(q_count, q_count * TOPK * 4 // (3 * n_mp))
    flat_ids = expert_ids.reshape(-1)
    one_hot = (flat_ids[:, None] == jnp.arange(n_mp, dtype=jnp.int32)[None, :]).astype(jnp.int32)
    slot_of = jnp.sum(jnp.cumsum(one_hot, axis=0) * one_hot, axis=1) - 1
    target = (flat_ids * capacity + slot_of).reshape(q_count, TOPK)
    hits = target[:, :, None] == jnp.arange(n_mp * capacity, dtype=jnp.int32)[None, None, :]
    dispatch = jnp.any(hits, axis=1).astype(jnp.bfloat16)
    combine = jnp.sum(jnp.where(hits, expert_gates[:, :, None], 0.0), axis=1)
    ff_width = experts_out.shape[1]
    if n_dp == 2:
        in_other = swap_dp(experts_in)
        out_other = swap_dp(experts_out)
        normed, in_other = lax.optimization_barrier((normed, in_other))
    sending = lax.dot_general(
        dispatch, normed, (((0,), (0,)), ((), ())), preferred_element_type=jnp.float32
    ).astype(jnp.bfloat16)
    received = lax.all_to_all(
        sending.reshape(n_mp, capacity, d_model), "mp", split_axis=0, concat_axis=0, tiled=True
    )
    flat_rows = received.reshape(-1, d_model)
    if n_dp == 2:
        first = row_index == 0
        gate_up = jnp.where(
            first,
            jnp.concatenate([experts_in[0], in_other[0]], axis=0),
            jnp.concatenate([in_other[0], experts_in[0]], axis=0),
        )
        flat_rows, out_other, gate_up = lax.optimization_barrier((flat_rows, out_other, gate_up))
        down = jnp.where(
            first,
            jnp.concatenate([experts_out[0], out_other[0]], axis=1),
            jnp.concatenate([out_other[0], experts_out[0]], axis=1),
        )
    else:
        gate_up = lax.all_gather(experts_in, "dp", axis=1, tiled=True)[0]
        down = lax.all_gather(experts_out, "dp", axis=2, tiled=True)[0]
    gate_vals = jnp.dot(flat_rows, gate_up, preferred_element_type=jnp.float32)
    act = (jax.nn.silu(gate_vals[:, :ff_width]) * gate_vals[:, ff_width:]).astype(jnp.bfloat16)
    outcome = jnp.dot(act, down, preferred_element_type=jnp.float32).astype(jnp.bfloat16)
    results = lax.all_to_all(
        outcome.reshape(n_mp, capacity, d_model), "mp", split_axis=0, concat_axis=0, tiled=True
    )
    expert_sum = jnp.dot(
        combine,
        results.reshape(-1, d_model).astype(jnp.float32),
        precision=lax.Precision.HIGHEST,
        preferred_element_type=jnp.float32,
    )
    return (resid_f + expert_sum).astype(jnp.bfloat16)


def solution(mesh):
    in_specs = (
        P(("dp", "mp"), None),
        P(("dp", "mp"), None),
        P(("dp", "mp"), None, None, None),
        P(),
        P(),
        P("dp", None),
        P("dp", "mp"),
        P(),
        P(("dp", "mp"), None),
        P(("dp", "mp"), None),
        P("mp", "dp", None),
        P("mp", None, "dp"),
    )
    out_specs = P(("dp", "mp"), None)
    return jax.shard_map(
        on_device, mesh=mesh, in_specs=in_specs, out_specs=out_specs, check_vma=False
    )
```

```python
import math

import jax
import jax.numpy as jnp
from jax import lax
from jax.sharding import PartitionSpec as P

HEADS = 8
HD = 128
TOPK = 6
PAGE = 16


epsilon = 1e-06


def attend_head(q_rows, key_rows, value_rows, key_pos, query_pos):
    scores = jnp.dot(q_rows, key_rows.T, preferred_element_type=jnp.float32) * (1.0 / math.sqrt(HD))
    allowed = key_pos[None, :] <= query_pos[:, None]
    scores = jnp.where(allowed, scores, -1e30)
    row_max = jnp.max(scores, axis=1, keepdims=True)
    weights = jnp.exp(scores - row_max)
    weights_bf = (weights / jnp.sum(weights, axis=1, keepdims=True)).astype(jnp.bfloat16)
    blended = jnp.dot(weights_bf, value_rows, preferred_element_type=jnp.float32)
    return blended.astype(jnp.bfloat16)


def swap_dp(x):
    return lax.ppermute(x, "dp", [(0, 1), (1, 0)])


def on_device(
    queries,
    hidden,
    kv_pages,
    page_table,
    cache_len,
    deal_table,
    out_weight,
    norm_gain,
    expert_ids,
    expert_gates,
    experts_in,
    experts_out,
):
    n_mp = lax.axis_size("mp")
    n_dp = lax.axis_size("dp")
    row_index = lax.axis_index("dp")
    column = lax.axis_index("mp")
    q_count = queries.shape[0]
    width = queries.shape[1]
    d_model = hidden.shape[1]
    heads = width // HD
    groups = n_mp // heads
    sub = q_count // groups
    my_head = column % heads
    my_group = column // heads
    page_share = page_table.shape[1] // n_mp
    pages_dev = kv_pages.shape[0]
    deal_row = deal_table[0]
    request = row_index
    page_count = page_table.shape[1]

    q_out = queries.reshape(sub, groups, heads, HD).transpose(1, 2, 0, 3).reshape(n_mp, sub, HD)
    kv_heads = kv_pages.reshape(pages_dev, PAGE, 2, heads, HD).transpose(3, 0, 1, 2, 4)
    kv_out = jnp.tile(kv_heads, (groups, 1, 1, 1, 1)).reshape(n_mp, pages_dev * PAGE * 2, HD)
    both = lax.all_to_all(
        jnp.concatenate([q_out, kv_out], axis=1), "mp", split_axis=0, concat_axis=0, tiled=True
    )
    q_in = both[:, :sub, :]
    arrived = both[:, sub:, :].reshape(n_mp, pages_dev, PAGE, 2, HD)
    first_pos = cache_len[request] + deal_row % n_mp * q_count
    query_pos = (
        first_pos[:, None] + jnp.arange(sub, dtype=jnp.int32)[None, :] * groups + my_group
    ).reshape(-1)
    slot_ids = jnp.arange(n_mp * page_share, dtype=jnp.int32)
    physical = (row_index * n_mp + slot_ids // page_share) * pages_dev + slot_ids % page_share
    table_row = page_table[request]
    matches = table_row[None, :] == physical[:, None]
    logical = jnp.sum(
        jnp.where(matches, jnp.arange(page_count, dtype=jnp.int32)[None, :], 0), axis=1
    )
    key_pos = (logical[:, None] * PAGE + jnp.arange(PAGE, dtype=jnp.int32)[None, :]).reshape(-1)
    key_rows = arrived[:, :, :, 0, :].reshape(-1, HD)
    value_rows = arrived[:, :, :, 1, :].reshape(-1, HD)
    blended = attend_head(q_in.reshape(-1, HD), key_rows, value_rows, key_pos, query_pos)
    back = lax.all_to_all(blended.reshape(n_mp, sub, HD), "mp", split_axis=0, concat_axis=0, tiled=True)
    attended = back.reshape(groups, heads, sub, HD).transpose(2, 0, 1, 3).reshape(q_count, width)

    if n_dp == 2:
        w_pair = swap_dp(out_weight)
        wo_rows = jnp.where(
            row_index == 0,
            jnp.concatenate([out_weight, w_pair], axis=0),
            jnp.concatenate([w_pair, out_weight], axis=0),
        )
    else:
        wo_rows = lax.all_gather(out_weight, "dp", axis=0, tiled=True)
    bits = n_mp.bit_length() - 1
    if n_mp == 1 << bits:
        block = wo_rows[None]
        for b in reversed(range(1, bits)):
            pair = lax.ppermute(block, "mp", [(m, m ^ (1 << b)) for m in range(n_mp)])
            low = (column >> b) % 2 == 0
            block = jnp.concatenate(
                [jnp.where(low, block, pair), jnp.where(low, pair, block)], axis=0
            )
        pair = lax.ppermute(block, "mp", [(m, m ^ 1) for m in range(n_mp)])
        own_part = jnp.einsum("tk,jkc->tjc", attended, block, preferred_element_type=jnp.float32)
        pair_part = jnp.einsum("tk,jkc->tjc", attended, pair, preferred_element_type=jnp.float32)
        low = column % 2 == 0
        by_shard = jnp.where(
            low,
            jnp.concatenate([own_part, pair_part], axis=1),
            jnp.concatenate([pair_part, own_part], axis=1),
        )
        order = (0,) + tuple(range(bits, 0, -1)) + (bits + 1,)
        shard_w = wo_rows.shape[1]
        projected = (
            by_shard.reshape((q_count,) + (2,) * bits + (shard_w,))
            .transpose(order)
            .reshape(q_count, d_model)
        )
    else:
        projected = jnp.dot(
            attended,
            lax.all_gather(wo_rows, "mp", axis=1, tiled=True),
            preferred_element_type=jnp.float32,
        )
    resid_f = (hidden.astype(jnp.float32) + projected).astype(jnp.bfloat16).astype(jnp.float32)
    mean_square = jnp.mean(resid_f * resid_f, axis=1, keepdims=True)
    normed = (resid_f * lax.rsqrt(mean_square + epsilon) * norm_gain[None, :]).astype(jnp.bfloat16)
    capacity = min(q_count, q_count * TOPK * 4 // (3 * n_mp))
    flat_ids = expert_ids.reshape(-1)
    one_hot = (flat_ids[:, None] == jnp.arange(n_mp, dtype=jnp.int32)[None, :]).astype(jnp.int32)
    slot_of = jnp.sum(jnp.cumsum(one_hot, axis=0) * one_hot, axis=1) - 1
    target = (flat_ids * capacity + slot_of).reshape(q_count, TOPK)
    hits = target[:, :, None] == jnp.arange(n_mp * capacity, dtype=jnp.int32)[None, None, :]
    dispatch = jnp.any(hits, axis=1).astype(jnp.bfloat16)
    combine = jnp.sum(jnp.where(hits, expert_gates[:, :, None], 0.0), axis=1)
    ff_width = experts_out.shape[1]
    if n_dp == 2:
        in_other = swap_dp(experts_in)
        out_other = swap_dp(experts_out)
        normed, in_other = lax.optimization_barrier((normed, in_other))
    sending = lax.dot_general(
        dispatch, normed, (((0,), (0,)), ((), ())), preferred_element_type=jnp.float32
    ).astype(jnp.bfloat16)
    received = lax.all_to_all(
        sending.reshape(n_mp, capacity, d_model), "mp", split_axis=0, concat_axis=0, tiled=True
    )
    flat_rows = received.reshape(-1, d_model)
    if n_dp == 2:
        first = row_index == 0
        gate_up = jnp.where(
            first,
            jnp.concatenate([experts_in[0], in_other[0]], axis=0),
            jnp.concatenate([in_other[0], experts_in[0]], axis=0),
        )
        down = jnp.where(
            first,
            jnp.concatenate([experts_out[0], out_other[0]], axis=1),
            jnp.concatenate([out_other[0], experts_out[0]], axis=1),
        )
        flat_rows, down, gate_up = lax.optimization_barrier((flat_rows, down, gate_up))
    else:
        gate_up = lax.all_gather(experts_in, "dp", axis=1, tiled=True)[0]
        down = lax.all_gather(experts_out, "dp", axis=2, tiled=True)[0]
    gate_vals = jnp.dot(flat_rows, gate_up, preferred_element_type=jnp.float32)
    act = (jax.nn.silu(gate_vals[:, :ff_width]) * gate_vals[:, ff_width:]).astype(jnp.bfloat16)
    outcome = jnp.dot(act, down, preferred_element_type=jnp.float32).astype(jnp.bfloat16)
    results = lax.all_to_all(
        outcome.reshape(n_mp, capacity, d_model), "mp", split_axis=0, concat_axis=0, tiled=True
    )
    expert_sum = jnp.dot(
        combine,
        results.reshape(-1, d_model).astype(jnp.float32),
        precision=lax.Precision.HIGHEST,
        preferred_element_type=jnp.float32,
    )
    return (resid_f + expert_sum).astype(jnp.bfloat16)


def solution(mesh):
    in_specs = (
        P(("dp", "mp"), None),
        P(("dp", "mp"), None),
        P(("dp", "mp"), None, None, None),
        P(),
        P(),
        P("dp", None),
        P("dp", "mp"),
        P(),
        P(("dp", "mp"), None),
        P(("dp", "mp"), None),
        P("mp", "dp", None),
        P("mp", None, "dp"),
    )
    out_specs = P(("dp", "mp"), None)
    return jax.shard_map(
        on_device, mesh=mesh, in_specs=in_specs, out_specs=out_specs, check_vma=False
    )
```

```python
import math

import jax
import jax.numpy as jnp
from jax import lax
from jax.sharding import PartitionSpec as P

HEADS = 8
HD = 128
TOPK = 6
PAGE = 16


epsilon = 1e-06


def attend_head(q_rows, key_rows, value_rows, key_pos, query_pos):
    scores = jnp.dot(q_rows, key_rows.T, preferred_element_type=jnp.float32) * (1.0 / math.sqrt(HD))
    allowed = key_pos[None, :] <= query_pos[:, None]
    scores = jnp.where(allowed, scores, -1e30)
    row_max = jnp.max(scores, axis=1, keepdims=True)
    weights = jnp.exp(scores - row_max)
    weights_bf = (weights / jnp.sum(weights, axis=1, keepdims=True)).astype(jnp.bfloat16)
    blended = jnp.dot(weights_bf, value_rows, preferred_element_type=jnp.float32)
    return blended.astype(jnp.bfloat16)


def swap_dp(x):
    return lax.ppermute(x, "dp", [(0, 1), (1, 0)])


def on_device(
    queries,
    hidden,
    kv_pages,
    page_table,
    cache_len,
    deal_table,
    out_weight,
    norm_gain,
    expert_ids,
    expert_gates,
    experts_in,
    experts_out,
):
    n_mp = lax.axis_size("mp")
    n_dp = lax.axis_size("dp")
    row_index = lax.axis_index("dp")
    column = lax.axis_index("mp")
    q_count = queries.shape[0]
    width = queries.shape[1]
    d_model = hidden.shape[1]
    heads = width // HD
    groups = n_mp // heads
    sub = q_count // groups
    my_head = column % heads
    my_group = column // heads
    page_share = page_table.shape[1] // n_mp
    pages_dev = kv_pages.shape[0]
    deal_row = deal_table[0]
    request = row_index
    page_count = page_table.shape[1]

    q_out = queries.reshape(sub, groups, heads, HD).transpose(1, 2, 0, 3).reshape(n_mp, sub, HD)
    kv_heads = kv_pages.reshape(pages_dev, PAGE, 2, heads, HD).transpose(3, 0, 1, 2, 4)
    kv_out = jnp.tile(kv_heads, (groups, 1, 1, 1, 1)).reshape(n_mp, pages_dev * PAGE * 2, HD)
    both = lax.all_to_all(
        jnp.concatenate([q_out, kv_out], axis=1), "mp", split_axis=0, concat_axis=0, tiled=True
    )
    q_in = both[:, :sub, :]
    arrived = both[:, sub:, :].reshape(n_mp, pages_dev, PAGE, 2, HD)
    first_pos = cache_len[request] + deal_row % n_mp * q_count
    query_pos = (
        first_pos[:, None] + jnp.arange(sub, dtype=jnp.int32)[None, :] * groups + my_group
    ).reshape(-1)
    slot_ids = jnp.arange(n_mp * page_share, dtype=jnp.int32)
    physical = (row_index * n_mp + slot_ids // page_share) * pages_dev + slot_ids % page_share
    table_row = page_table[request]
    matches = table_row[None, :] == physical[:, None]
    logical = jnp.sum(
        jnp.where(matches, jnp.arange(page_count, dtype=jnp.int32)[None, :], 0), axis=1
    )
    key_pos = (logical[:, None] * PAGE + jnp.arange(PAGE, dtype=jnp.int32)[None, :]).reshape(-1)
    key_rows = arrived[:, :, :, 0, :].reshape(-1, HD)
    value_rows = arrived[:, :, :, 1, :].reshape(-1, HD)
    blended = attend_head(q_in.reshape(-1, HD), key_rows, value_rows, key_pos, query_pos)
    back = lax.all_to_all(blended.reshape(n_mp, sub, HD), "mp", split_axis=0, concat_axis=0, tiled=True)
    attended = back.reshape(groups, heads, sub, HD).transpose(2, 0, 1, 3).reshape(q_count, width)

    if n_dp == 2:
        w_pair = swap_dp(out_weight)
        wo_rows = jnp.where(
            row_index == 0,
            jnp.concatenate([out_weight, w_pair], axis=0),
            jnp.concatenate([w_pair, out_weight], axis=0),
        )
    else:
        wo_rows = lax.all_gather(out_weight, "dp", axis=0, tiled=True)
    bits = n_mp.bit_length() - 1
    if n_mp == 1 << bits:
        block = wo_rows[None]
        for b in reversed(range(1, bits)):
            pair = lax.ppermute(block, "mp", [(m, m ^ (1 << b)) for m in range(n_mp)])
            low = (column >> b) % 2 == 0
            block = jnp.concatenate(
                [jnp.where(low, block, pair), jnp.where(low, pair, block)], axis=0
            )
        pair = lax.ppermute(block, "mp", [(m, m ^ 1) for m in range(n_mp)])
        own_part = jnp.einsum("tk,jkc->tjc", attended, block, preferred_element_type=jnp.float32)
        pair_part = jnp.einsum("tk,jkc->tjc", attended, pair, preferred_element_type=jnp.float32)
        low = column % 2 == 0
        by_shard = jnp.where(
            low,
            jnp.concatenate([own_part, pair_part], axis=1),
            jnp.concatenate([pair_part, own_part], axis=1),
        )
        order = (0,) + tuple(range(bits, 0, -1)) + (bits + 1,)
        shard_w = wo_rows.shape[1]
        projected = (
            by_shard.reshape((q_count,) + (2,) * bits + (shard_w,))
            .transpose(order)
            .reshape(q_count, d_model)
        )
    else:
        projected = jnp.dot(
            attended,
            lax.all_gather(wo_rows, "mp", axis=1, tiled=True),
            preferred_element_type=jnp.float32,
        )
    resid_f = (hidden.astype(jnp.float32) + projected).astype(jnp.bfloat16).astype(jnp.float32)
    mean_square = jnp.mean(resid_f * resid_f, axis=1, keepdims=True)
    normed = (resid_f * lax.rsqrt(mean_square + epsilon) * norm_gain[None, :]).astype(jnp.bfloat16)
    capacity = min(q_count, q_count * TOPK * 4 // (3 * n_mp))
    flat_ids = expert_ids.reshape(-1)
    one_hot = (flat_ids[:, None] == jnp.arange(n_mp, dtype=jnp.int32)[None, :]).astype(jnp.int32)
    slot_of = jnp.sum(jnp.cumsum(one_hot, axis=0) * one_hot, axis=1) - 1
    target = (flat_ids * capacity + slot_of).reshape(q_count, TOPK)
    hits = target[:, :, None] == jnp.arange(n_mp * capacity, dtype=jnp.int32)[None, None, :]
    dispatch = jnp.any(hits, axis=1).astype(jnp.bfloat16)
    combine = jnp.sum(jnp.where(hits, expert_gates[:, :, None], 0.0), axis=1)
    ff_width = experts_out.shape[1]
    if n_dp == 2:
        in_other = swap_dp(experts_in)
        out_other = swap_dp(experts_out)
        normed, in_other = lax.optimization_barrier((normed, in_other))
    sending = lax.dot_general(
        dispatch, normed, (((0,), (0,)), ((), ())), preferred_element_type=jnp.float32
    ).astype(jnp.bfloat16)
    received = lax.all_to_all(
        sending.reshape(n_mp, capacity, d_model), "mp", split_axis=0, concat_axis=0, tiled=True
    )
    flat_rows = received.reshape(-1, d_model)
    if n_dp == 2:
        first = row_index == 0
        gate_up = jnp.where(
            first,
            jnp.concatenate([experts_in[0], in_other[0]], axis=0),
            jnp.concatenate([in_other[0], experts_in[0]], axis=0),
        )
        flat_rows, out_other, gate_up = lax.optimization_barrier((flat_rows, out_other, gate_up))
        down = jnp.where(
            first,
            jnp.concatenate([experts_out[0], out_other[0]], axis=1),
            jnp.concatenate([out_other[0], experts_out[0]], axis=1),
        )
    else:
        gate_up = lax.all_gather(experts_in, "dp", axis=1, tiled=True)[0]
        down = lax.all_gather(experts_out, "dp", axis=2, tiled=True)[0]
    gate_vals = jnp.dot(flat_rows, gate_up, preferred_element_type=jnp.float32)
    act = (jax.nn.silu(gate_vals[:, :ff_width]) * gate_vals[:, ff_width:]).astype(jnp.bfloat16)
    outcome = jnp.dot(act, down, preferred_element_type=jnp.float32).astype(jnp.bfloat16)
    results = lax.all_to_all(
        outcome.reshape(n_mp, capacity, d_model), "mp", split_axis=0, concat_axis=0, tiled=True
    )
    expert_sum = jnp.dot(
        combine,
        results.reshape(-1, d_model).astype(jnp.float32),
        precision=lax.Precision.HIGHEST,
        preferred_element_type=jnp.float32,
    )
    return (resid_f + expert_sum).astype(jnp.bfloat16)


def solution(mesh):
    in_specs = (
        P(("dp", "mp"), None),
        P(("dp", "mp"), None),
        P(("dp", "mp"), None, None, None),
        P(),
        P(),
        P("dp", None),
        P("dp", "mp"),
        P(),
        P(("dp", "mp"), None),
        P(("dp", "mp"), None),
        P("mp", "dp", None),
        P("mp", None, "dp"),
    )
    out_specs = P(("dp", "mp"), None)
    return jax.shard_map(
        on_device, mesh=mesh, in_specs=in_specs, out_specs=out_specs, check_vma=False
    )
```

```python
import math

import jax
import jax.numpy as jnp
from jax import lax
from jax.sharding import PartitionSpec as P

HEADS = 8
HD = 128
TOPK = 6
PAGE = 16


epsilon = 1e-06


def attend_head(q_rows, key_rows, value_rows, key_pos, query_pos):
    scores = jnp.dot(q_rows, key_rows.T, preferred_element_type=jnp.float32) * (1.0 / math.sqrt(HD))
    allowed = key_pos[None, :] <= query_pos[:, None]
    scores = jnp.where(allowed, scores, -1e30)
    row_max = jnp.max(scores, axis=1, keepdims=True)
    weights = jnp.exp(scores - row_max)
    weights_bf = (weights / jnp.sum(weights, axis=1, keepdims=True)).astype(jnp.bfloat16)
    blended = jnp.dot(weights_bf, value_rows, preferred_element_type=jnp.float32)
    return blended.astype(jnp.bfloat16)


def swap_dp(x):
    return lax.ppermute(x, "dp", [(0, 1), (1, 0)])


def on_device(
    queries,
    hidden,
    kv_pages,
    page_table,
    cache_len,
    deal_table,
    out_weight,
    norm_gain,
    expert_ids,
    expert_gates,
    experts_in,
    experts_out,
):
    n_mp = lax.axis_size("mp")
    n_dp = lax.axis_size("dp")
    row_index = lax.axis_index("dp")
    column = lax.axis_index("mp")
    q_count = queries.shape[0]
    width = queries.shape[1]
    d_model = hidden.shape[1]
    heads = width // HD
    groups = n_mp // heads
    sub = q_count // groups
    my_head = column % heads
    my_group = column // heads
    page_share = page_table.shape[1] // n_mp
    pages_dev = kv_pages.shape[0]
    deal_row = deal_table[0]
    request = row_index
    page_count = page_table.shape[1]

    q_out = queries.reshape(sub, groups, heads, HD).transpose(1, 2, 0, 3).reshape(n_mp, sub, HD)
    kv_heads = kv_pages.reshape(pages_dev, PAGE, 2, heads, HD).transpose(3, 0, 1, 2, 4)
    kv_out = jnp.tile(kv_heads, (groups, 1, 1, 1, 1)).reshape(n_mp, pages_dev * PAGE * 2, HD)
    both = lax.all_to_all(
        jnp.concatenate([q_out, kv_out], axis=1), "mp", split_axis=0, concat_axis=0, tiled=True
    )
    if n_dp == 2:
        w_pair = swap_dp(out_weight)
        wo_rows = jnp.where(
            row_index == 0,
            jnp.concatenate([out_weight, w_pair], axis=0),
            jnp.concatenate([w_pair, out_weight], axis=0),
        )
    else:
        wo_rows = lax.all_gather(out_weight, "dp", axis=0, tiled=True)
    bits = n_mp.bit_length() - 1
    if n_mp == 1 << bits:
        block = wo_rows[None]
        if bits > 1:
            b = bits - 1
            pair = lax.ppermute(block, "mp", [(m, m ^ (1 << b)) for m in range(n_mp)])
            low = (column >> b) % 2 == 0
            block = jnp.concatenate(
                [jnp.where(low, block, pair), jnp.where(low, pair, block)], axis=0
            )
        block, both = lax.optimization_barrier((block, both))
    q_in = both[:, :sub, :]
    arrived = both[:, sub:, :].reshape(n_mp, pages_dev, PAGE, 2, HD)
    first_pos = cache_len[request] + deal_row % n_mp * q_count
    query_pos = (
        first_pos[:, None] + jnp.arange(sub, dtype=jnp.int32)[None, :] * groups + my_group
    ).reshape(-1)
    slot_ids = jnp.arange(n_mp * page_share, dtype=jnp.int32)
    physical = (row_index * n_mp + slot_ids // page_share) * pages_dev + slot_ids % page_share
    table_row = page_table[request]
    matches = table_row[None, :] == physical[:, None]
    logical = jnp.sum(
        jnp.where(matches, jnp.arange(page_count, dtype=jnp.int32)[None, :], 0), axis=1
    )
    key_pos = (logical[:, None] * PAGE + jnp.arange(PAGE, dtype=jnp.int32)[None, :]).reshape(-1)
    key_rows = arrived[:, :, :, 0, :].reshape(-1, HD)
    value_rows = arrived[:, :, :, 1, :].reshape(-1, HD)
    blended = attend_head(q_in.reshape(-1, HD), key_rows, value_rows, key_pos, query_pos)

    if n_mp == 1 << bits:
        back = lax.all_to_all(
            blended.reshape(n_mp, sub, HD), "mp", split_axis=0, concat_axis=0, tiled=True
        )
        for b in reversed(range(1, bits - 1)):
            pair = lax.ppermute(block, "mp", [(m, m ^ (1 << b)) for m in range(n_mp)])
            low = (column >> b) % 2 == 0
            block = jnp.concatenate(
                [jnp.where(low, block, pair), jnp.where(low, pair, block)], axis=0
            )
        pair = lax.ppermute(block, "mp", [(m, m ^ 1) for m in range(n_mp)])
        attended = back.reshape(groups, heads, sub, HD).transpose(2, 0, 1, 3).reshape(q_count, width)
        own_part = jnp.einsum("tk,jkc->tjc", attended, block, preferred_element_type=jnp.float32)
        pair_part = jnp.einsum("tk,jkc->tjc", attended, pair, preferred_element_type=jnp.float32)
        low = column % 2 == 0
        by_shard = jnp.where(
            low,
            jnp.concatenate([own_part, pair_part], axis=1),
            jnp.concatenate([pair_part, own_part], axis=1),
        )
        order = (0,) + tuple(range(bits, 0, -1)) + (bits + 1,)
        shard_w = wo_rows.shape[1]
        projected = (
            by_shard.reshape((q_count,) + (2,) * bits + (shard_w,))
            .transpose(order)
            .reshape(q_count, d_model)
        )
    else:
        back = lax.all_to_all(
            blended.reshape(n_mp, sub, HD), "mp", split_axis=0, concat_axis=0, tiled=True
        )
        attended = back.reshape(groups, heads, sub, HD).transpose(2, 0, 1, 3).reshape(q_count, width)
        projected = jnp.dot(
            attended,
            lax.all_gather(wo_rows, "mp", axis=1, tiled=True),
            preferred_element_type=jnp.float32,
        )
    resid_f = (hidden.astype(jnp.float32) + projected).astype(jnp.bfloat16).astype(jnp.float32)
    mean_square = jnp.mean(resid_f * resid_f, axis=1, keepdims=True)
    normed = (resid_f * lax.rsqrt(mean_square + epsilon) * norm_gain[None, :]).astype(jnp.bfloat16)
    capacity = min(q_count, q_count * TOPK * 4 // (3 * n_mp))
    flat_ids = expert_ids.reshape(-1)
    one_hot = (flat_ids[:, None] == jnp.arange(n_mp, dtype=jnp.int32)[None, :]).astype(jnp.int32)
    slot_of = jnp.sum(jnp.cumsum(one_hot, axis=0) * one_hot, axis=1) - 1
    target = (flat_ids * capacity + slot_of).reshape(q_count, TOPK)
    hits = target[:, :, None] == jnp.arange(n_mp * capacity, dtype=jnp.int32)[None, None, :]
    dispatch = jnp.any(hits, axis=1).astype(jnp.bfloat16)
    combine = jnp.sum(jnp.where(hits, expert_gates[:, :, None], 0.0), axis=1)
    ff_width = experts_out.shape[1]
    if n_dp == 2:
        in_other = swap_dp(experts_in)
        out_other = swap_dp(experts_out)
        normed, in_other = lax.optimization_barrier((normed, in_other))
    sending = lax.dot_general(
        dispatch, normed, (((0,), (0,)), ((), ())), preferred_element_type=jnp.float32
    ).astype(jnp.bfloat16)
    received = lax.all_to_all(
        sending.reshape(n_mp, capacity, d_model), "mp", split_axis=0, concat_axis=0, tiled=True
    )
    flat_rows = received.reshape(-1, d_model)
    if n_dp == 2:
        first = row_index == 0
        gate_up = jnp.where(
            first,
            jnp.concatenate([experts_in[0], in_other[0]], axis=0),
            jnp.concatenate([in_other[0], experts_in[0]], axis=0),
        )
        flat_rows, out_other, gate_up = lax.optimization_barrier((flat_rows, out_other, gate_up))
        down = jnp.where(
            first,
            jnp.concatenate([experts_out[0], out_other[0]], axis=1),
            jnp.concatenate([out_other[0], experts_out[0]], axis=1),
        )
    else:
        gate_up = lax.all_gather(experts_in, "dp", axis=1, tiled=True)[0]
        down = lax.all_gather(experts_out, "dp", axis=2, tiled=True)[0]
    gate_vals = jnp.dot(flat_rows, gate_up, preferred_element_type=jnp.float32)
    act = (jax.nn.silu(gate_vals[:, :ff_width]) * gate_vals[:, ff_width:]).astype(jnp.bfloat16)
    outcome = jnp.dot(act, down, preferred_element_type=jnp.float32).astype(jnp.bfloat16)
    results = lax.all_to_all(
        outcome.reshape(n_mp, capacity, d_model), "mp", split_axis=0, concat_axis=0, tiled=True
    )
    expert_sum = jnp.dot(
        combine,
        results.reshape(-1, d_model).astype(jnp.float32),
        precision=lax.Precision.HIGHEST,
        preferred_element_type=jnp.float32,
    )
    return (resid_f + expert_sum).astype(jnp.bfloat16)


def solution(mesh):
    in_specs = (
        P(("dp", "mp"), None),
        P(("dp", "mp"), None),
        P(("dp", "mp"), None, None, None),
        P(),
        P(),
        P("dp", None),
        P("dp", "mp"),
        P(),
        P(("dp", "mp"), None),
        P(("dp", "mp"), None),
        P("mp", "dp", None),
        P("mp", None, "dp"),
    )
    out_specs = P(("dp", "mp"), None)
    return jax.shard_map(
        on_device, mesh=mesh, in_specs=in_specs, out_specs=out_specs, check_vma=False
    )
```

```python
import math

import jax
import jax.numpy as jnp
from jax import lax
from jax.sharding import PartitionSpec as P

HEADS = 8
HD = 128
TOPK = 6
PAGE = 16


epsilon = 1e-06


def attend_head(q_rows, key_rows, value_rows, key_pos, query_pos):
    scores = jnp.dot(q_rows, key_rows.T, preferred_element_type=jnp.float32) * (1.0 / math.sqrt(HD))
    allowed = key_pos[None, :] <= query_pos[:, None]
    scores = jnp.where(allowed, scores, -1e30)
    row_max = jnp.max(scores, axis=1, keepdims=True)
    weights = jnp.exp(scores - row_max)
    weights_bf = (weights / jnp.sum(weights, axis=1, keepdims=True)).astype(jnp.bfloat16)
    blended = jnp.dot(weights_bf, value_rows, preferred_element_type=jnp.float32)
    return blended.astype(jnp.bfloat16)


def swap_dp(x):
    return lax.ppermute(x, "dp", [(0, 1), (1, 0)])


def on_device(
    queries,
    hidden,
    kv_pages,
    page_table,
    cache_len,
    deal_table,
    out_weight,
    norm_gain,
    expert_ids,
    expert_gates,
    experts_in,
    experts_out,
):
    n_mp = lax.axis_size("mp")
    n_dp = lax.axis_size("dp")
    row_index = lax.axis_index("dp")
    column = lax.axis_index("mp")
    q_count = queries.shape[0]
    width = queries.shape[1]
    d_model = hidden.shape[1]
    heads = width // HD
    groups = n_mp // heads
    sub = q_count // groups
    my_head = column % heads
    my_group = column // heads
    page_share = page_table.shape[1] // n_mp
    pages_dev = kv_pages.shape[0]
    deal_row = deal_table[0]
    request = row_index
    page_count = page_table.shape[1]

    q_out = queries.reshape(sub, groups, heads, HD).transpose(1, 2, 0, 3).reshape(n_mp, sub, HD)
    kv_heads = kv_pages.reshape(pages_dev, PAGE, 2, heads, HD).transpose(3, 0, 1, 2, 4)
    kv_out = jnp.tile(kv_heads, (groups, 1, 1, 1, 1)).reshape(n_mp, pages_dev * PAGE * 2, HD)
    both = lax.all_to_all(
        jnp.concatenate([q_out, kv_out], axis=1), "mp", split_axis=0, concat_axis=0, tiled=True
    )
    q_in = both[:, :sub, :]
    arrived = both[:, sub:, :].reshape(n_mp, pages_dev, PAGE, 2, HD)
    first_pos = cache_len[request] + deal_row % n_mp * q_count
    query_pos = (
        first_pos[:, None] + jnp.arange(sub, dtype=jnp.int32)[None, :] * groups + my_group
    ).reshape(-1)
    slot_ids = jnp.arange(n_mp * page_share, dtype=jnp.int32)
    physical = (row_index * n_mp + slot_ids // page_share) * pages_dev + slot_ids % page_share
    table_row = page_table[request]
    matches = table_row[None, :] == physical[:, None]
    logical = jnp.sum(
        jnp.where(matches, jnp.arange(page_count, dtype=jnp.int32)[None, :], 0), axis=1
    )
    key_pos = (logical[:, None] * PAGE + jnp.arange(PAGE, dtype=jnp.int32)[None, :]).reshape(-1)
    key_rows = arrived[:, :, :, 0, :].reshape(-1, HD)
    value_rows = arrived[:, :, :, 1, :].reshape(-1, HD)
    blended = attend_head(q_in.reshape(-1, HD), key_rows, value_rows, key_pos, query_pos)
    back = lax.all_to_all(blended.reshape(n_mp, sub, HD), "mp", split_axis=0, concat_axis=0, tiled=True)
    attended = back.reshape(groups, heads, sub, HD).transpose(2, 0, 1, 3).reshape(q_count, width)

    bits = n_mp.bit_length() - 1
    if n_dp == 2 and n_mp == 1 << bits:
        w_other = lax.all_gather(swap_dp(out_weight), "mp", axis=1, tiled=True)
        block = out_weight[None]
        for b in reversed(range(1, bits)):
            pair = lax.ppermute(block, "mp", [(m, m ^ (1 << b)) for m in range(n_mp)])
            low = (column >> b) % 2 == 0
            block = jnp.concatenate(
                [jnp.where(low, block, pair), jnp.where(low, pair, block)], axis=0
            )
        pair = lax.ppermute(block, "mp", [(m, m ^ 1) for m in range(n_mp)])
        half_w = out_weight.shape[0]
        att_mine = lax.dynamic_slice_in_dim(attended, row_index * half_w, half_w, axis=1)
        att_other = lax.dynamic_slice_in_dim(attended, (1 - row_index) * half_w, half_w, axis=1)
        own_part = jnp.einsum("tk,jkc->tjc", att_mine, block, preferred_element_type=jnp.float32)
        pair_part = jnp.einsum("tk,jkc->tjc", att_mine, pair, preferred_element_type=jnp.float32)
        low = column % 2 == 0
        by_shard = jnp.where(
            low,
            jnp.concatenate([own_part, pair_part], axis=1),
            jnp.concatenate([pair_part, own_part], axis=1),
        )
        order = (0,) + tuple(range(bits, 0, -1)) + (bits + 1,)
        shard_w = out_weight.shape[1]
        projected = by_shard.reshape((q_count,) + (2,) * bits + (shard_w,)).transpose(order).reshape(
            q_count, d_model
        ) + jnp.dot(att_other, w_other, preferred_element_type=jnp.float32)
    else:
        wo_rows = lax.all_gather(out_weight, "dp", axis=0, tiled=True)
        projected = jnp.dot(
            attended,
            lax.all_gather(wo_rows, "mp", axis=1, tiled=True),
            preferred_element_type=jnp.float32,
        )
    resid_f = (hidden.astype(jnp.float32) + projected).astype(jnp.bfloat16).astype(jnp.float32)
    mean_square = jnp.mean(resid_f * resid_f, axis=1, keepdims=True)
    normed = (resid_f * lax.rsqrt(mean_square + epsilon) * norm_gain[None, :]).astype(jnp.bfloat16)
    capacity = min(q_count, q_count * TOPK * 4 // (3 * n_mp))
    flat_ids = expert_ids.reshape(-1)
    one_hot = (flat_ids[:, None] == jnp.arange(n_mp, dtype=jnp.int32)[None, :]).astype(jnp.int32)
    slot_of = jnp.sum(jnp.cumsum(one_hot, axis=0) * one_hot, axis=1) - 1
    target = (flat_ids * capacity + slot_of).reshape(q_count, TOPK)
    hits = target[:, :, None] == jnp.arange(n_mp * capacity, dtype=jnp.int32)[None, None, :]
    dispatch = jnp.any(hits, axis=1).astype(jnp.bfloat16)
    combine = jnp.sum(jnp.where(hits, expert_gates[:, :, None], 0.0), axis=1)
    ff_width = experts_out.shape[1]
    if n_dp == 2:
        in_other = swap_dp(experts_in)
        out_other = swap_dp(experts_out)
        normed, in_other = lax.optimization_barrier((normed, in_other))
    sending = lax.dot_general(
        dispatch, normed, (((0,), (0,)), ((), ())), preferred_element_type=jnp.float32
    ).astype(jnp.bfloat16)
    received = lax.all_to_all(
        sending.reshape(n_mp, capacity, d_model), "mp", split_axis=0, concat_axis=0, tiled=True
    )
    flat_rows = received.reshape(-1, d_model)
    if n_dp == 2:
        first = row_index == 0
        gate_up = jnp.where(
            first,
            jnp.concatenate([experts_in[0], in_other[0]], axis=0),
            jnp.concatenate([in_other[0], experts_in[0]], axis=0),
        )
        down = jnp.where(
            first,
            jnp.concatenate([experts_out[0], out_other[0]], axis=1),
            jnp.concatenate([out_other[0], experts_out[0]], axis=1),
        )
        flat_rows, down, gate_up = lax.optimization_barrier((flat_rows, down, gate_up))
    else:
        gate_up = lax.all_gather(experts_in, "dp", axis=1, tiled=True)[0]
        down = lax.all_gather(experts_out, "dp", axis=2, tiled=True)[0]
    gate_vals = jnp.dot(flat_rows, gate_up, preferred_element_type=jnp.float32)
    act = (jax.nn.silu(gate_vals[:, :ff_width]) * gate_vals[:, ff_width:]).astype(jnp.bfloat16)
    outcome = jnp.dot(act, down, preferred_element_type=jnp.float32).astype(jnp.bfloat16)
    results = lax.all_to_all(
        outcome.reshape(n_mp, capacity, d_model), "mp", split_axis=0, concat_axis=0, tiled=True
    )
    expert_sum = jnp.dot(
        combine,
        results.reshape(-1, d_model).astype(jnp.float32),
        precision=lax.Precision.HIGHEST,
        preferred_element_type=jnp.float32,
    )
    return (resid_f + expert_sum).astype(jnp.bfloat16)


def solution(mesh):
    in_specs = (
        P(("dp", "mp"), None),
        P(("dp", "mp"), None),
        P(("dp", "mp"), None, None, None),
        P(),
        P(),
        P("dp", None),
        P("dp", "mp"),
        P(),
        P(("dp", "mp"), None),
        P(("dp", "mp"), None),
        P("mp", "dp", None),
        P("mp", None, "dp"),
    )
    out_specs = P(("dp", "mp"), None)
    return jax.shard_map(
        on_device, mesh=mesh, in_specs=in_specs, out_specs=out_specs, check_vma=False
    )
```

```python
import math

import jax
import jax.numpy as jnp
from jax import lax
from jax.sharding import PartitionSpec as P

HEADS = 8
HD = 128
TOPK = 6
PAGE = 16


epsilon = 1e-06


def attend_head(q_rows, key_rows, value_rows, key_pos, query_pos):
    scores = jnp.dot(q_rows, key_rows.T, preferred_element_type=jnp.float32) * (1.0 / math.sqrt(HD))
    allowed = key_pos[None, :] <= query_pos[:, None]
    scores = jnp.where(allowed, scores, -1e30)
    row_max = jnp.max(scores, axis=1, keepdims=True)
    weights = jnp.exp(scores - row_max)
    weights_bf = (weights / jnp.sum(weights, axis=1, keepdims=True)).astype(jnp.bfloat16)
    blended = jnp.dot(weights_bf, value_rows, preferred_element_type=jnp.float32)
    return blended.astype(jnp.bfloat16)


def swap_dp(x):
    return lax.ppermute(x, "dp", [(0, 1), (1, 0)])


def on_device(
    queries,
    hidden,
    kv_pages,
    page_table,
    cache_len,
    deal_table,
    out_weight,
    norm_gain,
    expert_ids,
    expert_gates,
    experts_in,
    experts_out,
):
    n_mp = lax.axis_size("mp")
    n_dp = lax.axis_size("dp")
    row_index = lax.axis_index("dp")
    column = lax.axis_index("mp")
    q_count = queries.shape[0]
    width = queries.shape[1]
    d_model = hidden.shape[1]
    heads = width // HD
    groups = n_mp // heads
    sub = q_count // groups
    my_head = column % heads
    my_group = column // heads
    page_share = page_table.shape[1] // n_mp
    pages_dev = kv_pages.shape[0]
    deal_row = deal_table[0]
    request = row_index
    page_count = page_table.shape[1]

    q_out = queries.reshape(sub, groups, heads, HD).transpose(1, 2, 0, 3).reshape(n_mp, sub, HD)
    kv_heads = kv_pages.reshape(pages_dev, PAGE, 2, heads, HD).transpose(3, 0, 1, 2, 4)
    kv_out = jnp.tile(kv_heads, (groups, 1, 1, 1, 1)).reshape(n_mp, pages_dev * PAGE * 2, HD)
    both = lax.all_to_all(
        jnp.concatenate([q_out, kv_out], axis=1), "mp", split_axis=0, concat_axis=0, tiled=True
    )
    q_in = both[:, :sub, :]
    arrived = both[:, sub:, :].reshape(n_mp, pages_dev, PAGE, 2, HD)
    first_pos = cache_len[request] + deal_row % n_mp * q_count
    query_pos = (
        first_pos[:, None] + jnp.arange(sub, dtype=jnp.int32)[None, :] * groups + my_group
    ).reshape(-1)
    slot_ids = jnp.arange(n_mp * page_share, dtype=jnp.int32)
    physical = (row_index * n_mp + slot_ids // page_share) * pages_dev + slot_ids % page_share
    table_row = page_table[request]
    matches = table_row[None, :] == physical[:, None]
    logical = jnp.sum(
        jnp.where(matches, jnp.arange(page_count, dtype=jnp.int32)[None, :], 0), axis=1
    )
    key_pos = (logical[:, None] * PAGE + jnp.arange(PAGE, dtype=jnp.int32)[None, :]).reshape(-1)
    key_rows = arrived[:, :, :, 0, :].reshape(-1, HD)
    value_rows = arrived[:, :, :, 1, :].reshape(-1, HD)
    blended = attend_head(q_in.reshape(-1, HD), key_rows, value_rows, key_pos, query_pos)
    back = lax.all_to_all(blended.reshape(n_mp, sub, HD), "mp", split_axis=0, concat_axis=0, tiled=True)
    attended = back.reshape(groups, heads, sub, HD).transpose(2, 0, 1, 3).reshape(q_count, width)

    if n_dp == 2:
        w_pair = swap_dp(out_weight)
        wo_rows = jnp.where(
            row_index == 0,
            jnp.concatenate([out_weight, w_pair], axis=0),
            jnp.concatenate([w_pair, out_weight], axis=0),
        )
    else:
        wo_rows = lax.all_gather(out_weight, "dp", axis=0, tiled=True)
    bits = n_mp.bit_length() - 1
    if n_mp == 1 << bits:
        block = wo_rows[None]
        for b in reversed(range(1, bits)):
            pair = lax.ppermute(block, "mp", [(m, m ^ (1 << b)) for m in range(n_mp)])
            low = (column >> b) % 2 == 0
            block = jnp.concatenate(
                [jnp.where(low, block, pair), jnp.where(low, pair, block)], axis=0
            )
        pair = lax.ppermute(block, "mp", [(m, m ^ 1) for m in range(n_mp)])
        own_part = jnp.einsum("tk,jkc->tjc", attended, block, preferred_element_type=jnp.float32)
        pair_part = jnp.einsum("tk,jkc->tjc", attended, pair, preferred_element_type=jnp.float32)
        low = column % 2 == 0
        by_shard = jnp.where(
            low,
            jnp.concatenate([own_part, pair_part], axis=1),
            jnp.concatenate([pair_part, own_part], axis=1),
        )
        order = (0,) + tuple(range(bits, 0, -1)) + (bits + 1,)
        shard_w = wo_rows.shape[1]
        projected = (
            by_shard.reshape((q_count,) + (2,) * bits + (shard_w,))
            .transpose(order)
            .reshape(q_count, d_model)
        )
    else:
        projected = jnp.dot(
            attended,
            lax.all_gather(wo_rows, "mp", axis=1, tiled=True),
            preferred_element_type=jnp.float32,
        )
    resid_f = (hidden.astype(jnp.float32) + projected).astype(jnp.bfloat16).astype(jnp.float32)
    mean_square = jnp.mean(resid_f * resid_f, axis=1, keepdims=True)
    normed = (resid_f * lax.rsqrt(mean_square + epsilon) * norm_gain[None, :]).astype(jnp.bfloat16)
    capacity = min(q_count, q_count * TOPK * 4 // (3 * n_mp))
    flat_ids = expert_ids.reshape(-1)
    one_hot = (flat_ids[:, None] == jnp.arange(n_mp, dtype=jnp.int32)[None, :]).astype(jnp.int32)
    slot_of = jnp.sum(jnp.cumsum(one_hot, axis=0) * one_hot, axis=1) - 1
    target = (flat_ids * capacity + slot_of).reshape(q_count, TOPK)
    hits = target[:, :, None] == jnp.arange(n_mp * capacity, dtype=jnp.int32)[None, None, :]
    dispatch = jnp.any(hits, axis=1).astype(jnp.bfloat16)
    combine = jnp.sum(jnp.where(hits, expert_gates[:, :, None], 0.0), axis=1)
    ff_width = experts_out.shape[1]
    if n_dp == 2:
        out_other = swap_dp(experts_out)
        in_other = swap_dp(experts_in)
        normed, out_other = lax.optimization_barrier((normed, out_other))
    sending = lax.dot_general(
        dispatch, normed, (((0,), (0,)), ((), ())), preferred_element_type=jnp.float32
    ).astype(jnp.bfloat16)
    received = lax.all_to_all(
        sending.reshape(n_mp, capacity, d_model), "mp", split_axis=0, concat_axis=0, tiled=True
    )
    flat_rows = received.reshape(-1, d_model)
    if n_dp == 2:
        first = row_index == 0
        gate_up = jnp.where(
            first,
            jnp.concatenate([experts_in[0], in_other[0]], axis=0),
            jnp.concatenate([in_other[0], experts_in[0]], axis=0),
        )
        down = jnp.where(
            first,
            jnp.concatenate([experts_out[0], out_other[0]], axis=1),
            jnp.concatenate([out_other[0], experts_out[0]], axis=1),
        )
        flat_rows, down, gate_up = lax.optimization_barrier((flat_rows, down, gate_up))
    else:
        gate_up = lax.all_gather(experts_in, "dp", axis=1, tiled=True)[0]
        down = lax.all_gather(experts_out, "dp", axis=2, tiled=True)[0]
    gate_vals = jnp.dot(flat_rows, gate_up, preferred_element_type=jnp.float32)
    act = (jax.nn.silu(gate_vals[:, :ff_width]) * gate_vals[:, ff_width:]).astype(jnp.bfloat16)
    outcome = jnp.dot(act, down, preferred_element_type=jnp.float32).astype(jnp.bfloat16)
    results = lax.all_to_all(
        outcome.reshape(n_mp, capacity, d_model), "mp", split_axis=0, concat_axis=0, tiled=True
    )
    expert_sum = jnp.dot(
        combine,
        results.reshape(-1, d_model).astype(jnp.float32),
        precision=lax.Precision.HIGHEST,
        preferred_element_type=jnp.float32,
    )
    return (resid_f + expert_sum).astype(jnp.bfloat16)


def solution(mesh):
    in_specs = (
        P(("dp", "mp"), None),
        P(("dp", "mp"), None),
        P(("dp", "mp"), None, None, None),
        P(),
        P(),
        P("dp", None),
        P("dp", "mp"),
        P(),
        P(("dp", "mp"), None),
        P(("dp", "mp"), None),
        P("mp", "dp", None),
        P("mp", None, "dp"),
    )
    out_specs = P(("dp", "mp"), None)
    return jax.shard_map(
        on_device, mesh=mesh, in_specs=in_specs, out_specs=out_specs, check_vma=False
    )
```

```python
import math

import jax
import jax.numpy as jnp
from jax import lax
from jax.sharding import PartitionSpec as P

HEADS = 8
HD = 128
TOPK = 6
PAGE = 16


epsilon = 1e-06


def attend_head(q_rows, key_rows, value_rows, key_pos, query_pos):
    scores = jnp.dot(q_rows, key_rows.T, preferred_element_type=jnp.float32) * (1.0 / math.sqrt(HD))
    allowed = key_pos[None, :] <= query_pos[:, None]
    scores = jnp.where(allowed, scores, -1e30)
    row_max = jnp.max(scores, axis=1, keepdims=True)
    weights = jnp.exp(scores - row_max)
    weights_bf = (weights / jnp.sum(weights, axis=1, keepdims=True)).astype(jnp.bfloat16)
    blended = jnp.dot(weights_bf, value_rows, preferred_element_type=jnp.float32)
    return blended.astype(jnp.bfloat16)


def swap_dp(x):
    return lax.ppermute(x, "dp", [(0, 1), (1, 0)])


def on_device(
    queries,
    hidden,
    kv_pages,
    page_table,
    cache_len,
    deal_table,
    out_weight,
    norm_gain,
    expert_ids,
    expert_gates,
    experts_in,
    experts_out,
):
    n_mp = lax.axis_size("mp")
    n_dp = lax.axis_size("dp")
    row_index = lax.axis_index("dp")
    column = lax.axis_index("mp")
    q_count = queries.shape[0]
    width = queries.shape[1]
    d_model = hidden.shape[1]
    heads = width // HD
    groups = n_mp // heads
    sub = q_count // groups
    my_head = column % heads
    my_group = column // heads
    page_share = page_table.shape[1] // n_mp
    pages_dev = kv_pages.shape[0]
    deal_row = deal_table[0]
    request = row_index
    page_count = page_table.shape[1]

    q_out = queries.reshape(sub, groups, heads, HD).transpose(1, 2, 0, 3).reshape(n_mp, sub, HD)
    kv_heads = kv_pages.reshape(pages_dev, PAGE, 2, heads, HD).transpose(3, 0, 1, 2, 4)
    kv_out = jnp.tile(kv_heads, (groups, 1, 1, 1, 1)).reshape(n_mp, pages_dev * PAGE * 2, HD)
    both = lax.all_to_all(
        jnp.concatenate([q_out, kv_out], axis=1), "mp", split_axis=0, concat_axis=0, tiled=True
    )
    q_in = both[:, :sub, :]
    arrived = both[:, sub:, :].reshape(n_mp, pages_dev, PAGE, 2, HD)
    first_pos = cache_len[request] + deal_row % n_mp * q_count
    query_pos = (
        first_pos[:, None] + jnp.arange(sub, dtype=jnp.int32)[None, :] * groups + my_group
    ).reshape(-1)
    slot_ids = jnp.arange(n_mp * page_share, dtype=jnp.int32)
    physical = (row_index * n_mp + slot_ids // page_share) * pages_dev + slot_ids % page_share
    table_row = page_table[request]
    matches = table_row[None, :] == physical[:, None]
    logical = jnp.sum(
        jnp.where(matches, jnp.arange(page_count, dtype=jnp.int32)[None, :], 0), axis=1
    )
    key_pos = (logical[:, None] * PAGE + jnp.arange(PAGE, dtype=jnp.int32)[None, :]).reshape(-1)
    key_rows = arrived[:, :, :, 0, :].reshape(-1, HD)
    value_rows = arrived[:, :, :, 1, :].reshape(-1, HD)
    blended = attend_head(q_in.reshape(-1, HD), key_rows, value_rows, key_pos, query_pos)
    back = lax.all_to_all(blended.reshape(n_mp, sub, HD), "mp", split_axis=0, concat_axis=0, tiled=True)
    attended = back.reshape(groups, heads, sub, HD).transpose(2, 0, 1, 3).reshape(q_count, width)

    if n_dp == 2:
        w_pair = swap_dp(out_weight)
        wo_rows = jnp.where(
            row_index == 0,
            jnp.concatenate([out_weight, w_pair], axis=0),
            jnp.concatenate([w_pair, out_weight], axis=0),
        )
    else:
        wo_rows = lax.all_gather(out_weight, "dp", axis=0, tiled=True)
    bits = n_mp.bit_length() - 1
    if n_mp == 1 << bits:
        block = wo_rows[None]
        for b in reversed(range(1, bits)):
            pair = lax.ppermute(block, "mp", [(m, m ^ (1 << b)) for m in range(n_mp)])
            low = (column >> b) % 2 == 0
            block = jnp.concatenate(
                [jnp.where(low, block, pair), jnp.where(low, pair, block)], axis=0
            )
        pair = lax.ppermute(block, "mp", [(m, m ^ 1) for m in range(n_mp)])
        own_part = jnp.einsum("tk,jkc->tjc", attended, block, preferred_element_type=jnp.float32)
        pair_part = jnp.einsum("tk,jkc->tjc", attended, pair, preferred_element_type=jnp.float32)
        low = column % 2 == 0
        by_shard = jnp.where(
            low,
            jnp.concatenate([own_part, pair_part], axis=1),
            jnp.concatenate([pair_part, own_part], axis=1),
        )
        order = (0,) + tuple(range(bits, 0, -1)) + (bits + 1,)
        shard_w = wo_rows.shape[1]
        projected = (
            by_shard.reshape((q_count,) + (2,) * bits + (shard_w,))
            .transpose(order)
            .reshape(q_count, d_model)
        )
    else:
        projected = jnp.dot(
            attended,
            lax.all_gather(wo_rows, "mp", axis=1, tiled=True),
            preferred_element_type=jnp.float32,
        )
    resid_f = (hidden.astype(jnp.float32) + projected).astype(jnp.bfloat16).astype(jnp.float32)
    mean_square = jnp.mean(resid_f * resid_f, axis=1, keepdims=True)
    normed = (resid_f * lax.rsqrt(mean_square + epsilon) * norm_gain[None, :]).astype(jnp.bfloat16)
    capacity = min(q_count, q_count * TOPK * 4 // (3 * n_mp))
    flat_ids = expert_ids.reshape(-1)
    one_hot = (flat_ids[:, None] == jnp.arange(n_mp, dtype=jnp.int32)[None, :]).astype(jnp.int32)
    slot_of = jnp.sum(jnp.cumsum(one_hot, axis=0) * one_hot, axis=1) - 1
    target = (flat_ids * capacity + slot_of).reshape(q_count, TOPK)
    hits = target[:, :, None] == jnp.arange(n_mp * capacity, dtype=jnp.int32)[None, None, :]
    dispatch = jnp.any(hits, axis=1).astype(jnp.bfloat16)
    combine = jnp.sum(jnp.where(hits, expert_gates[:, :, None], 0.0), axis=1)
    ff_width = experts_out.shape[1]
    if n_dp == 2:
        out_other = swap_dp(experts_out)
        in_other = swap_dp(experts_in)
        normed, out_other = lax.optimization_barrier((normed, out_other))
    sending = lax.dot_general(
        dispatch, normed, (((0,), (0,)), ((), ())), preferred_element_type=jnp.float32
    ).astype(jnp.bfloat16)
    chunks = 2 if capacity % 2 == 0 else 1
    part = capacity // chunks
    by_slot = sending.reshape(n_mp, capacity, d_model)
    arrivals = [
        lax.all_to_all(
            by_slot[:, k * part : (k + 1) * part], "mp", split_axis=0, concat_axis=0, tiled=True
        )
        for k in range(chunks)
    ]
    if n_dp == 2:
        first = row_index == 0
        gate_up = jnp.where(
            first,
            jnp.concatenate([experts_in[0], in_other[0]], axis=0),
            jnp.concatenate([in_other[0], experts_in[0]], axis=0),
        )
        down = jnp.where(
            first,
            jnp.concatenate([experts_out[0], out_other[0]], axis=1),
            jnp.concatenate([out_other[0], experts_out[0]], axis=1),
        )
        arrivals[0], down, gate_up = lax.optimization_barrier((arrivals[0], down, gate_up))
    else:
        gate_up = lax.all_gather(experts_in, "dp", axis=1, tiled=True)[0]
        down = lax.all_gather(experts_out, "dp", axis=2, tiled=True)[0]
    returned = []
    for arrived_rows in arrivals:
        gate_vals = jnp.dot(
            arrived_rows.reshape(-1, d_model), gate_up, preferred_element_type=jnp.float32
        )
        act = (jax.nn.silu(gate_vals[:, :ff_width]) * gate_vals[:, ff_width:]).astype(jnp.bfloat16)
        outcome = jnp.dot(act, down, preferred_element_type=jnp.float32).astype(jnp.bfloat16)
        returned.append(
            lax.all_to_all(
                outcome.reshape(n_mp, part, d_model), "mp", split_axis=0, concat_axis=0, tiled=True
            )
        )
    results = jnp.concatenate(returned, axis=1)
    expert_sum = jnp.dot(
        combine,
        results.reshape(-1, d_model).astype(jnp.float32),
        precision=lax.Precision.HIGHEST,
        preferred_element_type=jnp.float32,
    )
    return (resid_f + expert_sum).astype(jnp.bfloat16)


def solution(mesh):
    in_specs = (
        P(("dp", "mp"), None),
        P(("dp", "mp"), None),
        P(("dp", "mp"), None, None, None),
        P(),
        P(),
        P("dp", None),
        P("dp", "mp"),
        P(),
        P(("dp", "mp"), None),
        P(("dp", "mp"), None),
        P("mp", "dp", None),
        P("mp", None, "dp"),
    )
    out_specs = P(("dp", "mp"), None)
    return jax.shard_map(
        on_device, mesh=mesh, in_specs=in_specs, out_specs=out_specs, check_vma=False
    )
```

```python
import math

import jax
import jax.numpy as jnp
from jax import lax
from jax.sharding import PartitionSpec as P

HEADS = 8
HD = 128
TOPK = 6
PAGE = 16


epsilon = 1e-06


def attend_head(q_rows, key_rows, value_rows, key_pos, query_pos):
    scores = jnp.dot(q_rows, key_rows.T, preferred_element_type=jnp.float32) * (1.0 / math.sqrt(HD))
    allowed = key_pos[None, :] <= query_pos[:, None]
    scores = jnp.where(allowed, scores, -1e30)
    row_max = jnp.max(scores, axis=1, keepdims=True)
    weights = jnp.exp(scores - row_max)
    weights_bf = (weights / jnp.sum(weights, axis=1, keepdims=True)).astype(jnp.bfloat16)
    blended = jnp.dot(weights_bf, value_rows, preferred_element_type=jnp.float32)
    return blended.astype(jnp.bfloat16)


def swap_dp(x):
    return lax.ppermute(x, "dp", [(0, 1), (1, 0)])


def on_device(
    queries,
    hidden,
    kv_pages,
    page_table,
    cache_len,
    deal_table,
    out_weight,
    norm_gain,
    expert_ids,
    expert_gates,
    experts_in,
    experts_out,
):
    n_mp = lax.axis_size("mp")
    n_dp = lax.axis_size("dp")
    row_index = lax.axis_index("dp")
    column = lax.axis_index("mp")
    q_count = queries.shape[0]
    width = queries.shape[1]
    d_model = hidden.shape[1]
    heads = width // HD
    groups = n_mp // heads
    sub = q_count // groups
    my_head = column % heads
    my_group = column // heads
    page_share = page_table.shape[1] // n_mp
    pages_dev = kv_pages.shape[0]
    deal_row = deal_table[0]
    request = row_index
    page_count = page_table.shape[1]

    q_out = queries.reshape(sub, groups, heads, HD).transpose(1, 2, 0, 3).reshape(n_mp, sub, HD)
    kv_heads = kv_pages.reshape(pages_dev, PAGE, 2, heads, HD).transpose(3, 0, 1, 2, 4)
    kv_out = jnp.tile(kv_heads, (groups, 1, 1, 1, 1)).reshape(n_mp, pages_dev * PAGE * 2, HD)
    if n_dp == 2:
        w_pair = swap_dp(out_weight)
        wo_rows = jnp.where(
            row_index == 0,
            jnp.concatenate([out_weight, w_pair], axis=0),
            jnp.concatenate([w_pair, out_weight], axis=0),
        )
    else:
        wo_rows = lax.all_gather(out_weight, "dp", axis=0, tiled=True)
    bits = n_mp.bit_length() - 1
    kv_send = jnp.concatenate([q_out, kv_out], axis=1)
    if n_mp == 1 << bits:
        block = wo_rows[None]
        if bits > 1:
            b = bits - 1
            pair = lax.ppermute(block, "mp", [(m, m ^ (1 << b)) for m in range(n_mp)])
            low = (column >> b) % 2 == 0
            block = jnp.concatenate(
                [jnp.where(low, block, pair), jnp.where(low, pair, block)], axis=0
            )
        block, kv_send = lax.optimization_barrier((block, kv_send))
    both = lax.all_to_all(kv_send, "mp", split_axis=0, concat_axis=0, tiled=True)
    q_in = both[:, :sub, :]
    arrived = both[:, sub:, :].reshape(n_mp, pages_dev, PAGE, 2, HD)
    first_pos = cache_len[request] + deal_row % n_mp * q_count
    query_pos = (
        first_pos[:, None] + jnp.arange(sub, dtype=jnp.int32)[None, :] * groups + my_group
    ).reshape(-1)
    slot_ids = jnp.arange(n_mp * page_share, dtype=jnp.int32)
    physical = (row_index * n_mp + slot_ids // page_share) * pages_dev + slot_ids % page_share
    table_row = page_table[request]
    matches = table_row[None, :] == physical[:, None]
    logical = jnp.sum(
        jnp.where(matches, jnp.arange(page_count, dtype=jnp.int32)[None, :], 0), axis=1
    )
    key_pos = (logical[:, None] * PAGE + jnp.arange(PAGE, dtype=jnp.int32)[None, :]).reshape(-1)
    key_rows = arrived[:, :, :, 0, :].reshape(-1, HD)
    value_rows = arrived[:, :, :, 1, :].reshape(-1, HD)
    blended = attend_head(q_in.reshape(-1, HD), key_rows, value_rows, key_pos, query_pos)
    back = lax.all_to_all(blended.reshape(n_mp, sub, HD), "mp", split_axis=0, concat_axis=0, tiled=True)
    attended = back.reshape(groups, heads, sub, HD).transpose(2, 0, 1, 3).reshape(q_count, width)

    bits = n_mp.bit_length() - 1
    if n_mp == 1 << bits:
        for b in reversed(range(1, bits - 1)):
            pair = lax.ppermute(block, "mp", [(m, m ^ (1 << b)) for m in range(n_mp)])
            low = (column >> b) % 2 == 0
            block = jnp.concatenate(
                [jnp.where(low, block, pair), jnp.where(low, pair, block)], axis=0
            )
        pair = lax.ppermute(block, "mp", [(m, m ^ 1) for m in range(n_mp)])
        own_part = jnp.einsum("tk,jkc->tjc", attended, block, preferred_element_type=jnp.float32)
        pair_part = jnp.einsum("tk,jkc->tjc", attended, pair, preferred_element_type=jnp.float32)
        low = column % 2 == 0
        by_shard = jnp.where(
            low,
            jnp.concatenate([own_part, pair_part], axis=1),
            jnp.concatenate([pair_part, own_part], axis=1),
        )
        order = (0,) + tuple(range(bits, 0, -1)) + (bits + 1,)
        shard_w = wo_rows.shape[1]
        projected = (
            by_shard.reshape((q_count,) + (2,) * bits + (shard_w,))
            .transpose(order)
            .reshape(q_count, d_model)
        )
    else:
        projected = jnp.dot(
            attended,
            lax.all_gather(wo_rows, "mp", axis=1, tiled=True),
            preferred_element_type=jnp.float32,
        )
    resid_f = (hidden.astype(jnp.float32) + projected).astype(jnp.bfloat16).astype(jnp.float32)
    mean_square = jnp.mean(resid_f * resid_f, axis=1, keepdims=True)
    normed = (resid_f * lax.rsqrt(mean_square + epsilon) * norm_gain[None, :]).astype(jnp.bfloat16)
    capacity = min(q_count, q_count * TOPK * 4 // (3 * n_mp))
    flat_ids = expert_ids.reshape(-1)
    one_hot = (flat_ids[:, None] == jnp.arange(n_mp, dtype=jnp.int32)[None, :]).astype(jnp.int32)
    slot_of = jnp.sum(jnp.cumsum(one_hot, axis=0) * one_hot, axis=1) - 1
    target = (flat_ids * capacity + slot_of).reshape(q_count, TOPK)
    hits = target[:, :, None] == jnp.arange(n_mp * capacity, dtype=jnp.int32)[None, None, :]
    dispatch = jnp.any(hits, axis=1).astype(jnp.bfloat16)
    combine = jnp.sum(jnp.where(hits, expert_gates[:, :, None], 0.0), axis=1)
    ff_width = experts_out.shape[1]
    if n_dp == 2:
        out_other = swap_dp(experts_out)
        in_other = swap_dp(experts_in)
        normed, out_other = lax.optimization_barrier((normed, out_other))
    sending = lax.dot_general(
        dispatch, normed, (((0,), (0,)), ((), ())), preferred_element_type=jnp.float32
    ).astype(jnp.bfloat16)
    received = lax.all_to_all(
        sending.reshape(n_mp, capacity, d_model), "mp", split_axis=0, concat_axis=0, tiled=True
    )
    flat_rows = received.reshape(-1, d_model)
    if n_dp == 2:
        first = row_index == 0
        gate_up = jnp.where(
            first,
            jnp.concatenate([experts_in[0], in_other[0]], axis=0),
            jnp.concatenate([in_other[0], experts_in[0]], axis=0),
        )
        down = jnp.where(
            first,
            jnp.concatenate([experts_out[0], out_other[0]], axis=1),
            jnp.concatenate([out_other[0], experts_out[0]], axis=1),
        )
        flat_rows, down, gate_up = lax.optimization_barrier((flat_rows, down, gate_up))
    else:
        gate_up = lax.all_gather(experts_in, "dp", axis=1, tiled=True)[0]
        down = lax.all_gather(experts_out, "dp", axis=2, tiled=True)[0]
    gate_vals = jnp.dot(flat_rows, gate_up, preferred_element_type=jnp.float32)
    act = (jax.nn.silu(gate_vals[:, :ff_width]) * gate_vals[:, ff_width:]).astype(jnp.bfloat16)
    outcome = jnp.dot(act, down, preferred_element_type=jnp.float32).astype(jnp.bfloat16)
    results = lax.all_to_all(
        outcome.reshape(n_mp, capacity, d_model), "mp", split_axis=0, concat_axis=0, tiled=True
    )
    expert_sum = jnp.dot(
        combine,
        results.reshape(-1, d_model).astype(jnp.float32),
        precision=lax.Precision.HIGHEST,
        preferred_element_type=jnp.float32,
    )
    return (resid_f + expert_sum).astype(jnp.bfloat16)


def solution(mesh):
    in_specs = (
        P(("dp", "mp"), None),
        P(("dp", "mp"), None),
        P(("dp", "mp"), None, None, None),
        P(),
        P(),
        P("dp", None),
        P("dp", "mp"),
        P(),
        P(("dp", "mp"), None),
        P(("dp", "mp"), None),
        P("mp", "dp", None),
        P("mp", None, "dp"),
    )
    out_specs = P(("dp", "mp"), None)
    return jax.shard_map(
        on_device, mesh=mesh, in_specs=in_specs, out_specs=out_specs, check_vma=False
    )
```

```python
import math

import jax
import jax.numpy as jnp
from jax import lax
from jax.sharding import PartitionSpec as P

HEADS = 8
HD = 128
TOPK = 6
PAGE = 16


epsilon = 1e-06


def attend_head(q_rows, key_rows, value_rows, key_pos, query_pos):
    scores = jnp.dot(q_rows, key_rows.T, preferred_element_type=jnp.float32) * (1.0 / math.sqrt(HD))
    allowed = key_pos[None, :] <= query_pos[:, None]
    scores = jnp.where(allowed, scores, -1e30)
    row_max = jnp.max(scores, axis=1, keepdims=True)
    weights = jnp.exp(scores - row_max)
    weights_bf = (weights / jnp.sum(weights, axis=1, keepdims=True)).astype(jnp.bfloat16)
    blended = jnp.dot(weights_bf, value_rows, preferred_element_type=jnp.float32)
    return blended.astype(jnp.bfloat16)


def swap_dp(x):
    return lax.ppermute(x, "dp", [(0, 1), (1, 0)])


def on_device(
    queries,
    hidden,
    kv_pages,
    page_table,
    cache_len,
    deal_table,
    out_weight,
    norm_gain,
    expert_ids,
    expert_gates,
    experts_in,
    experts_out,
):
    n_mp = lax.axis_size("mp")
    n_dp = lax.axis_size("dp")
    row_index = lax.axis_index("dp")
    column = lax.axis_index("mp")
    q_count = queries.shape[0]
    width = queries.shape[1]
    d_model = hidden.shape[1]
    heads = width // HD
    groups = n_mp // heads
    sub = q_count // groups
    my_head = column % heads
    my_group = column // heads
    page_share = page_table.shape[1] // n_mp
    pages_dev = kv_pages.shape[0]
    deal_row = deal_table[0]
    request = row_index
    page_count = page_table.shape[1]

    q_out = queries.reshape(sub, groups, heads, HD).transpose(1, 2, 0, 3).reshape(n_mp, sub, HD)
    kv_heads = kv_pages.reshape(pages_dev, PAGE, 2, heads, HD).transpose(3, 0, 1, 2, 4)
    kv_out = jnp.tile(kv_heads, (groups, 1, 1, 1, 1)).reshape(n_mp, pages_dev * PAGE * 2, HD)
    if n_dp == 2:
        w_pair = swap_dp(out_weight)
        wo_rows = jnp.where(
            row_index == 0,
            jnp.concatenate([out_weight, w_pair], axis=0),
            jnp.concatenate([w_pair, out_weight], axis=0),
        )
    else:
        wo_rows = lax.all_gather(out_weight, "dp", axis=0, tiled=True)
    bits = n_mp.bit_length() - 1
    kv_send = jnp.concatenate([q_out, kv_out], axis=1)
    if n_mp == 1 << bits:
        block = wo_rows[None]
        for b in reversed(range(max(1, bits - 2), bits)):
            pair = lax.ppermute(block, "mp", [(m, m ^ (1 << b)) for m in range(n_mp)])
            low = (column >> b) % 2 == 0
            block = jnp.concatenate(
                [jnp.where(low, block, pair), jnp.where(low, pair, block)], axis=0
            )
        block, kv_send = lax.optimization_barrier((block, kv_send))
    both = lax.all_to_all(kv_send, "mp", split_axis=0, concat_axis=0, tiled=True)
    q_in = both[:, :sub, :]
    arrived = both[:, sub:, :].reshape(n_mp, pages_dev, PAGE, 2, HD)
    first_pos = cache_len[request] + deal_row % n_mp * q_count
    query_pos = (
        first_pos[:, None] + jnp.arange(sub, dtype=jnp.int32)[None, :] * groups + my_group
    ).reshape(-1)
    slot_ids = jnp.arange(n_mp * page_share, dtype=jnp.int32)
    physical = (row_index * n_mp + slot_ids // page_share) * pages_dev + slot_ids % page_share
    table_row = page_table[request]
    matches = table_row[None, :] == physical[:, None]
    logical = jnp.sum(
        jnp.where(matches, jnp.arange(page_count, dtype=jnp.int32)[None, :], 0), axis=1
    )
    key_pos = (logical[:, None] * PAGE + jnp.arange(PAGE, dtype=jnp.int32)[None, :]).reshape(-1)
    key_rows = arrived[:, :, :, 0, :].reshape(-1, HD)
    value_rows = arrived[:, :, :, 1, :].reshape(-1, HD)
    blended = attend_head(q_in.reshape(-1, HD), key_rows, value_rows, key_pos, query_pos)
    back = lax.all_to_all(blended.reshape(n_mp, sub, HD), "mp", split_axis=0, concat_axis=0, tiled=True)
    attended = back.reshape(groups, heads, sub, HD).transpose(2, 0, 1, 3).reshape(q_count, width)

    bits = n_mp.bit_length() - 1
    if n_mp == 1 << bits:
        for b in reversed(range(1, max(1, bits - 2))):
            pair = lax.ppermute(block, "mp", [(m, m ^ (1 << b)) for m in range(n_mp)])
            low = (column >> b) % 2 == 0
            block = jnp.concatenate(
                [jnp.where(low, block, pair), jnp.where(low, pair, block)], axis=0
            )
        pair = lax.ppermute(block, "mp", [(m, m ^ 1) for m in range(n_mp)])
        own_part = jnp.einsum("tk,jkc->tjc", attended, block, preferred_element_type=jnp.float32)
        pair_part = jnp.einsum("tk,jkc->tjc", attended, pair, preferred_element_type=jnp.float32)
        low = column % 2 == 0
        by_shard = jnp.where(
            low,
            jnp.concatenate([own_part, pair_part], axis=1),
            jnp.concatenate([pair_part, own_part], axis=1),
        )
        order = (0,) + tuple(range(bits, 0, -1)) + (bits + 1,)
        shard_w = wo_rows.shape[1]
        projected = (
            by_shard.reshape((q_count,) + (2,) * bits + (shard_w,))
            .transpose(order)
            .reshape(q_count, d_model)
        )
    else:
        projected = jnp.dot(
            attended,
            lax.all_gather(wo_rows, "mp", axis=1, tiled=True),
            preferred_element_type=jnp.float32,
        )
    resid_f = (hidden.astype(jnp.float32) + projected).astype(jnp.bfloat16).astype(jnp.float32)
    mean_square = jnp.mean(resid_f * resid_f, axis=1, keepdims=True)
    normed = (resid_f * lax.rsqrt(mean_square + epsilon) * norm_gain[None, :]).astype(jnp.bfloat16)
    capacity = min(q_count, q_count * TOPK * 4 // (3 * n_mp))
    flat_ids = expert_ids.reshape(-1)
    one_hot = (flat_ids[:, None] == jnp.arange(n_mp, dtype=jnp.int32)[None, :]).astype(jnp.int32)
    slot_of = jnp.sum(jnp.cumsum(one_hot, axis=0) * one_hot, axis=1) - 1
    target = (flat_ids * capacity + slot_of).reshape(q_count, TOPK)
    hits = target[:, :, None] == jnp.arange(n_mp * capacity, dtype=jnp.int32)[None, None, :]
    dispatch = jnp.any(hits, axis=1).astype(jnp.bfloat16)
    combine = jnp.sum(jnp.where(hits, expert_gates[:, :, None], 0.0), axis=1)
    ff_width = experts_out.shape[1]
    if n_dp == 2:
        out_other = swap_dp(experts_out)
        in_other = swap_dp(experts_in)
        normed, out_other = lax.optimization_barrier((normed, out_other))
    sending = lax.dot_general(
        dispatch, normed, (((0,), (0,)), ((), ())), preferred_element_type=jnp.float32
    ).astype(jnp.bfloat16)
    received = lax.all_to_all(
        sending.reshape(n_mp, capacity, d_model), "mp", split_axis=0, concat_axis=0, tiled=True
    )
    flat_rows = received.reshape(-1, d_model)
    if n_dp == 2:
        first = row_index == 0
        gate_up = jnp.where(
            first,
            jnp.concatenate([experts_in[0], in_other[0]], axis=0),
            jnp.concatenate([in_other[0], experts_in[0]], axis=0),
        )
        down = jnp.where(
            first,
            jnp.concatenate([experts_out[0], out_other[0]], axis=1),
            jnp.concatenate([out_other[0], experts_out[0]], axis=1),
        )
        flat_rows, down, gate_up = lax.optimization_barrier((flat_rows, down, gate_up))
    else:
        gate_up = lax.all_gather(experts_in, "dp", axis=1, tiled=True)[0]
        down = lax.all_gather(experts_out, "dp", axis=2, tiled=True)[0]
    gate_vals = jnp.dot(flat_rows, gate_up, preferred_element_type=jnp.float32)
    act = (jax.nn.silu(gate_vals[:, :ff_width]) * gate_vals[:, ff_width:]).astype(jnp.bfloat16)
    outcome = jnp.dot(act, down, preferred_element_type=jnp.float32).astype(jnp.bfloat16)
    results = lax.all_to_all(
        outcome.reshape(n_mp, capacity, d_model), "mp", split_axis=0, concat_axis=0, tiled=True
    )
    expert_sum = jnp.dot(
        combine,
        results.reshape(-1, d_model).astype(jnp.float32),
        precision=lax.Precision.HIGHEST,
        preferred_element_type=jnp.float32,
    )
    return (resid_f + expert_sum).astype(jnp.bfloat16)


def solution(mesh):
    in_specs = (
        P(("dp", "mp"), None),
        P(("dp", "mp"), None),
        P(("dp", "mp"), None, None, None),
        P(),
        P(),
        P("dp", None),
        P("dp", "mp"),
        P(),
        P(("dp", "mp"), None),
        P(("dp", "mp"), None),
        P("mp", "dp", None),
        P("mp", None, "dp"),
    )
    out_specs = P(("dp", "mp"), None)
    return jax.shard_map(
        on_device, mesh=mesh, in_specs=in_specs, out_specs=out_specs, check_vma=False
    )
```

```python
import math

import jax
import jax.numpy as jnp
from jax import lax
from jax.sharding import PartitionSpec as P

HEADS = 8
HD = 128
TOPK = 6
PAGE = 16


epsilon = 1e-06


def attend_head(q_rows, key_rows, value_rows, key_pos, query_pos):
    scores = jnp.dot(q_rows, key_rows.T, preferred_element_type=jnp.float32) * (1.0 / math.sqrt(HD))
    allowed = key_pos[None, :] <= query_pos[:, None]
    scores = jnp.where(allowed, scores, -1e30)
    row_max = jnp.max(scores, axis=1, keepdims=True)
    weights = jnp.exp(scores - row_max)
    weights_bf = (weights / jnp.sum(weights, axis=1, keepdims=True)).astype(jnp.bfloat16)
    blended = jnp.dot(weights_bf, value_rows, preferred_element_type=jnp.float32)
    return blended.astype(jnp.bfloat16)


def swap_dp(x):
    return lax.ppermute(x, "dp", [(0, 1), (1, 0)])


def on_device(
    queries,
    hidden,
    kv_pages,
    page_table,
    cache_len,
    deal_table,
    out_weight,
    norm_gain,
    expert_ids,
    expert_gates,
    experts_in,
    experts_out,
):
    n_mp = lax.axis_size("mp")
    n_dp = lax.axis_size("dp")
    row_index = lax.axis_index("dp")
    column = lax.axis_index("mp")
    q_count = queries.shape[0]
    width = queries.shape[1]
    d_model = hidden.shape[1]
    heads = width // HD
    groups = n_mp // heads
    sub = q_count // groups
    my_head = column % heads
    my_group = column // heads
    page_share = page_table.shape[1] // n_mp
    pages_dev = kv_pages.shape[0]
    deal_row = deal_table[0]
    request = row_index
    page_count = page_table.shape[1]

    q_out = queries.reshape(sub, groups, heads, HD).transpose(1, 2, 0, 3).reshape(n_mp, sub, HD)
    kv_heads = kv_pages.reshape(pages_dev, PAGE, 2, heads, HD).transpose(3, 0, 1, 2, 4)
    kv_out = jnp.tile(kv_heads, (groups, 1, 1, 1, 1)).reshape(n_mp, pages_dev * PAGE * 2, HD)
    if n_dp == 2:
        w_pair = swap_dp(out_weight)
        wo_rows = jnp.where(
            row_index == 0,
            jnp.concatenate([out_weight, w_pair], axis=0),
            jnp.concatenate([w_pair, out_weight], axis=0),
        )
    else:
        wo_rows = lax.all_gather(out_weight, "dp", axis=0, tiled=True)
    bits = n_mp.bit_length() - 1
    kv_send = jnp.concatenate([q_out, kv_out], axis=1)
    if n_mp == 1 << bits:
        block = wo_rows[None]
        if bits > 1:
            b = bits - 1
            pair = lax.ppermute(block, "mp", [(m, m ^ (1 << b)) for m in range(n_mp)])
            low = (column >> b) % 2 == 0
            block = jnp.concatenate(
                [jnp.where(low, block, pair), jnp.where(low, pair, block)], axis=0
            )
        block, kv_send = lax.optimization_barrier((block, kv_send))
    both = lax.all_to_all(kv_send, "mp", split_axis=0, concat_axis=0, tiled=True)
    q_in = both[:, :sub, :]
    arrived = both[:, sub:, :].reshape(n_mp, pages_dev, PAGE, 2, HD)
    first_pos = cache_len[request] + deal_row % n_mp * q_count
    query_pos = (
        first_pos[:, None] + jnp.arange(sub, dtype=jnp.int32)[None, :] * groups + my_group
    ).reshape(-1)
    slot_ids = jnp.arange(n_mp * page_share, dtype=jnp.int32)
    physical = (row_index * n_mp + slot_ids // page_share) * pages_dev + slot_ids % page_share
    table_row = page_table[request]
    matches = table_row[None, :] == physical[:, None]
    logical = jnp.sum(
        jnp.where(matches, jnp.arange(page_count, dtype=jnp.int32)[None, :], 0), axis=1
    )
    key_pos = (logical[:, None] * PAGE + jnp.arange(PAGE, dtype=jnp.int32)[None, :]).reshape(-1)
    key_rows = arrived[:, :, :, 0, :].reshape(-1, HD)
    value_rows = arrived[:, :, :, 1, :].reshape(-1, HD)
    blended = attend_head(q_in.reshape(-1, HD), key_rows, value_rows, key_pos, query_pos)
    back = lax.all_to_all(blended.reshape(n_mp, sub, HD), "mp", split_axis=0, concat_axis=0, tiled=True)
    attended = back.reshape(groups, heads, sub, HD).transpose(2, 0, 1, 3).reshape(q_count, width)

    bits = n_mp.bit_length() - 1
    if n_mp == 1 << bits:
        for b in reversed(range(1, bits - 1)):
            pair = lax.ppermute(block, "mp", [(m, m ^ (1 << b)) for m in range(n_mp)])
            low = (column >> b) % 2 == 0
            block = jnp.concatenate(
                [jnp.where(low, block, pair), jnp.where(low, pair, block)], axis=0
            )
        pair = lax.ppermute(block, "mp", [(m, m ^ 1) for m in range(n_mp)])
        own_part = jnp.einsum("tk,jkc->tjc", attended, block, preferred_element_type=jnp.float32)
        pair_part = jnp.einsum("tk,jkc->tjc", attended, pair, preferred_element_type=jnp.float32)
        low = column % 2 == 0
        by_shard = jnp.where(
            low,
            jnp.concatenate([own_part, pair_part], axis=1),
            jnp.concatenate([pair_part, own_part], axis=1),
        )
        order = (0,) + tuple(range(bits, 0, -1)) + (bits + 1,)
        shard_w = wo_rows.shape[1]
        projected = (
            by_shard.reshape((q_count,) + (2,) * bits + (shard_w,))
            .transpose(order)
            .reshape(q_count, d_model)
        )
    else:
        projected = jnp.dot(
            attended,
            lax.all_gather(wo_rows, "mp", axis=1, tiled=True),
            preferred_element_type=jnp.float32,
        )
    resid_f = (hidden.astype(jnp.float32) + projected).astype(jnp.bfloat16).astype(jnp.float32)
    mean_square = jnp.mean(resid_f * resid_f, axis=1, keepdims=True)
    normed = (resid_f * lax.rsqrt(mean_square + epsilon) * norm_gain[None, :]).astype(jnp.bfloat16)
    capacity = min(q_count, q_count * TOPK * 4 // (3 * n_mp))
    flat_ids = expert_ids.reshape(-1)
    one_hot = (flat_ids[:, None] == jnp.arange(n_mp, dtype=jnp.int32)[None, :]).astype(jnp.int32)
    slot_of = jnp.sum(jnp.cumsum(one_hot, axis=0) * one_hot, axis=1) - 1
    target = (flat_ids * capacity + slot_of).reshape(q_count, TOPK)
    hits = target[:, :, None] == jnp.arange(n_mp * capacity, dtype=jnp.int32)[None, None, :]
    dispatch = jnp.any(hits, axis=1).astype(jnp.bfloat16)
    combine = jnp.sum(jnp.where(hits, expert_gates[:, :, None], 0.0), axis=1)
    ff_width = experts_out.shape[1]
    if n_dp == 2:
        out_other = swap_dp(experts_out)
        in_other = swap_dp(experts_in)
        normed, out_other = lax.optimization_barrier((normed, out_other))
    sending = lax.dot_general(
        dispatch, normed, (((0,), (0,)), ((), ())), preferred_element_type=jnp.float32
    ).astype(jnp.bfloat16)
    received = lax.all_to_all(
        sending.reshape(n_mp, capacity, d_model), "mp", split_axis=0, concat_axis=0, tiled=True
    )
    flat_rows = received.reshape(-1, d_model)
    if n_dp == 2:
        first = row_index == 0
        gate_up = jnp.where(
            first,
            jnp.concatenate([experts_in[0], in_other[0]], axis=0),
            jnp.concatenate([in_other[0], experts_in[0]], axis=0),
        )
        down = jnp.where(
            first,
            jnp.concatenate([experts_out[0], out_other[0]], axis=1),
            jnp.concatenate([out_other[0], experts_out[0]], axis=1),
        )
        flat_rows, down, gate_up = lax.optimization_barrier((flat_rows, down, gate_up))
    else:
        gate_up = lax.all_gather(experts_in, "dp", axis=1, tiled=True)[0]
        down = lax.all_gather(experts_out, "dp", axis=2, tiled=True)[0]
    gate_vals = jnp.dot(flat_rows, gate_up, preferred_element_type=jnp.float32)
    act = (jax.nn.silu(gate_vals[:, :ff_width]) * gate_vals[:, ff_width:]).astype(jnp.bfloat16)
    outcome = jnp.dot(act, down, preferred_element_type=jnp.float32).astype(jnp.bfloat16)
    results = lax.all_to_all(
        outcome.reshape(n_mp, capacity, d_model), "mp", split_axis=0, concat_axis=0, tiled=True
    )
    comb_hi = combine.astype(jnp.bfloat16)
    comb_lo = (combine - comb_hi.astype(jnp.float32)).astype(jnp.bfloat16)
    flat_results = results.reshape(-1, d_model)
    expert_sum = jnp.dot(comb_hi, flat_results, preferred_element_type=jnp.float32) + jnp.dot(
        comb_lo, flat_results, preferred_element_type=jnp.float32
    )
    return (resid_f + expert_sum).astype(jnp.bfloat16)


def solution(mesh):
    in_specs = (
        P(("dp", "mp"), None),
        P(("dp", "mp"), None),
        P(("dp", "mp"), None, None, None),
        P(),
        P(),
        P("dp", None),
        P("dp", "mp"),
        P(),
        P(("dp", "mp"), None),
        P(("dp", "mp"), None),
        P("mp", "dp", None),
        P("mp", None, "dp"),
    )
    out_specs = P(("dp", "mp"), None)
    return jax.shard_map(
        on_device, mesh=mesh, in_specs=in_specs, out_specs=out_specs, check_vma=False
    )
```

```python
import math

import jax
import jax.numpy as jnp
from jax import lax
from jax.sharding import PartitionSpec as P

HEADS = 8
HD = 128
TOPK = 6
PAGE = 16


epsilon = 1e-06


def attend_head(q_rows, key_rows, value_rows, key_pos, query_pos):
    scores = jnp.dot(q_rows, key_rows.T, preferred_element_type=jnp.float32) * (1.0 / math.sqrt(HD))
    allowed = key_pos[None, :] <= query_pos[:, None]
    scores = jnp.where(allowed, scores, -1e30)
    row_max = jnp.max(scores, axis=1, keepdims=True)
    weights = jnp.exp(scores - row_max)
    weights_bf = (weights / jnp.sum(weights, axis=1, keepdims=True)).astype(jnp.bfloat16)
    blended = jnp.dot(weights_bf, value_rows, preferred_element_type=jnp.float32)
    return blended.astype(jnp.bfloat16)


def swap_dp(x):
    return lax.ppermute(x, "dp", [(0, 1), (1, 0)])


def on_device(
    queries,
    hidden,
    kv_pages,
    page_table,
    cache_len,
    deal_table,
    out_weight,
    norm_gain,
    expert_ids,
    expert_gates,
    experts_in,
    experts_out,
):
    n_mp = lax.axis_size("mp")
    n_dp = lax.axis_size("dp")
    row_index = lax.axis_index("dp")
    column = lax.axis_index("mp")
    q_count = queries.shape[0]
    width = queries.shape[1]
    d_model = hidden.shape[1]
    heads = width // HD
    groups = n_mp // heads
    sub = q_count // groups
    my_head = column % heads
    my_group = column // heads
    page_share = page_table.shape[1] // n_mp
    pages_dev = kv_pages.shape[0]
    deal_row = deal_table[0]
    request = row_index
    page_count = page_table.shape[1]

    q_out = queries.reshape(sub, groups, heads, HD).transpose(1, 2, 0, 3).reshape(n_mp, sub, HD)
    kv_heads = kv_pages.reshape(pages_dev, PAGE, 2, heads, HD).transpose(3, 0, 1, 2, 4)
    kv_out = jnp.tile(kv_heads, (groups, 1, 1, 1, 1)).reshape(n_mp, pages_dev * PAGE * 2, HD)
    if n_dp == 2:
        w_pair = swap_dp(out_weight)
        wo_rows = jnp.where(
            row_index == 0,
            jnp.concatenate([out_weight, w_pair], axis=0),
            jnp.concatenate([w_pair, out_weight], axis=0),
        )
    else:
        wo_rows = lax.all_gather(out_weight, "dp", axis=0, tiled=True)
    bits = n_mp.bit_length() - 1
    kv_send = jnp.concatenate([q_out, kv_out], axis=1)
    if n_mp == 1 << bits:
        block = wo_rows[None]
        if bits > 1 and n_dp == 2:
            far = 1 << (bits - 1)
            mid = lax.ppermute(out_weight, "mp", [(m, m ^ far) for m in range(n_mp)])
            diag = lax.ppermute(
                out_weight,
                ("dp", "mp"),
                [(d * n_mp + m, (1 - d) * n_mp + (m ^ far)) for d in range(2) for m in range(n_mp)],
            )
            far_rows = jnp.where(
                row_index == 0,
                jnp.concatenate([mid, diag], axis=0),
                jnp.concatenate([diag, mid], axis=0),
            )
            low = (column >> (bits - 1)) % 2 == 0
            block = jnp.stack([jnp.where(low, wo_rows, far_rows), jnp.where(low, far_rows, wo_rows)])
        elif bits > 1:
            b = bits - 1
            pair = lax.ppermute(block, "mp", [(m, m ^ (1 << b)) for m in range(n_mp)])
            low = (column >> b) % 2 == 0
            block = jnp.concatenate(
                [jnp.where(low, block, pair), jnp.where(low, pair, block)], axis=0
            )
        block, kv_send = lax.optimization_barrier((block, kv_send))
    both = lax.all_to_all(kv_send, "mp", split_axis=0, concat_axis=0, tiled=True)
    q_in = both[:, :sub, :]
    arrived = both[:, sub:, :].reshape(n_mp, pages_dev, PAGE, 2, HD)
    first_pos = cache_len[request] + deal_row % n_mp * q_count
    query_pos = (
        first_pos[:, None] + jnp.arange(sub, dtype=jnp.int32)[None, :] * groups + my_group
    ).reshape(-1)
    slot_ids = jnp.arange(n_mp * page_share, dtype=jnp.int32)
    physical = (row_index * n_mp + slot_ids // page_share) * pages_dev + slot_ids % page_share
    table_row = page_table[request]
    matches = table_row[None, :] == physical[:, None]
    logical = jnp.sum(
        jnp.where(matches, jnp.arange(page_count, dtype=jnp.int32)[None, :], 0), axis=1
    )
    key_pos = (logical[:, None] * PAGE + jnp.arange(PAGE, dtype=jnp.int32)[None, :]).reshape(-1)
    key_rows = arrived[:, :, :, 0, :].reshape(-1, HD)
    value_rows = arrived[:, :, :, 1, :].reshape(-1, HD)
    blended = attend_head(q_in.reshape(-1, HD), key_rows, value_rows, key_pos, query_pos)
    back = lax.all_to_all(blended.reshape(n_mp, sub, HD), "mp", split_axis=0, concat_axis=0, tiled=True)
    attended = back.reshape(groups, heads, sub, HD).transpose(2, 0, 1, 3).reshape(q_count, width)

    bits = n_mp.bit_length() - 1
    if n_mp == 1 << bits:
        for b in reversed(range(1, bits - 1)):
            pair = lax.ppermute(block, "mp", [(m, m ^ (1 << b)) for m in range(n_mp)])
            low = (column >> b) % 2 == 0
            block = jnp.concatenate(
                [jnp.where(low, block, pair), jnp.where(low, pair, block)], axis=0
            )
        pair = lax.ppermute(block, "mp", [(m, m ^ 1) for m in range(n_mp)])
        own_part = jnp.einsum("tk,jkc->tjc", attended, block, preferred_element_type=jnp.float32)
        pair_part = jnp.einsum("tk,jkc->tjc", attended, pair, preferred_element_type=jnp.float32)
        low = column % 2 == 0
        by_shard = jnp.where(
            low,
            jnp.concatenate([own_part, pair_part], axis=1),
            jnp.concatenate([pair_part, own_part], axis=1),
        )
        order = (0,) + tuple(range(bits, 0, -1)) + (bits + 1,)
        shard_w = wo_rows.shape[1]
        projected = (
            by_shard.reshape((q_count,) + (2,) * bits + (shard_w,))
            .transpose(order)
            .reshape(q_count, d_model)
        )
    else:
        projected = jnp.dot(
            attended,
            lax.all_gather(wo_rows, "mp", axis=1, tiled=True),
            preferred_element_type=jnp.float32,
        )
    resid_f = (hidden.astype(jnp.float32) + projected).astype(jnp.bfloat16).astype(jnp.float32)
    mean_square = jnp.mean(resid_f * resid_f, axis=1, keepdims=True)
    normed = (resid_f * lax.rsqrt(mean_square + epsilon) * norm_gain[None, :]).astype(jnp.bfloat16)
    capacity = min(q_count, q_count * TOPK * 4 // (3 * n_mp))
    flat_ids = expert_ids.reshape(-1)
    one_hot = (flat_ids[:, None] == jnp.arange(n_mp, dtype=jnp.int32)[None, :]).astype(jnp.int32)
    slot_of = jnp.sum(jnp.cumsum(one_hot, axis=0) * one_hot, axis=1) - 1
    target = (flat_ids * capacity + slot_of).reshape(q_count, TOPK)
    hits = target[:, :, None] == jnp.arange(n_mp * capacity, dtype=jnp.int32)[None, None, :]
    dispatch = jnp.any(hits, axis=1).astype(jnp.bfloat16)
    combine = jnp.sum(jnp.where(hits, expert_gates[:, :, None], 0.0), axis=1)
    ff_width = experts_out.shape[1]
    if n_dp == 2:
        out_other = swap_dp(experts_out)
        in_other = swap_dp(experts_in)
        normed, out_other = lax.optimization_barrier((normed, out_other))
    sending = lax.dot_general(
        dispatch, normed, (((0,), (0,)), ((), ())), preferred_element_type=jnp.float32
    ).astype(jnp.bfloat16)
    received = lax.all_to_all(
        sending.reshape(n_mp, capacity, d_model), "mp", split_axis=0, concat_axis=0, tiled=True
    )
    flat_rows = received.reshape(-1, d_model)
    if n_dp == 2:
        first = row_index == 0
        gate_up = jnp.where(
            first,
            jnp.concatenate([experts_in[0], in_other[0]], axis=0),
            jnp.concatenate([in_other[0], experts_in[0]], axis=0),
        )
        down = jnp.where(
            first,
            jnp.concatenate([experts_out[0], out_other[0]], axis=1),
            jnp.concatenate([out_other[0], experts_out[0]], axis=1),
        )
        flat_rows, down, gate_up = lax.optimization_barrier((flat_rows, down, gate_up))
    else:
        gate_up = lax.all_gather(experts_in, "dp", axis=1, tiled=True)[0]
        down = lax.all_gather(experts_out, "dp", axis=2, tiled=True)[0]
    gate_vals = jnp.dot(flat_rows, gate_up, preferred_element_type=jnp.float32)
    act = (jax.nn.silu(gate_vals[:, :ff_width]) * gate_vals[:, ff_width:]).astype(jnp.bfloat16)
    outcome = jnp.dot(act, down, preferred_element_type=jnp.float32).astype(jnp.bfloat16)
    results = lax.all_to_all(
        outcome.reshape(n_mp, capacity, d_model), "mp", split_axis=0, concat_axis=0, tiled=True
    )
    expert_sum = jnp.dot(
        combine,
        results.reshape(-1, d_model).astype(jnp.float32),
        precision=lax.Precision.HIGHEST,
        preferred_element_type=jnp.float32,
    )
    return (resid_f + expert_sum).astype(jnp.bfloat16)


def solution(mesh):
    in_specs = (
        P(("dp", "mp"), None),
        P(("dp", "mp"), None),
        P(("dp", "mp"), None, None, None),
        P(),
        P(),
        P("dp", None),
        P("dp", "mp"),
        P(),
        P(("dp", "mp"), None),
        P(("dp", "mp"), None),
        P("mp", "dp", None),
        P("mp", None, "dp"),
    )
    out_specs = P(("dp", "mp"), None)
    return jax.shard_map(
        on_device, mesh=mesh, in_specs=in_specs, out_specs=out_specs, check_vma=False
    )
```

```python
import math

import jax
import jax.numpy as jnp
from jax import lax
from jax.sharding import PartitionSpec as P

HEADS = 8
HD = 128
TOPK = 6
PAGE = 16


epsilon = 1e-06


def attend_head(q_rows, key_rows, value_rows, key_pos, query_pos):
    scores = jnp.dot(q_rows, key_rows.T, preferred_element_type=jnp.float32) * (1.0 / math.sqrt(HD))
    allowed = key_pos[None, :] <= query_pos[:, None]
    scores = jnp.where(allowed, scores, -1e30)
    row_max = jnp.max(scores, axis=1, keepdims=True)
    weights = jnp.exp(scores - row_max)
    weights_bf = (weights / jnp.sum(weights, axis=1, keepdims=True)).astype(jnp.bfloat16)
    blended = jnp.dot(weights_bf, value_rows, preferred_element_type=jnp.float32)
    return blended.astype(jnp.bfloat16)


def swap_dp(x):
    return lax.ppermute(x, "dp", [(0, 1), (1, 0)])


def on_device(
    queries,
    hidden,
    kv_pages,
    page_table,
    cache_len,
    deal_table,
    out_weight,
    norm_gain,
    expert_ids,
    expert_gates,
    experts_in,
    experts_out,
):
    n_mp = lax.axis_size("mp")
    n_dp = lax.axis_size("dp")
    row_index = lax.axis_index("dp")
    column = lax.axis_index("mp")
    q_count = queries.shape[0]
    width = queries.shape[1]
    d_model = hidden.shape[1]
    heads = width // HD
    groups = n_mp // heads
    sub = q_count // groups
    my_head = column % heads
    my_group = column // heads
    page_share = page_table.shape[1] // n_mp
    pages_dev = kv_pages.shape[0]
    deal_row = deal_table[0]
    request = row_index
    page_count = page_table.shape[1]

    q_out = queries.reshape(sub, groups, heads, HD).transpose(1, 2, 0, 3).reshape(n_mp, sub, HD)
    kv_heads = kv_pages.reshape(pages_dev, PAGE, 2, heads, HD).transpose(3, 0, 1, 2, 4)
    kv_out = jnp.tile(kv_heads, (groups, 1, 1, 1, 1)).reshape(n_mp, pages_dev * PAGE * 2, HD)
    if n_dp == 2:
        w_pair = swap_dp(out_weight)
        wo_rows = jnp.where(
            row_index == 0,
            jnp.concatenate([out_weight, w_pair], axis=0),
            jnp.concatenate([w_pair, out_weight], axis=0),
        )
    else:
        wo_rows = lax.all_gather(out_weight, "dp", axis=0, tiled=True)
    bits = n_mp.bit_length() - 1
    kv_send = jnp.concatenate([q_out, kv_out], axis=1)
    if n_mp == 1 << bits:
        block = wo_rows[None]
        if bits > 2 and n_dp == 2:
            t1, t2 = bits - 1, bits - 2
            fetched = {}
            for a in range(2):
                for c in range(2):
                    off = (a << t1) | (c << t2)
                    near = out_weight if off == 0 else lax.ppermute(
                        out_weight, "mp", [(m, m ^ off) for m in range(n_mp)]
                    )
                    other = lax.ppermute(
                        out_weight,
                        ("dp", "mp"),
                        [(d * n_mp + m, (1 - d) * n_mp + (m ^ off)) for d in range(2) for m in range(n_mp)],
                    )
                    fetched[a, c] = jnp.where(
                        row_index == 0,
                        jnp.concatenate([near, other], axis=0),
                        jnp.concatenate([other, near], axis=0),
                    )
            b1 = (column >> t1) % 2
            b2 = (column >> t2) % 2
            shards = []
            for x2 in range(2):
                for x3 in range(2):
                    a0 = (b1 ^ x3) == 0
                    c0 = (b2 ^ x2) == 0
                    shards.append(
                        jnp.where(
                            a0,
                            jnp.where(c0, fetched[0, 0], fetched[0, 1]),
                            jnp.where(c0, fetched[1, 0], fetched[1, 1]),
                        )
                    )
            block = jnp.stack(shards)
        elif bits > 1:
            b = bits - 1
            pair = lax.ppermute(block, "mp", [(m, m ^ (1 << b)) for m in range(n_mp)])
            low = (column >> b) % 2 == 0
            block = jnp.concatenate(
                [jnp.where(low, block, pair), jnp.where(low, pair, block)], axis=0
            )
        block, kv_send = lax.optimization_barrier((block, kv_send))
    both = lax.all_to_all(kv_send, "mp", split_axis=0, concat_axis=0, tiled=True)
    q_in = both[:, :sub, :]
    arrived = both[:, sub:, :].reshape(n_mp, pages_dev, PAGE, 2, HD)
    first_pos = cache_len[request] + deal_row % n_mp * q_count
    query_pos = (
        first_pos[:, None] + jnp.arange(sub, dtype=jnp.int32)[None, :] * groups + my_group
    ).reshape(-1)
    slot_ids = jnp.arange(n_mp * page_share, dtype=jnp.int32)
    physical = (row_index * n_mp + slot_ids // page_share) * pages_dev + slot_ids % page_share
    table_row = page_table[request]
    matches = table_row[None, :] == physical[:, None]
    logical = jnp.sum(
        jnp.where(matches, jnp.arange(page_count, dtype=jnp.int32)[None, :], 0), axis=1
    )
    key_pos = (logical[:, None] * PAGE + jnp.arange(PAGE, dtype=jnp.int32)[None, :]).reshape(-1)
    key_rows = arrived[:, :, :, 0, :].reshape(-1, HD)
    value_rows = arrived[:, :, :, 1, :].reshape(-1, HD)
    blended = attend_head(q_in.reshape(-1, HD), key_rows, value_rows, key_pos, query_pos)
    back = lax.all_to_all(blended.reshape(n_mp, sub, HD), "mp", split_axis=0, concat_axis=0, tiled=True)
    attended = back.reshape(groups, heads, sub, HD).transpose(2, 0, 1, 3).reshape(q_count, width)

    bits = n_mp.bit_length() - 1
    if n_mp == 1 << bits:
        for b in reversed(range(1, bits - 2 if n_dp == 2 and bits > 2 else bits - 1)):
            pair = lax.ppermute(block, "mp", [(m, m ^ (1 << b)) for m in range(n_mp)])
            low = (column >> b) % 2 == 0
            block = jnp.concatenate(
                [jnp.where(low, block, pair), jnp.where(low, pair, block)], axis=0
            )
        pair = lax.ppermute(block, "mp", [(m, m ^ 1) for m in range(n_mp)])
        own_part = jnp.einsum("tk,jkc->tjc", attended, block, preferred_element_type=jnp.float32)
        pair_part = jnp.einsum("tk,jkc->tjc", attended, pair, preferred_element_type=jnp.float32)
        low = column % 2 == 0
        by_shard = jnp.where(
            low,
            jnp.concatenate([own_part, pair_part], axis=1),
            jnp.concatenate([pair_part, own_part], axis=1),
        )
        order = (0,) + tuple(range(bits, 0, -1)) + (bits + 1,)
        shard_w = wo_rows.shape[1]
        projected = (
            by_shard.reshape((q_count,) + (2,) * bits + (shard_w,))
            .transpose(order)
            .reshape(q_count, d_model)
        )
    else:
        projected = jnp.dot(
            attended,
            lax.all_gather(wo_rows, "mp", axis=1, tiled=True),
            preferred_element_type=jnp.float32,
        )
    resid_f = (hidden.astype(jnp.float32) + projected).astype(jnp.bfloat16).astype(jnp.float32)
    mean_square = jnp.mean(resid_f * resid_f, axis=1, keepdims=True)
    normed = (resid_f * lax.rsqrt(mean_square + epsilon) * norm_gain[None, :]).astype(jnp.bfloat16)
    capacity = min(q_count, q_count * TOPK * 4 // (3 * n_mp))
    flat_ids = expert_ids.reshape(-1)
    one_hot = (flat_ids[:, None] == jnp.arange(n_mp, dtype=jnp.int32)[None, :]).astype(jnp.int32)
    slot_of = jnp.sum(jnp.cumsum(one_hot, axis=0) * one_hot, axis=1) - 1
    target = (flat_ids * capacity + slot_of).reshape(q_count, TOPK)
    hits = target[:, :, None] == jnp.arange(n_mp * capacity, dtype=jnp.int32)[None, None, :]
    dispatch = jnp.any(hits, axis=1).astype(jnp.bfloat16)
    combine = jnp.sum(jnp.where(hits, expert_gates[:, :, None], 0.0), axis=1)
    ff_width = experts_out.shape[1]
    if n_dp == 2:
        out_other = swap_dp(experts_out)
        in_other = swap_dp(experts_in)
        normed, out_other = lax.optimization_barrier((normed, out_other))
    sending = lax.dot_general(
        dispatch, normed, (((0,), (0,)), ((), ())), preferred_element_type=jnp.float32
    ).astype(jnp.bfloat16)
    received = lax.all_to_all(
        sending.reshape(n_mp, capacity, d_model), "mp", split_axis=0, concat_axis=0, tiled=True
    )
    flat_rows = received.reshape(-1, d_model)
    if n_dp == 2:
        first = row_index == 0
        gate_up = jnp.where(
            first,
            jnp.concatenate([experts_in[0], in_other[0]], axis=0),
            jnp.concatenate([in_other[0], experts_in[0]], axis=0),
        )
        down = jnp.where(
            first,
            jnp.concatenate([experts_out[0], out_other[0]], axis=1),
            jnp.concatenate([out_other[0], experts_out[0]], axis=1),
        )
        flat_rows, down, gate_up = lax.optimization_barrier((flat_rows, down, gate_up))
    else:
        gate_up = lax.all_gather(experts_in, "dp", axis=1, tiled=True)[0]
        down = lax.all_gather(experts_out, "dp", axis=2, tiled=True)[0]
    gate_vals = jnp.dot(flat_rows, gate_up, preferred_element_type=jnp.float32)
    act = (jax.nn.silu(gate_vals[:, :ff_width]) * gate_vals[:, ff_width:]).astype(jnp.bfloat16)
    outcome = jnp.dot(act, down, preferred_element_type=jnp.float32).astype(jnp.bfloat16)
    results = lax.all_to_all(
        outcome.reshape(n_mp, capacity, d_model), "mp", split_axis=0, concat_axis=0, tiled=True
    )
    expert_sum = jnp.dot(
        combine,
        results.reshape(-1, d_model).astype(jnp.float32),
        precision=lax.Precision.HIGHEST,
        preferred_element_type=jnp.float32,
    )
    return (resid_f + expert_sum).astype(jnp.bfloat16)


def solution(mesh):
    in_specs = (
        P(("dp", "mp"), None),
        P(("dp", "mp"), None),
        P(("dp", "mp"), None, None, None),
        P(),
        P(),
        P("dp", None),
        P("dp", "mp"),
        P(),
        P(("dp", "mp"), None),
        P(("dp", "mp"), None),
        P("mp", "dp", None),
        P("mp", None, "dp"),
    )
    out_specs = P(("dp", "mp"), None)
    return jax.shard_map(
        on_device, mesh=mesh, in_specs=in_specs, out_specs=out_specs, check_vma=False
    )
```

```python
import math

import jax
import jax.numpy as jnp
from jax import lax
from jax.sharding import PartitionSpec as P

HEADS = 8
HD = 128
TOPK = 6
PAGE = 16


epsilon = 1e-06


def attend_head(q_rows, key_rows, value_rows, key_pos, query_pos):
    scores = jnp.dot(q_rows, key_rows.T, preferred_element_type=jnp.float32) * (1.0 / math.sqrt(HD))
    allowed = key_pos[None, :] <= query_pos[:, None]
    scores = jnp.where(allowed, scores, -1e30)
    row_max = jnp.max(scores, axis=1, keepdims=True)
    weights = jnp.exp(scores - row_max)
    weights_bf = (weights / jnp.sum(weights, axis=1, keepdims=True)).astype(jnp.bfloat16)
    blended = jnp.dot(weights_bf, value_rows, preferred_element_type=jnp.float32)
    return blended.astype(jnp.bfloat16)


def swap_dp(x):
    return lax.ppermute(x, "dp", [(0, 1), (1, 0)])


def on_device(
    queries,
    hidden,
    kv_pages,
    page_table,
    cache_len,
    deal_table,
    out_weight,
    norm_gain,
    expert_ids,
    expert_gates,
    experts_in,
    experts_out,
):
    n_mp = lax.axis_size("mp")
    n_dp = lax.axis_size("dp")
    row_index = lax.axis_index("dp")
    column = lax.axis_index("mp")
    q_count = queries.shape[0]
    width = queries.shape[1]
    d_model = hidden.shape[1]
    heads = width // HD
    groups = n_mp // heads
    sub = q_count // groups
    my_head = column % heads
    my_group = column // heads
    page_share = page_table.shape[1] // n_mp
    pages_dev = kv_pages.shape[0]
    deal_row = deal_table[0]
    request = row_index
    page_count = page_table.shape[1]

    q_out = queries.reshape(sub, groups, heads, HD).transpose(1, 2, 0, 3).reshape(n_mp, sub, HD)
    kv_heads = kv_pages.reshape(pages_dev, PAGE, 2, heads, HD).transpose(3, 0, 1, 2, 4)
    kv_out = jnp.tile(kv_heads, (groups, 1, 1, 1, 1)).reshape(n_mp, pages_dev * PAGE * 2, HD)
    if n_dp == 2:
        w_pair = swap_dp(out_weight)
        wo_rows = jnp.where(
            row_index == 0,
            jnp.concatenate([out_weight, w_pair], axis=0),
            jnp.concatenate([w_pair, out_weight], axis=0),
        )
    else:
        wo_rows = lax.all_gather(out_weight, "dp", axis=0, tiled=True)
    bits = n_mp.bit_length() - 1
    kv_send = jnp.concatenate([q_out, kv_out], axis=1)
    if n_mp == 1 << bits:
        block = wo_rows[None]
        steps = min(3, bits - 1)
        if steps > 1 and n_dp == 2:
            tops = [bits - 1 - i for i in range(steps)]
            fetched = []
            for code in range(1 << steps):
                off = sum(((code >> i) & 1) << t for i, t in enumerate(tops))
                near = out_weight if off == 0 else lax.ppermute(
                    out_weight, "mp", [(m, m ^ off) for m in range(n_mp)]
                )
                other = lax.ppermute(
                    out_weight,
                    ("dp", "mp"),
                    [(d * n_mp + m, (1 - d) * n_mp + (m ^ off)) for d in range(2) for m in range(n_mp)],
                )
                fetched.append(
                    jnp.where(
                        row_index == 0,
                        jnp.concatenate([near, other], axis=0),
                        jnp.concatenate([other, near], axis=0),
                    )
                )
            fetched = jnp.stack(fetched)
            mine = [(column >> t) % 2 for t in tops]
            shards = []
            for j in range(1 << steps):
                want = [(j >> i) & 1 for i in range(steps)]
                code = sum((mine[i] ^ want[i]) << i for i in range(steps))
                shards.append(lax.dynamic_index_in_dim(fetched, code, 0, keepdims=False))
            block = jnp.stack(shards)
        elif bits > 1:
            b = bits - 1
            pair = lax.ppermute(block, "mp", [(m, m ^ (1 << b)) for m in range(n_mp)])
            low = (column >> b) % 2 == 0
            block = jnp.concatenate(
                [jnp.where(low, block, pair), jnp.where(low, pair, block)], axis=0
            )
        block, kv_send = lax.optimization_barrier((block, kv_send))
    both = lax.all_to_all(kv_send, "mp", split_axis=0, concat_axis=0, tiled=True)
    q_in = both[:, :sub, :]
    arrived = both[:, sub:, :].reshape(n_mp, pages_dev, PAGE, 2, HD)
    first_pos = cache_len[request] + deal_row % n_mp * q_count
    query_pos = (
        first_pos[:, None] + jnp.arange(sub, dtype=jnp.int32)[None, :] * groups + my_group
    ).reshape(-1)
    slot_ids = jnp.arange(n_mp * page_share, dtype=jnp.int32)
    physical = (row_index * n_mp + slot_ids // page_share) * pages_dev + slot_ids % page_share
    table_row = page_table[request]
    matches = table_row[None, :] == physical[:, None]
    logical = jnp.sum(
        jnp.where(matches, jnp.arange(page_count, dtype=jnp.int32)[None, :], 0), axis=1
    )
    key_pos = (logical[:, None] * PAGE + jnp.arange(PAGE, dtype=jnp.int32)[None, :]).reshape(-1)
    key_rows = arrived[:, :, :, 0, :].reshape(-1, HD)
    value_rows = arrived[:, :, :, 1, :].reshape(-1, HD)
    blended = attend_head(q_in.reshape(-1, HD), key_rows, value_rows, key_pos, query_pos)
    back = lax.all_to_all(blended.reshape(n_mp, sub, HD), "mp", split_axis=0, concat_axis=0, tiled=True)
    attended = back.reshape(groups, heads, sub, HD).transpose(2, 0, 1, 3).reshape(q_count, width)

    bits = n_mp.bit_length() - 1
    if n_mp == 1 << bits:
        for b in reversed(range(1, bits - steps if n_dp == 2 and steps > 1 else bits - 1)):
            pair = lax.ppermute(block, "mp", [(m, m ^ (1 << b)) for m in range(n_mp)])
            low = (column >> b) % 2 == 0
            block = jnp.concatenate(
                [jnp.where(low, block, pair), jnp.where(low, pair, block)], axis=0
            )
        pair = lax.ppermute(block, "mp", [(m, m ^ 1) for m in range(n_mp)])
        own_part = jnp.einsum("tk,jkc->tjc", attended, block, preferred_element_type=jnp.float32)
        pair_part = jnp.einsum("tk,jkc->tjc", attended, pair, preferred_element_type=jnp.float32)
        low = column % 2 == 0
        by_shard = jnp.where(
            low,
            jnp.concatenate([own_part, pair_part], axis=1),
            jnp.concatenate([pair_part, own_part], axis=1),
        )
        order = (0,) + tuple(range(bits, 0, -1)) + (bits + 1,)
        shard_w = wo_rows.shape[1]
        projected = (
            by_shard.reshape((q_count,) + (2,) * bits + (shard_w,))
            .transpose(order)
            .reshape(q_count, d_model)
        )
    else:
        projected = jnp.dot(
            attended,
            lax.all_gather(wo_rows, "mp", axis=1, tiled=True),
            preferred_element_type=jnp.float32,
        )
    resid_f = (hidden.astype(jnp.float32) + projected).astype(jnp.bfloat16).astype(jnp.float32)
    mean_square = jnp.mean(resid_f * resid_f, axis=1, keepdims=True)
    normed = (resid_f * lax.rsqrt(mean_square + epsilon) * norm_gain[None, :]).astype(jnp.bfloat16)
    capacity = min(q_count, q_count * TOPK * 4 // (3 * n_mp))
    flat_ids = expert_ids.reshape(-1)
    one_hot = (flat_ids[:, None] == jnp.arange(n_mp, dtype=jnp.int32)[None, :]).astype(jnp.int32)
    slot_of = jnp.sum(jnp.cumsum(one_hot, axis=0) * one_hot, axis=1) - 1
    target = (flat_ids * capacity + slot_of).reshape(q_count, TOPK)
    hits = target[:, :, None] == jnp.arange(n_mp * capacity, dtype=jnp.int32)[None, None, :]
    dispatch = jnp.any(hits, axis=1).astype(jnp.bfloat16)
    combine = jnp.sum(jnp.where(hits, expert_gates[:, :, None], 0.0), axis=1)
    ff_width = experts_out.shape[1]
    if n_dp == 2:
        out_other = swap_dp(experts_out)
        in_other = swap_dp(experts_in)
        normed, out_other = lax.optimization_barrier((normed, out_other))
    sending = lax.dot_general(
        dispatch, normed, (((0,), (0,)), ((), ())), preferred_element_type=jnp.float32
    ).astype(jnp.bfloat16)
    received = lax.all_to_all(
        sending.reshape(n_mp, capacity, d_model), "mp", split_axis=0, concat_axis=0, tiled=True
    )
    flat_rows = received.reshape(-1, d_model)
    if n_dp == 2:
        first = row_index == 0
        gate_up = jnp.where(
            first,
            jnp.concatenate([experts_in[0], in_other[0]], axis=0),
            jnp.concatenate([in_other[0], experts_in[0]], axis=0),
        )
        down = jnp.where(
            first,
            jnp.concatenate([experts_out[0], out_other[0]], axis=1),
            jnp.concatenate([out_other[0], experts_out[0]], axis=1),
        )
        flat_rows, down, gate_up = lax.optimization_barrier((flat_rows, down, gate_up))
    else:
        gate_up = lax.all_gather(experts_in, "dp", axis=1, tiled=True)[0]
        down = lax.all_gather(experts_out, "dp", axis=2, tiled=True)[0]
    gate_vals = jnp.dot(flat_rows, gate_up, preferred_element_type=jnp.float32)
    act = (jax.nn.silu(gate_vals[:, :ff_width]) * gate_vals[:, ff_width:]).astype(jnp.bfloat16)
    outcome = jnp.dot(act, down, preferred_element_type=jnp.float32).astype(jnp.bfloat16)
    results = lax.all_to_all(
        outcome.reshape(n_mp, capacity, d_model), "mp", split_axis=0, concat_axis=0, tiled=True
    )
    expert_sum = jnp.dot(
        combine,
        results.reshape(-1, d_model).astype(jnp.float32),
        precision=lax.Precision.HIGHEST,
        preferred_element_type=jnp.float32,
    )
    return (resid_f + expert_sum).astype(jnp.bfloat16)


def solution(mesh):
    in_specs = (
        P(("dp", "mp"), None),
        P(("dp", "mp"), None),
        P(("dp", "mp"), None, None, None),
        P(),
        P(),
        P("dp", None),
        P("dp", "mp"),
        P(),
        P(("dp", "mp"), None),
        P(("dp", "mp"), None),
        P("mp", "dp", None),
        P("mp", None, "dp"),
    )
    out_specs = P(("dp", "mp"), None)
    return jax.shard_map(
        on_device, mesh=mesh, in_specs=in_specs, out_specs=out_specs, check_vma=False
    )
```
